32 devices in a mesh: lat: 8 (over z, y), lon: 4 (over x, core).
Axes of the slice: x: 2, y: 2, z: 4, core: 2. Of those that a mesh axis runs over, the one named last changes fastest.
Arguments:
- fields: float32 [6, 32, 32, 4096], P(None, None, 'lat', 'lon'), may hold values from -6 to 6
- weights: float32 [16, 32, 4096], P(None, 'lat', 'lon'), may hold values from -2 to 2
- stencil: int32 [2, 32, 4096], P(None, 'lat', 'lon'), may hold values from -3 to 4095, as said below
- bands: float32 [6, 5, 32], replicated, may hold values from -3 to 3
Outputs:
- spectral_real: float32 [192, 32, 1280], P('lon', 'lat')
- spectral_imag: float32 [192, 32, 1280], P('lon', 'lat')
The draws below stay inside these ranges and needn't reach their ends.
Inputs may be any that keep to these rules, and one draw needn't show every extreme that they name: stencil[0, i, j] lies in i - 3 to i; stencil[1, i, j] is (j - 16 + d) mod 4096 for some d of 0 to 29.
All inputs are finite; a program needn't handle non-finite values.
Results may differ from the reference program's by a relative error of at most 0.00007.
Values sent between devices are 32-bit elements; how exact they have to be, the bound alone decides.
No kernel may reach another device: no remote copies, remote signals or barrier semaphores. Data moves between devices by JAX's collectives and lax.ppermute only.
A program may use at most 128 MiB of HBM per device.

```python
import math
import jax
import jax.numpy as jnp
from jax import lax

FIELDS = 6
LEV = 32
LINE = 4096
NK = 1280
HALO = 16
NLAT = 32
ITEMS = 192


def draw_stencil(key, part):
    key_row, key_col = jax.random.split(jax.random.fold_in(key, 17))
    line_index = jnp.arange(NLAT, dtype=jnp.int32)[:, None]
    column_index = jnp.arange(LINE, dtype=jnp.int32)[None, :]
    step_row = jax.random.randint(key_row, (NLAT, LINE), 0, 4, dtype=jnp.int32)
    step_col = jax.random.randint(key_col, (NLAT, LINE), 0, 2 * HALO - 2, dtype=jnp.int32)
    step_row = step_row.at[0, 0].set(0)
    step_col = step_col.at[0, LINE - 1].set(HALO)
    first_row = line_index - 3 + step_row
    first_col = (column_index - HALO + step_col) % LINE
    return jnp.stack([first_row, first_col]).astype(jnp.int32)


def shard_levels(key, shape, cuts, smallest, high):
    def one(dim, shards_of):
        steps = jax.random.uniform(jax.random.fold_in(jax.random.fold_in(key, 6), dim), (shards_of,), jnp.float32, smallest / len(cuts), high / len(cuts))
        return jnp.repeat(jnp.exp(steps), shape[dim] // shards_of).reshape((-1,) + (1,) * (len(shape) - dim - 1))

    level = one(*cuts[0])
    for cut in cuts[1:]:
        level = level * one(*cut)
    return level


def gaussian(rng, shape, spread, reach, cuts=(), kind=jnp.bfloat16):
    entries = spread * jax.random.normal(rng, shape, jnp.float32)
    if cuts:
        entries = entries * shard_levels(rng, shape, cuts, -0.22, 0.18)
    return jnp.clip(entries, -reach, reach).astype(kind)


def setup_inputs(seed: int = 0) -> dict:
    key_of = jax.random.split(jax.random.key(seed), 5)
    fields = gaussian(key_of[0], (FIELDS, LEV, NLAT, LINE), 1.0, 6.0, ((2, 8), (3, 4)), jnp.float32)
    weights = gaussian(key_of[1], (16, NLAT, LINE), 0.3, 2.0, ((1, 8), (2, 4)), jnp.float32)
    stencil = draw_stencil(jax.random.fold_in(key_of[4], 71), 0)
    bands = gaussian(key_of[3], (FIELDS, 5, LEV), 0.5, 3.0, (), jnp.float32)
    return {"fields": fields, "weights": weights, "stencil": stencil, "bands": bands}


def reference(fields, weights, stencil, bands):
    base_row = stencil[0]
    base_col = stencil[1]

    def one_field(pair):
        field, band = pair
        padded = jnp.pad(field, ((0, 0), (3, 3), (0, 0))).reshape(LEV, (NLAT + 6) * LINE)
        total = jnp.zeros((LEV, NLAT, LINE), jnp.float32)
        for offset_a in range(4):
            for offset_b in range(4):
                where_at = ((base_row + (offset_a + 3)) * LINE + (base_col + offset_b) % LINE).astype(jnp.int32)
                picked = jnp.take(padded, where_at.reshape(-1), axis=1).reshape(LEV, NLAT, LINE)
                total = total + weights[4 * offset_a + offset_b][None] * picked
        stacked = jnp.pad(total, ((2, 2), (0, 0), (0, 0)))
        mixed = jnp.zeros((LEV, NLAT, LINE), jnp.float32)
        for shift_k in range(5):
            mixed = mixed + band[shift_k][:, None, None] * stacked[shift_k:shift_k + LEV]
        spectrum = jnp.fft.rfft(mixed, axis=-1)[..., :NK] / math.sqrt(LINE)
        return (jnp.real(spectrum).astype(jnp.float32), jnp.imag(spectrum).astype(jnp.float32))
    real_part, imag_part = lax.map(one_field, (fields, bands))
    return (real_part.reshape(ITEMS, NLAT, NK), imag_part.reshape(ITEMS, NLAT, NK))
```

```python
import functools
import math

import jax
import jax.numpy as jnp
from jax import lax
from jax.experimental import pallas as pl
from jax.experimental.pallas import tpu as pltpu
from jax.sharding import PartitionSpec as P

RADIX = 64
NK = 1280
HALO = 16
ROWS_OUT = 3
TAPS = 4
LANES = 128
WINDOW = 256


def shifted(block, axis, width, dim, periodic):
    count = lax.axis_size(axis)
    forward = [(i, i + 1) for i in range(count - 1)]
    if periodic:
        forward.append((count - 1, 0))
    backward = [(target, source) for source, target in forward]
    low = lax.ppermute(
        lax.slice_in_dim(block, block.shape[dim] - width, None, axis=dim), axis, forward
    )
    high = lax.ppermute(lax.slice_in_dim(block, 0, width, axis=dim), axis, backward)
    return low, high


def spectrum(block):
    n_items, n_lines, line_len = block.shape
    highest = lax.Precision.HIGHEST
    folded = block.reshape(n_items * n_lines, RADIX, RADIX)
    digits = jnp.arange(RADIX, dtype=jnp.int32)
    angle_one = (
        2.0 * math.pi / RADIX * (digits[:, None] * digits[None, :] % RADIX).astype(jnp.float32)
    )
    first_table = jnp.concatenate([jnp.cos(angle_one), -jnp.sin(angle_one)], axis=1)
    partial_value = jnp.einsum("rab,ac->rbc", folded, first_table, precision=highest)
    angle_two = (
        2.0
        * math.pi
        / line_len
        * (digits[:, None] * digits[None, :] % line_len).astype(jnp.float32)
    )
    cos_two = jnp.cos(angle_two)
    sin_two = jnp.sin(angle_two)
    part_re = partial_value[..., :RADIX]
    part_im = partial_value[..., RADIX:]
    twisted = jnp.concatenate(
        [part_re * cos_two + part_im * sin_two, part_im * cos_two - part_re * sin_two], axis=-1
    )
    quotients = jnp.arange(NK // RADIX, dtype=jnp.int32)
    angle_three = (
        2.0 * math.pi / RADIX * (digits[:, None] * quotients[None, :] % RADIX).astype(jnp.float32)
    )
    with_cos = jnp.einsum("rbc,bq->rqc", twisted, jnp.cos(angle_three), precision=highest)
    with_sin = jnp.einsum("rbc,bq->rqc", twisted, jnp.sin(angle_three), precision=highest)
    scale = 1.0 / math.sqrt(line_len)
    real_part = (with_cos[..., :RADIX] + with_sin[..., RADIX:]) * scale
    imag_part = (with_cos[..., RADIX:] - with_sin[..., :RADIX]) * scale
    return (real_part.reshape(n_items, n_lines, NK), imag_part.reshape(n_items, n_lines, NK))


def interp_kernel(hi_ref, lo_ref, info_ref, out_ref):
    row = pl.program_id(0)
    block = pl.program_id(1)
    info = info_ref[0]
    offset_r = info[16:17, :]
    offset_d = info[17:18, :]
    c_index = lax.broadcasted_iota(jnp.int32, (WINDOW, LANES), 0).astype(jnp.float32)
    j_index = lax.broadcasted_iota(jnp.int32, (WINDOW, LANES), 1).astype(jnp.float32)
    tap = c_index - j_index - offset_d
    masks = [tap == float(b) for b in range(TAPS)]
    start = pl.multiple_of(block * LANES, LANES)
    acc = jnp.zeros(out_ref.shape[1:], jnp.float32)
    for p in range(2 * ROWS_OUT + 1):
        picked = []
        for b in range(TAPS):
            value = jnp.zeros_like(offset_r)
            for a in range(TAPS):
                if 0 <= p - a <= ROWS_OUT:
                    value = jnp.where(offset_r == float(p - a), info[4 * a + b : 4 * a + b + 1, :], value)
            picked.append(value)
        matrix = jnp.where(
            masks[0],
            picked[0],
            jnp.where(masks[1], picked[1], jnp.where(masks[2], picked[2], jnp.where(masks[3], picked[3], 0.0))),
        )
        m_hi = matrix.astype(jnp.bfloat16)
        m_lo = (matrix - m_hi.astype(jnp.float32)).astype(jnp.bfloat16)
        x_hi = hi_ref[row + p, :, pl.ds(start, WINDOW)]
        x_lo = lo_ref[row + p, :, pl.ds(start, WINDOW)]
        acc = acc + jnp.dot(x_hi, m_hi, preferred_element_type=jnp.float32)
        acc = acc + jnp.dot(x_hi, m_lo, preferred_element_type=jnp.float32)
        acc = acc + jnp.dot(x_lo, m_hi, preferred_element_type=jnp.float32)
    out_ref[0] = acc


def interpolate(x_hi, x_lo, info, lat_rows, lon_cols):
    n_rows, n_items, width = x_hi.shape
    blocks = lon_cols // LANES
    return pl.pallas_call(
        interp_kernel,
        out_shape=jax.ShapeDtypeStruct((lat_rows, n_items, lon_cols), jnp.float32),
        grid=(lat_rows, blocks),
        in_specs=[
            pl.BlockSpec((n_rows, n_items, width), lambda i, jb: (0, 0, 0)),
            pl.BlockSpec((n_rows, n_items, width), lambda i, jb: (0, 0, 0)),
            pl.BlockSpec((1, info.shape[1], LANES), lambda i, jb: (i, 0, jb)),
        ],
        out_specs=pl.BlockSpec((1, n_items, LANES), lambda i, jb: (i, 0, jb)),
        compiler_params=pltpu.CompilerParams(vmem_limit_bytes=60 * 1024 * 1024),
    )(x_hi, x_lo, info)


def on_device(fields, weights, stencil, bands):
    n_fields, n_levels, lat_rows, lon_cols = fields.shape
    n_items = n_fields * n_levels
    rows_major = jnp.transpose(fields, (2, 0, 1, 3))
    stacked = jnp.pad(rows_major, ((0, 0), (0, 0), (2, 2), (0, 0)))
    mixed = bands[None, :, 0, :, None] * stacked[:, :, 0:n_levels]
    for shift_k in range(1, 5):
        mixed = mixed + bands[None, :, shift_k, :, None] * stacked[:, :, shift_k : shift_k + n_levels]
    tile = mixed.reshape(lat_rows, n_items, lon_cols)
    left, right = shifted(tile, "lon", HALO, 2, True)
    wide = jnp.concatenate([left, tile, right], axis=2)
    below, above = shifted(wide, "lat", ROWS_OUT, 0, False)
    haloed = jnp.concatenate([below, wide, above], axis=0)
    width = lon_cols + LANES
    haloed = jnp.pad(haloed, ((0, 0), (0, 0), (0, width - haloed.shape[2])))
    rounded = lax.reduce_precision(haloed, exponent_bits=8, mantissa_bits=7)
    x_hi = rounded.astype(jnp.bfloat16)
    x_lo = (haloed - rounded).astype(jnp.bfloat16)

    lat_start = lax.axis_index("lat") * lat_rows
    lon_start = lax.axis_index("lon") * lon_cols
    line_len = lon_cols * lax.axis_size("lon")
    row_g = lat_start + jnp.arange(lat_rows, dtype=jnp.int32)[:, None]
    col_g = lon_start + jnp.arange(lon_cols, dtype=jnp.int32)[None, :]
    offset_r = (stencil[0] - row_g + ROWS_OUT).astype(jnp.float32)
    offset_d = jnp.mod(stencil[1] - col_g + HALO, line_len).astype(jnp.float32)
    info = jnp.concatenate(
        [
            jnp.transpose(weights, (1, 0, 2)),
            offset_r[:, None, :],
            offset_d[:, None, :],
            jnp.zeros((lat_rows, 6, lon_cols), jnp.float32),
        ],
        axis=1,
    )
    departed = interpolate(x_hi, x_lo, info, lat_rows, lon_cols)
    gathered = lax.all_to_all(departed, "lon", split_axis=1, concat_axis=2, tiled=True)
    lines = jnp.transpose(gathered, (1, 0, 2))
    real_part, imag_part = spectrum(lines)
    return (real_part, imag_part)


def solution(mesh):
    placed = (P(None, None, "lat", "lon"), P(None, "lat", "lon"), P(None, "lat", "lon"), P())
    return jax.shard_map(
        on_device,
        mesh=mesh,
        in_specs=placed,
        out_specs=(P("lon", "lat", None), P("lon", "lat", None)),
        check_vma=False,
    )
```

```python
import functools
import math

import jax
import jax.numpy as jnp
from jax import lax
from jax.experimental import pallas as pl
from jax.experimental.pallas import tpu as pltpu
from jax.sharding import PartitionSpec as P

RADIX = 64
NK = 1280
HALO = 16
ROWS_OUT = 3
TAPS = 4
LANES = 128
WINDOW = 256


def shifted(block, axis, width, dim, periodic):
    count = lax.axis_size(axis)
    forward = [(i, i + 1) for i in range(count - 1)]
    if periodic:
        forward.append((count - 1, 0))
    backward = [(target, source) for source, target in forward]
    low = lax.ppermute(
        lax.slice_in_dim(block, block.shape[dim] - width, None, axis=dim), axis, forward
    )
    high = lax.ppermute(lax.slice_in_dim(block, 0, width, axis=dim), axis, backward)
    return low, high


def spectrum(block):
    n_items, n_lines, line_len = block.shape
    highest = lax.Precision.HIGHEST
    folded = block.reshape(n_items * n_lines, RADIX, RADIX)
    digits = jnp.arange(RADIX, dtype=jnp.int32)
    angle_one = (
        2.0 * math.pi / RADIX * (digits[:, None] * digits[None, :] % RADIX).astype(jnp.float32)
    )
    first_table = jnp.concatenate([jnp.cos(angle_one), -jnp.sin(angle_one)], axis=1)
    partial_value = jnp.einsum("rab,ac->rbc", folded, first_table, precision=highest)
    angle_two = (
        2.0
        * math.pi
        / line_len
        * (digits[:, None] * digits[None, :] % line_len).astype(jnp.float32)
    )
    cos_two = jnp.cos(angle_two)
    sin_two = jnp.sin(angle_two)
    part_re = partial_value[..., :RADIX]
    part_im = partial_value[..., RADIX:]
    twisted = jnp.concatenate(
        [part_re * cos_two + part_im * sin_two, part_im * cos_two - part_re * sin_two], axis=-1
    )
    quotients = jnp.arange(NK // RADIX, dtype=jnp.int32)
    angle_three = (
        2.0 * math.pi / RADIX * (digits[:, None] * quotients[None, :] % RADIX).astype(jnp.float32)
    )
    with_cos = jnp.einsum("rbc,bq->rqc", twisted, jnp.cos(angle_three), precision=highest)
    with_sin = jnp.einsum("rbc,bq->rqc", twisted, jnp.sin(angle_three), precision=highest)
    scale = 1.0 / math.sqrt(line_len)
    real_part = (with_cos[..., :RADIX] + with_sin[..., RADIX:]) * scale
    imag_part = (with_cos[..., RADIX:] - with_sin[..., :RADIX]) * scale
    return (real_part.reshape(n_items, n_lines, NK), imag_part.reshape(n_items, n_lines, NK))


def interp_kernel(*refs):
    span = 2 * ROWS_OUT + 1
    hi_refs = refs[:span]
    lo_refs = refs[span : 2 * span]
    info_ref = refs[2 * span]
    out_ref = refs[2 * span + 1]
    block = pl.program_id(0)
    info = info_ref[...]
    offset_r = info[16:17, :]
    offset_d = info[17:18, :]
    c_index = lax.broadcasted_iota(jnp.int32, (WINDOW, LANES), 0).astype(jnp.float32)
    j_index = lax.broadcasted_iota(jnp.int32, (WINDOW, LANES), 1).astype(jnp.float32)
    tap = c_index - j_index - offset_d
    masks = [tap == float(b) for b in range(TAPS)]
    start = pl.multiple_of(block * LANES, LANES)
    acc = jnp.zeros(out_ref.shape, jnp.float32)
    for p in range(span):
        picked = []
        for b in range(TAPS):
            value = jnp.zeros_like(offset_r)
            for a in range(TAPS):
                if 0 <= p - a <= ROWS_OUT:
                    value = jnp.where(offset_r == float(p - a), info[4 * a + b : 4 * a + b + 1, :], value)
            picked.append(value)
        matrix = jnp.where(
            masks[0],
            picked[0],
            jnp.where(masks[1], picked[1], jnp.where(masks[2], picked[2], jnp.where(masks[3], picked[3], 0.0))),
        )
        m_hi = matrix.astype(jnp.bfloat16)
        m_lo = (matrix - m_hi.astype(jnp.float32)).astype(jnp.bfloat16)
        x_hi = hi_refs[p][:, pl.ds(start, WINDOW)]
        x_lo = lo_refs[p][:, pl.ds(start, WINDOW)]
        acc = acc + jnp.dot(x_hi, m_hi, preferred_element_type=jnp.float32)
        acc = acc + jnp.dot(x_hi, m_lo, preferred_element_type=jnp.float32)
        acc = acc + jnp.dot(x_lo, m_hi, preferred_element_type=jnp.float32)
    out_ref[...] = acc


def interpolate_row(his, los, info_row, lon_cols):
    n_items, width = his[0].shape
    blocks = lon_cols // LANES
    whole = pl.BlockSpec((n_items, width), lambda jb: (0, 0))
    return pl.pallas_call(
        interp_kernel,
        out_shape=jax.ShapeDtypeStruct((n_items, lon_cols), jnp.float32),
        grid=(blocks,),
        in_specs=[whole] * (2 * len(his)) + [pl.BlockSpec((info_row.shape[0], LANES), lambda jb: (0, jb))],
        out_specs=pl.BlockSpec((n_items, LANES), lambda jb: (0, jb)),
        compiler_params=pltpu.CompilerParams(vmem_limit_bytes=48 * 1024 * 1024),
    )(*his, *los, info_row)


def split_row(row, width):
    padded = jnp.pad(row, ((0, 0), (0, width - row.shape[1])))
    rounded = lax.reduce_precision(padded, exponent_bits=8, mantissa_bits=7)
    return rounded.astype(jnp.bfloat16), (padded - rounded).astype(jnp.bfloat16)


def ready_step(i, lat_rows):
    below = ROWS_OUT - 1 - i if i < ROWS_OUT else -1
    above = i + ROWS_OUT - lat_rows
    return max(below, above)


def on_device(fields, weights, stencil, bands):
    n_fields, n_levels, lat_rows, lon_cols = fields.shape
    n_items = n_fields * n_levels
    rows_major = jnp.transpose(fields, (2, 0, 1, 3))
    stacked = jnp.pad(rows_major, ((0, 0), (0, 0), (2, 2), (0, 0)))
    mixed = bands[None, :, 0, :, None] * stacked[:, :, 0:n_levels]
    for shift_k in range(1, 5):
        mixed = mixed + bands[None, :, shift_k, :, None] * stacked[:, :, shift_k : shift_k + n_levels]
    tile = mixed.reshape(lat_rows, n_items, lon_cols)
    left, right = shifted(tile, "lon", HALO, 2, True)
    wide = jnp.concatenate([left, tile, right], axis=2)

    count = lax.axis_size("lat")
    forward = [(i, i + 1) for i in range(count - 1)]
    backward = [(target, source) for source, target in forward]
    below = [None] * ROWS_OUT
    above = [None] * ROWS_OUT
    previous = None
    for step in range(ROWS_OUT):
        h_below = ROWS_OUT - 1 - step
        src_below = wide[lat_rows - ROWS_OUT + h_below]
        src_above = wide[step]
        if previous is not None:
            src_below, src_above, _ = lax.optimization_barrier((src_below, src_above, previous))
        below[h_below] = lax.ppermute(src_below, "lat", forward)
        above[step] = lax.ppermute(src_above, "lat", backward)
        previous = (below[h_below], above[step])
    rows = below + [wide[i] for i in range(lat_rows)] + above
    width = lon_cols + LANES
    split = [split_row(r, width) for r in rows]

    lat_start = lax.axis_index("lat") * lat_rows
    lon_start = lax.axis_index("lon") * lon_cols
    line_len = lon_cols * lax.axis_size("lon")
    row_g = lat_start + jnp.arange(lat_rows, dtype=jnp.int32)[:, None]
    col_g = lon_start + jnp.arange(lon_cols, dtype=jnp.int32)[None, :]
    offset_r = (stencil[0] - row_g + ROWS_OUT).astype(jnp.float32)
    offset_d = jnp.mod(stencil[1] - col_g + HALO, line_len).astype(jnp.float32)
    info = jnp.concatenate(
        [
            jnp.transpose(weights, (1, 0, 2)),
            offset_r[:, None, :],
            offset_d[:, None, :],
            jnp.zeros((lat_rows, 6, lon_cols), jnp.float32),
        ],
        axis=1,
    )
    span = 2 * ROWS_OUT + 1
    real_rows = [None] * lat_rows
    imag_rows = [None] * lat_rows
    for i in sorted(range(lat_rows), key=lambda i: ready_step(i, lat_rows)):
        his = [split[i + p][0] for p in range(span)]
        los = [split[i + p][1] for p in range(span)]
        departed = interpolate_row(his, los, info[i], lon_cols)
        gathered = lax.all_to_all(departed, "lon", split_axis=0, concat_axis=1, tiled=True)
        real_part, imag_part = spectrum(gathered[:, None, :])
        real_rows[i] = real_part
        imag_rows[i] = imag_part
    return (jnp.concatenate(real_rows, axis=1), jnp.concatenate(imag_rows, axis=1))


def solution(mesh):
    placed = (P(None, None, "lat", "lon"), P(None, "lat", "lon"), P(None, "lat", "lon"), P())
    return jax.shard_map(
        on_device,
        mesh=mesh,
        in_specs=placed,
        out_specs=(P("lon", "lat", None), P("lon", "lat", None)),
        check_vma=False,
    )
```

```python
import functools
import math

import jax
import jax.numpy as jnp
from jax import lax
from jax.experimental import pallas as pl
from jax.experimental.pallas import tpu as pltpu
from jax.sharding import PartitionSpec as P

RADIX = 64
NK = 1280
HALO = 16
ROWS_OUT = 3
TAPS = 4
LANES = 128
WINDOW = 256


def shifted(block, axis, width, dim, periodic):
    count = lax.axis_size(axis)
    forward = [(i, i + 1) for i in range(count - 1)]
    if periodic:
        forward.append((count - 1, 0))
    backward = [(target, source) for source, target in forward]
    low = lax.ppermute(
        lax.slice_in_dim(block, block.shape[dim] - width, None, axis=dim), axis, forward
    )
    high = lax.ppermute(lax.slice_in_dim(block, 0, width, axis=dim), axis, backward)
    return low, high


def spectrum(block):
    n_items, n_lines, line_len = block.shape
    highest = lax.Precision.HIGHEST
    folded = block.reshape(n_items * n_lines, RADIX, RADIX)
    digits = jnp.arange(RADIX, dtype=jnp.int32)
    angle_one = (
        2.0 * math.pi / RADIX * (digits[:, None] * digits[None, :] % RADIX).astype(jnp.float32)
    )
    first_table = jnp.concatenate([jnp.cos(angle_one), -jnp.sin(angle_one)], axis=1)
    partial_value = jnp.einsum("rab,ac->rbc", folded, first_table, precision=highest)
    angle_two = (
        2.0
        * math.pi
        / line_len
        * (digits[:, None] * digits[None, :] % line_len).astype(jnp.float32)
    )
    cos_two = jnp.cos(angle_two)
    sin_two = jnp.sin(angle_two)
    part_re = partial_value[..., :RADIX]
    part_im = partial_value[..., RADIX:]
    twisted = jnp.concatenate(
        [part_re * cos_two + part_im * sin_two, part_im * cos_two - part_re * sin_two], axis=-1
    )
    quotients = jnp.arange(NK // RADIX, dtype=jnp.int32)
    angle_three = (
        2.0 * math.pi / RADIX * (digits[:, None] * quotients[None, :] % RADIX).astype(jnp.float32)
    )
    with_cos = jnp.einsum("rbc,bq->rqc", twisted, jnp.cos(angle_three), precision=highest)
    with_sin = jnp.einsum("rbc,bq->rqc", twisted, jnp.sin(angle_three), precision=highest)
    scale = 1.0 / math.sqrt(line_len)
    real_part = (with_cos[..., :RADIX] + with_sin[..., RADIX:]) * scale
    imag_part = (with_cos[..., RADIX:] - with_sin[..., :RADIX]) * scale
    return (real_part.reshape(n_items, n_lines, NK), imag_part.reshape(n_items, n_lines, NK))


def interp_kernel(bases, hi_ref, lo_ref, info_ref, out_ref):
    member = pl.program_id(0)
    block = pl.program_id(1)
    base = bases[0]
    for slot in range(1, len(bases)):
        base = jnp.where(member == slot, bases[slot], base)
    info = info_ref[0]
    offset_r = info[16:17, :]
    offset_d = info[17:18, :]
    c_index = lax.broadcasted_iota(jnp.int32, (WINDOW, LANES), 0).astype(jnp.float32)
    j_index = lax.broadcasted_iota(jnp.int32, (WINDOW, LANES), 1).astype(jnp.float32)
    tap = c_index - j_index - offset_d
    masks = [tap == float(b) for b in range(TAPS)]
    start = pl.multiple_of(block * LANES, LANES)
    acc = jnp.zeros(out_ref.shape[1:], jnp.float32)
    for p in range(2 * ROWS_OUT + 1):
        picked = []
        for b in range(TAPS):
            value = jnp.zeros_like(offset_r)
            for a in range(TAPS):
                if 0 <= p - a <= ROWS_OUT:
                    value = jnp.where(offset_r == float(p - a), info[4 * a + b : 4 * a + b + 1, :], value)
            picked.append(value)
        matrix = jnp.where(
            masks[0],
            picked[0],
            jnp.where(masks[1], picked[1], jnp.where(masks[2], picked[2], jnp.where(masks[3], picked[3], 0.0))),
        )
        m_hi = matrix.astype(jnp.bfloat16)
        m_lo = (matrix - m_hi.astype(jnp.float32)).astype(jnp.bfloat16)
        x_hi = hi_ref[base + p, :, pl.ds(start, WINDOW)]
        x_lo = lo_ref[base + p, :, pl.ds(start, WINDOW)]
        acc = acc + jnp.dot(x_hi, m_hi, preferred_element_type=jnp.float32)
        acc = acc + jnp.dot(x_hi, m_lo, preferred_element_type=jnp.float32)
        acc = acc + jnp.dot(x_lo, m_hi, preferred_element_type=jnp.float32)
    out_ref[0] = acc


def interpolate_rows(bases, x_hi, x_lo, info, members, lon_cols):
    n_rows, n_items, width = x_hi.shape
    blocks = lon_cols // LANES
    first = members[0]
    step = members[1] - members[0] if len(members) > 1 else 1
    whole = pl.BlockSpec((n_rows, n_items, width), lambda m, jb: (0, 0, 0))
    return pl.pallas_call(
        functools.partial(interp_kernel, tuple(bases)),
        out_shape=jax.ShapeDtypeStruct((len(members), n_items, lon_cols), jnp.float32),
        grid=(len(members), blocks),
        in_specs=[
            whole,
            whole,
            pl.BlockSpec((1, info.shape[1], LANES), lambda m, jb: (first + step * m, 0, jb)),
        ],
        out_specs=pl.BlockSpec((1, n_items, LANES), lambda m, jb: (m, 0, jb)),
        compiler_params=pltpu.CompilerParams(vmem_limit_bytes=48 * 1024 * 1024),
    )(x_hi, x_lo, info)


def split_row(row, width):
    pad = [(0, 0)] * (row.ndim - 1) + [(0, width - row.shape[-1])]
    padded = jnp.pad(row, pad)
    rounded = lax.reduce_precision(padded, exponent_bits=8, mantissa_bits=7)
    return rounded.astype(jnp.bfloat16), (padded - rounded).astype(jnp.bfloat16)


def ready_step(i, lat_rows):
    below = ROWS_OUT - 1 - i if i < ROWS_OUT else -1
    above = i + ROWS_OUT - lat_rows
    return max(below, above)


def vertical_mix(raw, bands):
    n_levels = raw.shape[-2]
    pad = [(0, 0)] * raw.ndim
    pad[-2] = (2, 2)
    stacked = jnp.pad(raw, pad)
    lead = (None,) * (raw.ndim - 3)
    mixed = bands[lead + (slice(None), 0, slice(None), None)] * stacked[..., 0:n_levels, :]
    for shift_k in range(1, 5):
        mixed = mixed + bands[lead + (slice(None), shift_k, slice(None), None)] * stacked[
            ..., shift_k : shift_k + n_levels, :
        ]
    return mixed


def widen(row):
    left, right = shifted(row, "lon", HALO, row.ndim - 1, True)
    return jnp.concatenate([left, row, right], axis=row.ndim - 1)


def on_device(fields, weights, stencil, bands):
    n_fields, n_levels, lat_rows, lon_cols = fields.shape
    n_items = n_fields * n_levels

    count = lax.axis_size("lat")
    forward = [(i, i + 1) for i in range(count - 1)]
    backward = [(target, source) for source, target in forward]
    below = [None] * ROWS_OUT
    above = [None] * ROWS_OUT
    previous = None
    for step in range(ROWS_OUT):
        h_below = ROWS_OUT - 1 - step
        src_below = fields[:, :, lat_rows - ROWS_OUT + h_below, :]
        src_above = fields[:, :, step, :]
        if previous is not None:
            src_below, src_above, _ = lax.optimization_barrier((src_below, src_above, previous))
        below[h_below] = lax.ppermute(src_below, "lat", forward)
        above[step] = lax.ppermute(src_above, "lat", backward)
        previous = (below[h_below], above[step])

    rows_major = jnp.transpose(fields, (2, 0, 1, 3))
    tile = vertical_mix(rows_major, bands).reshape(lat_rows, n_items, lon_cols)
    wide = widen(tile)
    halo_raw = below + above
    width = lon_cols + LANES

    lat_start = lax.axis_index("lat") * lat_rows
    lon_start = lax.axis_index("lon") * lon_cols
    line_len = lon_cols * lax.axis_size("lon")
    row_g = lat_start + jnp.arange(lat_rows, dtype=jnp.int32)[:, None]
    col_g = lon_start + jnp.arange(lon_cols, dtype=jnp.int32)[None, :]
    offset_r = (stencil[0] - row_g + ROWS_OUT).astype(jnp.float32)
    offset_d = jnp.mod(stencil[1] - col_g + HALO, line_len).astype(jnp.float32)
    info = jnp.concatenate(
        [
            jnp.transpose(weights, (1, 0, 2)),
            offset_r[:, None, :],
            offset_d[:, None, :],
            jnp.zeros((lat_rows, 6, lon_cols), jnp.float32),
        ],
        axis=1,
    )
    span = 2 * ROWS_OUT + 1
    groups = {}
    for i in range(lat_rows):
        groups.setdefault(ready_step(i, lat_rows), []).append(i)
    real_rows = [None] * lat_rows
    imag_rows = [None] * lat_rows
    done = None
    halo_wide = {}
    for key in sorted(groups):
        members = groups[key]
        needed = sorted({i + p for i in members for p in range(span)})
        fresh = [h for h in needed if (h < ROWS_OUT or h >= ROWS_OUT + lat_rows) and h not in halo_wide]
        raw = [halo_raw[h if h < ROWS_OUT else h - lat_rows] for h in fresh]
        if done is not None and raw:
            raw, _ = lax.optimization_barrier((raw, done))
        for h, r in zip(fresh, raw):
            halo_wide[h] = widen(vertical_mix(r, bands).reshape(n_items, lon_cols))
        stacked = jnp.stack(
            [halo_wide[h] if h in halo_wide else wide[h - ROWS_OUT] for h in needed]
        )
        x_hi, x_lo = split_row(stacked, width)
        bases = [needed.index(i) for i in members]
        departed = interpolate_rows(bases, x_hi, x_lo, info, members, lon_cols)
        gathered = lax.all_to_all(departed, "lon", split_axis=1, concat_axis=2, tiled=True)
        real_part, imag_part = spectrum(jnp.transpose(gathered, (1, 0, 2)))
        for slot, i in enumerate(members):
            real_rows[i] = real_part[:, slot : slot + 1]
            imag_rows[i] = imag_part[:, slot : slot + 1]
        done = (real_part, imag_part)
    return (jnp.concatenate(real_rows, axis=1), jnp.concatenate(imag_rows, axis=1))


def solution(mesh):
    placed = (P(None, None, "lat", "lon"), P(None, "lat", "lon"), P(None, "lat", "lon"), P())
    return jax.shard_map(
        on_device,
        mesh=mesh,
        in_specs=placed,
        out_specs=(P("lon", "lat", None), P("lon", "lat", None)),
        check_vma=False,
    )
```

```python
import functools
import math

import jax
import jax.numpy as jnp
from jax import lax
from jax.experimental import pallas as pl
from jax.experimental.pallas import tpu as pltpu
from jax.sharding import PartitionSpec as P

RADIX = 64
NK = 1280
HALO = 16
ROWS_OUT = 3
TAPS = 4
LANES = 128
WINDOW = 256


def shifted(block, axis, width, dim, periodic):
    count = lax.axis_size(axis)
    forward = [(i, i + 1) for i in range(count - 1)]
    if periodic:
        forward.append((count - 1, 0))
    backward = [(target, source) for source, target in forward]
    low = lax.ppermute(
        lax.slice_in_dim(block, block.shape[dim] - width, None, axis=dim), axis, forward
    )
    high = lax.ppermute(lax.slice_in_dim(block, 0, width, axis=dim), axis, backward)
    return low, high


def spectrum(block):
    n_items, n_lines, line_len = block.shape
    highest = lax.Precision.HIGHEST
    folded = block.reshape(n_items * n_lines, RADIX, RADIX)
    digits = jnp.arange(RADIX, dtype=jnp.int32)
    angle_one = (
        2.0 * math.pi / RADIX * (digits[:, None] * digits[None, :] % RADIX).astype(jnp.float32)
    )
    first_table = jnp.concatenate([jnp.cos(angle_one), -jnp.sin(angle_one)], axis=1)
    partial_value = jnp.einsum("rab,ac->rbc", folded, first_table, precision=highest)
    angle_two = (
        2.0
        * math.pi
        / line_len
        * (digits[:, None] * digits[None, :] % line_len).astype(jnp.float32)
    )
    cos_two = jnp.cos(angle_two)
    sin_two = jnp.sin(angle_two)
    part_re = partial_value[..., :RADIX]
    part_im = partial_value[..., RADIX:]
    twisted = jnp.concatenate(
        [part_re * cos_two + part_im * sin_two, part_im * cos_two - part_re * sin_two], axis=-1
    )
    quotients = jnp.arange(NK // RADIX, dtype=jnp.int32)
    angle_three = (
        2.0 * math.pi / RADIX * (digits[:, None] * quotients[None, :] % RADIX).astype(jnp.float32)
    )
    with_cos = jnp.einsum("rbc,bq->rqc", twisted, jnp.cos(angle_three), precision=highest)
    with_sin = jnp.einsum("rbc,bq->rqc", twisted, jnp.sin(angle_three), precision=highest)
    scale = 1.0 / math.sqrt(line_len)
    real_part = (with_cos[..., :RADIX] + with_sin[..., RADIX:]) * scale
    imag_part = (with_cos[..., RADIX:] - with_sin[..., :RADIX]) * scale
    return (real_part.reshape(n_items, n_lines, NK), imag_part.reshape(n_items, n_lines, NK))


def interp_kernel(local, lat_rows, *refs):
    if local:
        hi_ref, lo_ref, info_ref, out_ref, acc_ref = refs
    else:
        hi_ref, lo_ref, info_ref, base_ref, out_ref, acc_ref = refs
    row = pl.program_id(0)
    block = pl.program_id(1)
    info = info_ref[0]
    offset_r = info[16:17, :]
    offset_d = info[17:18, :]
    c_index = lax.broadcasted_iota(jnp.int32, (WINDOW, LANES), 0).astype(jnp.float32)
    j_index = lax.broadcasted_iota(jnp.int32, (WINDOW, LANES), 1).astype(jnp.float32)
    tap = c_index - j_index - offset_d
    masks = [tap == float(b) for b in range(TAPS)]
    start = pl.multiple_of(block * LANES, LANES)
    if local:
        acc_ref[...] = jnp.zeros(acc_ref.shape, jnp.float32)
    else:
        acc_ref[...] = base_ref[0]
    n_stack = hi_ref.shape[0]
    for p in range(2 * ROWS_OUT + 1):
        h = row + p
        if local:
            valid = jnp.logical_and(h >= ROWS_OUT, h < ROWS_OUT + lat_rows)
            index = h - ROWS_OUT
        else:
            valid = jnp.logical_or(h < ROWS_OUT, h >= ROWS_OUT + lat_rows)
            index = jnp.where(h < ROWS_OUT, h, h - lat_rows)
        index = jnp.clip(index, 0, n_stack - 1)

        @pl.when(valid)
        def _(p=p, index=index):
            picked = []
            for b in range(TAPS):
                value = jnp.zeros_like(offset_r)
                for a in range(TAPS):
                    if 0 <= p - a <= ROWS_OUT:
                        value = jnp.where(offset_r == float(p - a), info[4 * a + b : 4 * a + b + 1, :], value)
                picked.append(value)
            matrix = jnp.where(
                masks[0],
                picked[0],
                jnp.where(masks[1], picked[1], jnp.where(masks[2], picked[2], jnp.where(masks[3], picked[3], 0.0))),
            )
            m_hi = matrix.astype(jnp.bfloat16)
            m_lo = (matrix - m_hi.astype(jnp.float32)).astype(jnp.bfloat16)
            x_hi = hi_ref[index, :, pl.ds(start, WINDOW)]
            x_lo = lo_ref[index, :, pl.ds(start, WINDOW)]
            total = jnp.dot(x_hi, m_hi, preferred_element_type=jnp.float32)
            total = total + jnp.dot(x_hi, m_lo, preferred_element_type=jnp.float32)
            total = total + jnp.dot(x_lo, m_hi, preferred_element_type=jnp.float32)
            acc_ref[...] += total

    out_ref[0] = acc_ref[...]


def interpolate(x_hi, x_lo, info, lat_rows, lon_cols, base=None):
    n_rows, n_items, width = x_hi.shape
    blocks = lon_cols // LANES
    whole = pl.BlockSpec((n_rows, n_items, width), lambda i, jb: (0, 0, 0))
    tile = pl.BlockSpec((1, n_items, LANES), lambda i, jb: (i, 0, jb))
    specs = [whole, whole, pl.BlockSpec((1, info.shape[1], LANES), lambda i, jb: (i, 0, jb))]
    operands = [x_hi, x_lo, info]
    if base is not None:
        specs.append(tile)
        operands.append(base)
    return pl.pallas_call(
        functools.partial(interp_kernel, base is None, lat_rows),
        out_shape=jax.ShapeDtypeStruct((lat_rows, n_items, lon_cols), jnp.float32),
        grid=(lat_rows, blocks),
        in_specs=specs,
        out_specs=tile,
        scratch_shapes=[pltpu.VMEM((n_items, LANES), jnp.float32)],
        compiler_params=pltpu.CompilerParams(vmem_limit_bytes=48 * 1024 * 1024),
    )(*operands)


def vertical_mix(raw, bands):
    n_levels = raw.shape[-2]
    pad = [(0, 0)] * raw.ndim
    pad[-2] = (2, 2)
    stacked = jnp.pad(raw, pad)
    lead = (None,) * (raw.ndim - 3)
    mixed = bands[lead + (slice(None), 0, slice(None), None)] * stacked[..., 0:n_levels, :]
    for shift_k in range(1, 5):
        mixed = mixed + bands[lead + (slice(None), shift_k, slice(None), None)] * stacked[
            ..., shift_k : shift_k + n_levels, :
        ]
    return mixed


def widen(block):
    left, right = shifted(block, "lon", HALO, block.ndim - 1, True)
    return jnp.concatenate([left, block, right], axis=block.ndim - 1)


def split_rows(rows, width):
    pad = [(0, 0)] * (rows.ndim - 1) + [(0, width - rows.shape[-1])]
    padded = jnp.pad(rows, pad)
    rounded = lax.reduce_precision(padded, exponent_bits=8, mantissa_bits=7)
    return rounded.astype(jnp.bfloat16), (padded - rounded).astype(jnp.bfloat16)


def on_device(fields, weights, stencil, bands):
    n_fields, n_levels, lat_rows, lon_cols = fields.shape
    n_items = n_fields * n_levels
    below_raw, above_raw = shifted(fields, "lat", ROWS_OUT, 2, False)

    width = lon_cols + LANES
    local_rows = vertical_mix(jnp.transpose(fields, (2, 0, 1, 3)), bands)
    local_hi, local_lo = split_rows(widen(local_rows.reshape(lat_rows, n_items, lon_cols)), width)

    lat_start = lax.axis_index("lat") * lat_rows
    lon_start = lax.axis_index("lon") * lon_cols
    line_len = lon_cols * lax.axis_size("lon")
    row_g = lat_start + jnp.arange(lat_rows, dtype=jnp.int32)[:, None]
    col_g = lon_start + jnp.arange(lon_cols, dtype=jnp.int32)[None, :]
    offset_r = (stencil[0] - row_g + ROWS_OUT).astype(jnp.float32)
    offset_d = jnp.mod(stencil[1] - col_g + HALO, line_len).astype(jnp.float32)
    info = jnp.concatenate(
        [
            jnp.transpose(weights, (1, 0, 2)),
            offset_r[:, None, :],
            offset_d[:, None, :],
            jnp.zeros((lat_rows, 6, lon_cols), jnp.float32),
        ],
        axis=1,
    )
    partial = interpolate(local_hi, local_lo, info, lat_rows, lon_cols)

    below_raw, above_raw, partial = lax.optimization_barrier((below_raw, above_raw, partial))
    halo_raw = jnp.concatenate([below_raw, above_raw], axis=2)
    halo_rows = vertical_mix(jnp.transpose(halo_raw, (2, 0, 1, 3)), bands)
    halo_hi, halo_lo = split_rows(widen(halo_rows.reshape(2 * ROWS_OUT, n_items, lon_cols)), width)
    departed = interpolate(halo_hi, halo_lo, info, lat_rows, lon_cols, base=partial)

    gathered = lax.all_to_all(departed, "lon", split_axis=1, concat_axis=2, tiled=True)
    lines = jnp.transpose(gathered, (1, 0, 2))
    real_part, imag_part = spectrum(lines)
    return (real_part, imag_part)


def solution(mesh):
    placed = (P(None, None, "lat", "lon"), P(None, "lat", "lon"), P(None, "lat", "lon"), P())
    return jax.shard_map(
        on_device,
        mesh=mesh,
        in_specs=placed,
        out_specs=(P("lon", "lat", None), P("lon", "lat", None)),
        check_vma=False,
    )
```

```python
import functools
import math

import jax
import jax.numpy as jnp
from jax import lax
from jax.experimental import pallas as pl
from jax.experimental.pallas import tpu as pltpu
from jax.sharding import PartitionSpec as P

RADIX = 64
NK = 1280
HALO = 16
ROWS_OUT = 3
TAPS = 4
LANES = 128
WINDOW = 256


def shifted(block, axis, width, dim, periodic):
    count = lax.axis_size(axis)
    forward = [(i, i + 1) for i in range(count - 1)]
    if periodic:
        forward.append((count - 1, 0))
    backward = [(target, source) for source, target in forward]
    low = lax.ppermute(
        lax.slice_in_dim(block, block.shape[dim] - width, None, axis=dim), axis, forward
    )
    high = lax.ppermute(lax.slice_in_dim(block, 0, width, axis=dim), axis, backward)
    return low, high


def spectrum(block):
    n_items, n_lines, line_len = block.shape
    highest = lax.Precision.HIGHEST
    folded = block.reshape(n_items * n_lines, RADIX, RADIX)
    digits = jnp.arange(RADIX, dtype=jnp.int32)
    angle_one = (
        2.0 * math.pi / RADIX * (digits[:, None] * digits[None, :] % RADIX).astype(jnp.float32)
    )
    first_table = jnp.concatenate([jnp.cos(angle_one), -jnp.sin(angle_one)], axis=1)
    partial_value = jnp.einsum("rab,ac->rbc", folded, first_table, precision=highest)
    angle_two = (
        2.0
        * math.pi
        / line_len
        * (digits[:, None] * digits[None, :] % line_len).astype(jnp.float32)
    )
    cos_two = jnp.cos(angle_two)
    sin_two = jnp.sin(angle_two)
    part_re = partial_value[..., :RADIX]
    part_im = partial_value[..., RADIX:]
    twisted = jnp.concatenate(
        [part_re * cos_two + part_im * sin_two, part_im * cos_two - part_re * sin_two], axis=-1
    )
    quotients = jnp.arange(NK // RADIX, dtype=jnp.int32)
    angle_three = (
        2.0 * math.pi / RADIX * (digits[:, None] * quotients[None, :] % RADIX).astype(jnp.float32)
    )
    with_cos = jnp.einsum("rbc,bq->rqc", twisted, jnp.cos(angle_three), precision=highest)
    with_sin = jnp.einsum("rbc,bq->rqc", twisted, jnp.sin(angle_three), precision=highest)
    scale = 1.0 / math.sqrt(line_len)
    real_part = (with_cos[..., :RADIX] + with_sin[..., RADIX:]) * scale
    imag_part = (with_cos[..., RADIX:] - with_sin[..., :RADIX]) * scale
    return (real_part.reshape(n_items, n_lines, NK), imag_part.reshape(n_items, n_lines, NK))


def interp_kernel(local, lat_rows, *refs):
    if local:
        hi_ref, lo_ref, info_ref, out_ref = refs
    else:
        hi_ref, lo_ref, info_ref, base_ref, out_ref = refs
    block = pl.program_id(0)
    start = pl.multiple_of(block * LANES, LANES)
    c_index = lax.broadcasted_iota(jnp.int32, (WINDOW, LANES), 0).astype(jnp.float32)
    j_index = lax.broadcasted_iota(jnp.int32, (WINDOW, LANES), 1).astype(jnp.float32)
    for row in range(lat_rows):
        info = info_ref[row]
        offset_r = info[16:17, :]
        offset_d = info[17:18, :]
        tap = c_index - j_index - offset_d
        masks = [tap == float(b) for b in range(TAPS)]
        if local:
            acc = jnp.zeros(out_ref.shape[1:], jnp.float32)
        else:
            acc = base_ref[row]
        for p in range(2 * ROWS_OUT + 1):
            h = row + p
            inside = ROWS_OUT <= h < ROWS_OUT + lat_rows
            if inside != local:
                continue
            if local:
                index = h - ROWS_OUT
            else:
                index = h if h < ROWS_OUT else h - lat_rows
            picked = []
            for b in range(TAPS):
                value = jnp.zeros_like(offset_r)
                for a in range(TAPS):
                    if 0 <= p - a <= ROWS_OUT:
                        value = jnp.where(offset_r == float(p - a), info[4 * a + b : 4 * a + b + 1, :], value)
                picked.append(value)
            matrix = jnp.where(
                masks[0],
                picked[0],
                jnp.where(masks[1], picked[1], jnp.where(masks[2], picked[2], jnp.where(masks[3], picked[3], 0.0))),
            )
            m_hi = matrix.astype(jnp.bfloat16)
            m_lo = (matrix - m_hi.astype(jnp.float32)).astype(jnp.bfloat16)
            x_hi = hi_ref[index, :, pl.ds(start, WINDOW)]
            x_lo = lo_ref[index, :, pl.ds(start, WINDOW)]
            acc = acc + jnp.dot(x_hi, m_hi, preferred_element_type=jnp.float32)
            acc = acc + jnp.dot(x_hi, m_lo, preferred_element_type=jnp.float32)
            acc = acc + jnp.dot(x_lo, m_hi, preferred_element_type=jnp.float32)
        out_ref[row] = acc


def interpolate(x_hi, x_lo, info, lat_rows, lon_cols, base=None):
    n_rows, n_items, width = x_hi.shape
    blocks = lon_cols // LANES
    whole = pl.BlockSpec((n_rows, n_items, width), lambda jb: (0, 0, 0))
    tile = pl.BlockSpec((lat_rows, n_items, LANES), lambda jb: (0, 0, jb))
    specs = [whole, whole, pl.BlockSpec((lat_rows, info.shape[1], LANES), lambda jb: (0, 0, jb))]
    operands = [x_hi, x_lo, info]
    if base is not None:
        specs.append(tile)
        operands.append(base)
    return pl.pallas_call(
        functools.partial(interp_kernel, base is None, lat_rows),
        out_shape=jax.ShapeDtypeStruct((lat_rows, n_items, lon_cols), jnp.float32),
        grid=(blocks,),
        in_specs=specs,
        out_specs=tile,
        compiler_params=pltpu.CompilerParams(vmem_limit_bytes=48 * 1024 * 1024),
    )(*operands)


def vertical_mix(raw, bands):
    n_levels = raw.shape[-2]
    pad = [(0, 0)] * raw.ndim
    pad[-2] = (2, 2)
    stacked = jnp.pad(raw, pad)
    lead = (None,) * (raw.ndim - 3)
    mixed = bands[lead + (slice(None), 0, slice(None), None)] * stacked[..., 0:n_levels, :]
    for shift_k in range(1, 5):
        mixed = mixed + bands[lead + (slice(None), shift_k, slice(None), None)] * stacked[
            ..., shift_k : shift_k + n_levels, :
        ]
    return mixed


def widen(block):
    left, right = shifted(block, "lon", HALO, block.ndim - 1, True)
    return jnp.concatenate([left, block, right], axis=block.ndim - 1)


def split_rows(rows, width):
    pad = [(0, 0)] * (rows.ndim - 1) + [(0, width - rows.shape[-1])]
    padded = jnp.pad(rows, pad)
    rounded = lax.reduce_precision(padded, exponent_bits=8, mantissa_bits=7)
    return rounded.astype(jnp.bfloat16), (padded - rounded).astype(jnp.bfloat16)


def on_device(fields, weights, stencil, bands):
    n_fields, n_levels, lat_rows, lon_cols = fields.shape
    n_items = n_fields * n_levels
    below_raw, above_raw = shifted(fields, "lat", ROWS_OUT, 2, False)

    width = lon_cols + LANES
    local_rows = vertical_mix(jnp.transpose(fields, (2, 0, 1, 3)), bands)
    local_hi, local_lo = split_rows(widen(local_rows.reshape(lat_rows, n_items, lon_cols)), width)

    lat_start = lax.axis_index("lat") * lat_rows
    lon_start = lax.axis_index("lon") * lon_cols
    line_len = lon_cols * lax.axis_size("lon")
    row_g = lat_start + jnp.arange(lat_rows, dtype=jnp.int32)[:, None]
    col_g = lon_start + jnp.arange(lon_cols, dtype=jnp.int32)[None, :]
    offset_r = (stencil[0] - row_g + ROWS_OUT).astype(jnp.float32)
    offset_d = jnp.mod(stencil[1] - col_g + HALO, line_len).astype(jnp.float32)
    info = jnp.concatenate(
        [
            jnp.transpose(weights, (1, 0, 2)),
            offset_r[:, None, :],
            offset_d[:, None, :],
            jnp.zeros((lat_rows, 6, lon_cols), jnp.float32),
        ],
        axis=1,
    )
    partial = interpolate(local_hi, local_lo, info, lat_rows, lon_cols)

    below_raw, above_raw, partial = lax.optimization_barrier((below_raw, above_raw, partial))
    halo_raw = jnp.concatenate([below_raw, above_raw], axis=2)
    halo_rows = vertical_mix(jnp.transpose(halo_raw, (2, 0, 1, 3)), bands)
    halo_hi, halo_lo = split_rows(widen(halo_rows.reshape(2 * ROWS_OUT, n_items, lon_cols)), width)
    departed = interpolate(halo_hi, halo_lo, info, lat_rows, lon_cols, base=partial)

    gathered = lax.all_to_all(departed, "lon", split_axis=1, concat_axis=2, tiled=True)
    lines = jnp.transpose(gathered, (1, 0, 2))
    real_part, imag_part = spectrum(lines)
    return (real_part, imag_part)


def solution(mesh):
    placed = (P(None, None, "lat", "lon"), P(None, "lat", "lon"), P(None, "lat", "lon"), P())
    return jax.shard_map(
        on_device,
        mesh=mesh,
        in_specs=placed,
        out_specs=(P("lon", "lat", None), P("lon", "lat", None)),
        check_vma=False,
    )
```

```python
import functools
import math

import jax
import jax.numpy as jnp
from jax import lax
from jax.experimental import pallas as pl
from jax.experimental.pallas import tpu as pltpu
from jax.sharding import PartitionSpec as P

RADIX = 64
NK = 1280
HALO = 16
ROWS_OUT = 3
TAPS = 4
LANES = 128
WINDOW = 256


def shifted(block, axis, width, dim, periodic):
    count = lax.axis_size(axis)
    forward = [(i, i + 1) for i in range(count - 1)]
    if periodic:
        forward.append((count - 1, 0))
    backward = [(target, source) for source, target in forward]
    low = lax.ppermute(
        lax.slice_in_dim(block, block.shape[dim] - width, None, axis=dim), axis, forward
    )
    high = lax.ppermute(lax.slice_in_dim(block, 0, width, axis=dim), axis, backward)
    return low, high


def spectrum(block):
    n_items, n_lines, line_len = block.shape
    highest = lax.Precision.HIGH
    folded = block.reshape(n_items * n_lines, RADIX, RADIX)
    digits = jnp.arange(RADIX, dtype=jnp.int32)
    angle_one = (
        2.0 * math.pi / RADIX * (digits[:, None] * digits[None, :] % RADIX).astype(jnp.float32)
    )
    first_table = jnp.concatenate([jnp.cos(angle_one), -jnp.sin(angle_one)], axis=1)
    partial_value = jnp.einsum("rab,ac->rbc", folded, first_table, precision=highest)
    angle_two = (
        2.0
        * math.pi
        / line_len
        * (digits[:, None] * digits[None, :] % line_len).astype(jnp.float32)
    )
    cos_two = jnp.cos(angle_two)
    sin_two = jnp.sin(angle_two)
    part_re = partial_value[..., :RADIX]
    part_im = partial_value[..., RADIX:]
    twisted = jnp.concatenate(
        [part_re * cos_two + part_im * sin_two, part_im * cos_two - part_re * sin_two], axis=-1
    )
    quotients = jnp.arange(NK // RADIX, dtype=jnp.int32)
    angle_three = (
        2.0 * math.pi / RADIX * (digits[:, None] * quotients[None, :] % RADIX).astype(jnp.float32)
    )
    with_cos = jnp.einsum("rbc,bq->rqc", twisted, jnp.cos(angle_three), precision=highest)
    with_sin = jnp.einsum("rbc,bq->rqc", twisted, jnp.sin(angle_three), precision=highest)
    scale = 1.0 / math.sqrt(line_len)
    real_part = (with_cos[..., :RADIX] + with_sin[..., RADIX:]) * scale
    imag_part = (with_cos[..., RADIX:] - with_sin[..., :RADIX]) * scale
    return (real_part.reshape(n_items, n_lines, NK), imag_part.reshape(n_items, n_lines, NK))


def interp_kernel(local, lat_rows, *refs):
    if local:
        hi_ref, lo_ref, info_ref, out_ref = refs
    else:
        hi_ref, lo_ref, info_ref, base_ref, out_ref = refs
    block = pl.program_id(0)
    start = pl.multiple_of(block * LANES, LANES)
    c_index = lax.broadcasted_iota(jnp.int32, (WINDOW, LANES), 0).astype(jnp.float32)
    j_index = lax.broadcasted_iota(jnp.int32, (WINDOW, LANES), 1).astype(jnp.float32)
    for row in range(lat_rows):
        info = info_ref[row]
        offset_r = info[16:17, :]
        offset_d = info[17:18, :]
        tap = c_index - j_index - offset_d
        masks = [tap == float(b) for b in range(TAPS)]
        if local:
            acc = jnp.zeros(out_ref.shape[1:], jnp.float32)
        else:
            acc = base_ref[row]
        for p in range(2 * ROWS_OUT + 1):
            h = row + p
            inside = ROWS_OUT <= h < ROWS_OUT + lat_rows
            if inside != local:
                continue
            if local:
                index = h - ROWS_OUT
            else:
                index = h if h < ROWS_OUT else h - lat_rows
            picked = []
            for b in range(TAPS):
                value = jnp.zeros_like(offset_r)
                for a in range(TAPS):
                    if 0 <= p - a <= ROWS_OUT:
                        value = jnp.where(offset_r == float(p - a), info[4 * a + b : 4 * a + b + 1, :], value)
                picked.append(value)
            matrix = jnp.where(
                masks[0],
                picked[0],
                jnp.where(masks[1], picked[1], jnp.where(masks[2], picked[2], jnp.where(masks[3], picked[3], 0.0))),
            )
            m_hi = matrix.astype(jnp.bfloat16)
            m_lo = (matrix - m_hi.astype(jnp.float32)).astype(jnp.bfloat16)
            x_hi = hi_ref[index, :, pl.ds(start, WINDOW)]
            x_lo = lo_ref[index, :, pl.ds(start, WINDOW)]
            acc = acc + jnp.dot(x_hi, m_hi, preferred_element_type=jnp.float32)
            acc = acc + jnp.dot(x_hi, m_lo, preferred_element_type=jnp.float32)
            acc = acc + jnp.dot(x_lo, m_hi, preferred_element_type=jnp.float32)
        out_ref[row] = acc


def interpolate(x_hi, x_lo, info, lat_rows, lon_cols, base=None):
    n_rows, n_items, width = x_hi.shape
    blocks = lon_cols // LANES
    whole = pl.BlockSpec((n_rows, n_items, width), lambda jb: (0, 0, 0))
    tile = pl.BlockSpec((lat_rows, n_items, LANES), lambda jb: (0, 0, jb))
    specs = [whole, whole, pl.BlockSpec((lat_rows, info.shape[1], LANES), lambda jb: (0, 0, jb))]
    operands = [x_hi, x_lo, info]
    if base is not None:
        specs.append(tile)
        operands.append(base)
    return pl.pallas_call(
        functools.partial(interp_kernel, base is None, lat_rows),
        out_shape=jax.ShapeDtypeStruct((lat_rows, n_items, lon_cols), jnp.float32),
        grid=(blocks,),
        in_specs=specs,
        out_specs=tile,
        compiler_params=pltpu.CompilerParams(vmem_limit_bytes=48 * 1024 * 1024),
    )(*operands)


def vertical_mix(raw, bands):
    n_levels = raw.shape[-2]
    pad = [(0, 0)] * raw.ndim
    pad[-2] = (2, 2)
    stacked = jnp.pad(raw, pad)
    lead = (None,) * (raw.ndim - 3)
    mixed = bands[lead + (slice(None), 0, slice(None), None)] * stacked[..., 0:n_levels, :]
    for shift_k in range(1, 5):
        mixed = mixed + bands[lead + (slice(None), shift_k, slice(None), None)] * stacked[
            ..., shift_k : shift_k + n_levels, :
        ]
    return mixed


def widen(block):
    left, right = shifted(block, "lon", HALO, block.ndim - 1, True)
    return jnp.concatenate([left, block, right], axis=block.ndim - 1)


def split_rows(rows, width):
    pad = [(0, 0)] * (rows.ndim - 1) + [(0, width - rows.shape[-1])]
    padded = jnp.pad(rows, pad)
    rounded = lax.reduce_precision(padded, exponent_bits=8, mantissa_bits=7)
    return rounded.astype(jnp.bfloat16), (padded - rounded).astype(jnp.bfloat16)


def on_device(fields, weights, stencil, bands):
    n_fields, n_levels, lat_rows, lon_cols = fields.shape
    n_items = n_fields * n_levels
    below_raw, above_raw = shifted(fields, "lat", ROWS_OUT, 2, False)

    width = lon_cols + LANES
    local_rows = vertical_mix(jnp.transpose(fields, (2, 0, 1, 3)), bands)
    local_hi, local_lo = split_rows(widen(local_rows.reshape(lat_rows, n_items, lon_cols)), width)

    lat_start = lax.axis_index("lat") * lat_rows
    lon_start = lax.axis_index("lon") * lon_cols
    line_len = lon_cols * lax.axis_size("lon")
    row_g = lat_start + jnp.arange(lat_rows, dtype=jnp.int32)[:, None]
    col_g = lon_start + jnp.arange(lon_cols, dtype=jnp.int32)[None, :]
    offset_r = (stencil[0] - row_g + ROWS_OUT).astype(jnp.float32)
    offset_d = jnp.mod(stencil[1] - col_g + HALO, line_len).astype(jnp.float32)
    info = jnp.concatenate(
        [
            jnp.transpose(weights, (1, 0, 2)),
            offset_r[:, None, :],
            offset_d[:, None, :],
            jnp.zeros((lat_rows, 6, lon_cols), jnp.float32),
        ],
        axis=1,
    )
    partial = interpolate(local_hi, local_lo, info, lat_rows, lon_cols)

    below_raw, above_raw, partial = lax.optimization_barrier((below_raw, above_raw, partial))
    halo_raw = jnp.concatenate([below_raw, above_raw], axis=2)
    halo_rows = vertical_mix(jnp.transpose(halo_raw, (2, 0, 1, 3)), bands)
    halo_hi, halo_lo = split_rows(widen(halo_rows.reshape(2 * ROWS_OUT, n_items, lon_cols)), width)
    departed = interpolate(halo_hi, halo_lo, info, lat_rows, lon_cols, base=partial)

    gathered = lax.all_to_all(departed, "lon", split_axis=1, concat_axis=2, tiled=True)
    real_part, imag_part = spectrum(gathered)
    return (jnp.transpose(real_part, (1, 0, 2)), jnp.transpose(imag_part, (1, 0, 2)))


def solution(mesh):
    placed = (P(None, None, "lat", "lon"), P(None, "lat", "lon"), P(None, "lat", "lon"), P())
    return jax.shard_map(
        on_device,
        mesh=mesh,
        in_specs=placed,
        out_specs=(P("lon", "lat", None), P("lon", "lat", None)),
        check_vma=False,
    )
```

```python
import functools
import math

import jax
import jax.numpy as jnp
from jax import lax
from jax.experimental import pallas as pl
from jax.experimental.pallas import tpu as pltpu
from jax.sharding import PartitionSpec as P

RADIX = 64
NK = 1280
HALO = 16
ROWS_OUT = 3
TAPS = 4
LANES = 128
WINDOW = 256


def shifted(block, axis, width, dim, periodic):
    count = lax.axis_size(axis)
    forward = [(i, i + 1) for i in range(count - 1)]
    if periodic:
        forward.append((count - 1, 0))
    backward = [(target, source) for source, target in forward]
    low = lax.ppermute(
        lax.slice_in_dim(block, block.shape[dim] - width, None, axis=dim), axis, forward
    )
    high = lax.ppermute(lax.slice_in_dim(block, 0, width, axis=dim), axis, backward)
    return low, high


def spectrum(block):
    n_items, n_lines, line_len = block.shape
    highest = lax.Precision.HIGH
    folded = block.reshape(n_items * n_lines, RADIX, RADIX)
    digits = jnp.arange(RADIX, dtype=jnp.int32)
    angle_one = (
        2.0 * math.pi / RADIX * (digits[:, None] * digits[None, :] % RADIX).astype(jnp.float32)
    )
    first_table = jnp.concatenate([jnp.cos(angle_one), -jnp.sin(angle_one)], axis=1)
    partial_value = jnp.einsum("rab,ac->rbc", folded, first_table, precision=highest)
    angle_two = (
        2.0
        * math.pi
        / line_len
        * (digits[:, None] * digits[None, :] % line_len).astype(jnp.float32)
    )
    cos_two = jnp.cos(angle_two)
    sin_two = jnp.sin(angle_two)
    part_re = partial_value[..., :RADIX]
    part_im = partial_value[..., RADIX:]
    twisted = jnp.concatenate(
        [part_re * cos_two + part_im * sin_two, part_im * cos_two - part_re * sin_two], axis=-1
    )
    quotients = jnp.arange(NK // RADIX, dtype=jnp.int32)
    angle_three = (
        2.0 * math.pi / RADIX * (digits[:, None] * quotients[None, :] % RADIX).astype(jnp.float32)
    )
    with_cos = jnp.einsum("rbc,bq->rqc", twisted, jnp.cos(angle_three), precision=highest)
    with_sin = jnp.einsum("rbc,bq->rqc", twisted, jnp.sin(angle_three), precision=highest)
    scale = 1.0 / math.sqrt(line_len)
    real_part = (with_cos[..., :RADIX] + with_sin[..., RADIX:]) * scale
    imag_part = (with_cos[..., RADIX:] - with_sin[..., :RADIX]) * scale
    return (real_part.reshape(n_items, n_lines, NK), imag_part.reshape(n_items, n_lines, NK))


def interp_kernel(local, lat_rows, out_rows, *refs):
    if local:
        hi_ref, lo_ref, info_ref, out_ref = refs
    else:
        hi_ref, lo_ref, info_ref, base_ref, out_ref = refs
    block = pl.program_id(0)
    start = pl.multiple_of(block * LANES, LANES)
    c_index = lax.broadcasted_iota(jnp.int32, (WINDOW, LANES), 0).astype(jnp.float32)
    j_index = lax.broadcasted_iota(jnp.int32, (WINDOW, LANES), 1).astype(jnp.float32)
    for slot, row in enumerate(out_rows):
        info = info_ref[row]
        offset_r = info[16:17, :]
        offset_d = info[17:18, :]
        tap = c_index - j_index - offset_d
        masks = [tap == float(b) for b in range(TAPS)]
        if local:
            acc = jnp.zeros(out_ref.shape[1:], jnp.float32)
        else:
            acc = base_ref[row]
        for p in range(2 * ROWS_OUT + 1):
            h = row + p
            inside = ROWS_OUT <= h < ROWS_OUT + lat_rows
            if inside != local:
                continue
            if local:
                index = h - ROWS_OUT
            else:
                index = h if h < ROWS_OUT else h - lat_rows
            picked = []
            for b in range(TAPS):
                value = jnp.zeros_like(offset_r)
                for a in range(TAPS):
                    if 0 <= p - a <= ROWS_OUT:
                        value = jnp.where(offset_r == float(p - a), info[4 * a + b : 4 * a + b + 1, :], value)
                picked.append(value)
            matrix = jnp.where(
                masks[0],
                picked[0],
                jnp.where(masks[1], picked[1], jnp.where(masks[2], picked[2], jnp.where(masks[3], picked[3], 0.0))),
            )
            m_hi = matrix.astype(jnp.bfloat16)
            m_lo = (matrix - m_hi.astype(jnp.float32)).astype(jnp.bfloat16)
            x_hi = hi_ref[index, :, pl.ds(start, WINDOW)]
            x_lo = lo_ref[index, :, pl.ds(start, WINDOW)]
            acc = acc + jnp.dot(x_hi, m_hi, preferred_element_type=jnp.float32)
            acc = acc + jnp.dot(x_hi, m_lo, preferred_element_type=jnp.float32)
            acc = acc + jnp.dot(x_lo, m_hi, preferred_element_type=jnp.float32)
        out_ref[slot] = acc


def interpolate(x_hi, x_lo, info, lat_rows, lon_cols, base=None, out_rows=None):
    n_rows, n_items, width = x_hi.shape
    blocks = lon_cols // LANES
    if out_rows is None:
        out_rows = tuple(range(lat_rows))
    whole = pl.BlockSpec((n_rows, n_items, width), lambda jb: (0, 0, 0))
    tile = pl.BlockSpec((lat_rows, n_items, LANES), lambda jb: (0, 0, jb))
    out_tile = pl.BlockSpec((len(out_rows), n_items, LANES), lambda jb: (0, 0, jb))
    specs = [whole, whole, pl.BlockSpec((lat_rows, info.shape[1], LANES), lambda jb: (0, 0, jb))]
    operands = [x_hi, x_lo, info]
    if base is not None:
        specs.append(tile)
        operands.append(base)
    return pl.pallas_call(
        functools.partial(interp_kernel, base is None, lat_rows, tuple(out_rows)),
        out_shape=jax.ShapeDtypeStruct((len(out_rows), n_items, lon_cols), jnp.float32),
        grid=(blocks,),
        in_specs=specs,
        out_specs=out_tile,
        compiler_params=pltpu.CompilerParams(vmem_limit_bytes=48 * 1024 * 1024),
    )(*operands)


def vertical_mix(raw, bands):
    n_levels = raw.shape[-2]
    pad = [(0, 0)] * raw.ndim
    pad[-2] = (2, 2)
    stacked = jnp.pad(raw, pad)
    lead = (None,) * (raw.ndim - 3)
    mixed = bands[lead + (slice(None), 0, slice(None), None)] * stacked[..., 0:n_levels, :]
    for shift_k in range(1, 5):
        mixed = mixed + bands[lead + (slice(None), shift_k, slice(None), None)] * stacked[
            ..., shift_k : shift_k + n_levels, :
        ]
    return mixed


def widen(block):
    left, right = shifted(block, "lon", HALO, block.ndim - 1, True)
    return jnp.concatenate([left, block, right], axis=block.ndim - 1)


def split_rows(rows, width):
    pad = [(0, 0)] * (rows.ndim - 1) + [(0, width - rows.shape[-1])]
    padded = jnp.pad(rows, pad)
    rounded = lax.reduce_precision(padded, exponent_bits=8, mantissa_bits=7)
    return rounded.astype(jnp.bfloat16), (padded - rounded).astype(jnp.bfloat16)


def on_device(fields, weights, stencil, bands):
    n_fields, n_levels, lat_rows, lon_cols = fields.shape
    n_items = n_fields * n_levels
    below_raw, above_raw = shifted(fields, "lat", ROWS_OUT, 2, False)

    width = lon_cols + LANES
    local_rows = vertical_mix(jnp.transpose(fields, (2, 0, 1, 3)), bands)
    local_hi, local_lo = split_rows(widen(local_rows.reshape(lat_rows, n_items, lon_cols)), width)

    lat_start = lax.axis_index("lat") * lat_rows
    lon_start = lax.axis_index("lon") * lon_cols
    line_len = lon_cols * lax.axis_size("lon")
    row_g = lat_start + jnp.arange(lat_rows, dtype=jnp.int32)[:, None]
    col_g = lon_start + jnp.arange(lon_cols, dtype=jnp.int32)[None, :]
    offset_r = (stencil[0] - row_g + ROWS_OUT).astype(jnp.float32)
    offset_d = jnp.mod(stencil[1] - col_g + HALO, line_len).astype(jnp.float32)
    info = jnp.concatenate(
        [
            jnp.transpose(weights, (1, 0, 2)),
            offset_r[:, None, :],
            offset_d[:, None, :],
            jnp.zeros((lat_rows, 6, lon_cols), jnp.float32),
        ],
        axis=1,
    )
    partial = interpolate(local_hi, local_lo, info, lat_rows, lon_cols)

    below_raw, above_raw, partial = lax.optimization_barrier((below_raw, above_raw, partial))
    halo_raw = jnp.concatenate([below_raw, above_raw], axis=2)
    halo_rows = vertical_mix(jnp.transpose(halo_raw, (2, 0, 1, 3)), bands)
    halo_hi, halo_lo = split_rows(widen(halo_rows.reshape(2 * ROWS_OUT, n_items, lon_cols)), width)
    half = max(1, lat_rows // 2)
    chunks = [tuple(range(lat_rows)[k : k + half]) for k in range(0, lat_rows, half)]
    real_parts = []
    imag_parts = []
    for out_rows in chunks:
        departed = interpolate(halo_hi, halo_lo, info, lat_rows, lon_cols, base=partial, out_rows=out_rows)
        gathered = lax.all_to_all(departed, "lon", split_axis=1, concat_axis=2, tiled=True)
        if real_parts:
            gathered, _ = lax.optimization_barrier((gathered, (real_parts[-1], imag_parts[-1])))
        real_part, imag_part = spectrum(gathered)
        real_parts.append(real_part)
        imag_parts.append(imag_part)
    real_part = jnp.concatenate(real_parts, axis=0)
    imag_part = jnp.concatenate(imag_parts, axis=0)
    return (jnp.transpose(real_part, (1, 0, 2)), jnp.transpose(imag_part, (1, 0, 2)))


def solution(mesh):
    placed = (P(None, None, "lat", "lon"), P(None, "lat", "lon"), P(None, "lat", "lon"), P())
    return jax.shard_map(
        on_device,
        mesh=mesh,
        in_specs=placed,
        out_specs=(P("lon", "lat", None), P("lon", "lat", None)),
        check_vma=False,
    )
```

```python
import functools
import math

import jax
import jax.numpy as jnp
from jax import lax
from jax.experimental import pallas as pl
from jax.experimental.pallas import tpu as pltpu
from jax.sharding import PartitionSpec as P

RADIX = 64
NK = 1280
HALO = 16
ROWS_OUT = 3
TAPS = 4
LANES = 128
WINDOW = 256


def shifted(block, axis, width, dim, periodic):
    count = lax.axis_size(axis)
    forward = [(i, i + 1) for i in range(count - 1)]
    if periodic:
        forward.append((count - 1, 0))
    backward = [(target, source) for source, target in forward]
    low = lax.ppermute(
        lax.slice_in_dim(block, block.shape[dim] - width, None, axis=dim), axis, forward
    )
    high = lax.ppermute(lax.slice_in_dim(block, 0, width, axis=dim), axis, backward)
    return low, high


def shifted_pair(to_next, to_previous, axis, periodic):
    count = lax.axis_size(axis)
    forward = [(i, i + 1) for i in range(count - 1)]
    if periodic:
        forward.append((count - 1, 0))
    backward = [(target, source) for source, target in forward]
    return lax.ppermute(to_next, axis, forward), lax.ppermute(to_previous, axis, backward)


def spectrum(block):
    n_items, n_lines, line_len = block.shape
    highest = lax.Precision.HIGH
    folded = block.reshape(n_items * n_lines, RADIX, RADIX)
    digits = jnp.arange(RADIX, dtype=jnp.int32)
    angle_one = (
        2.0 * math.pi / RADIX * (digits[:, None] * digits[None, :] % RADIX).astype(jnp.float32)
    )
    first_table = jnp.concatenate([jnp.cos(angle_one), -jnp.sin(angle_one)], axis=1)
    partial_value = jnp.einsum("rab,ac->rbc", folded, first_table, precision=highest)
    angle_two = (
        2.0
        * math.pi
        / line_len
        * (digits[:, None] * digits[None, :] % line_len).astype(jnp.float32)
    )
    cos_two = jnp.cos(angle_two)
    sin_two = jnp.sin(angle_two)
    part_re = partial_value[..., :RADIX]
    part_im = partial_value[..., RADIX:]
    twisted = jnp.concatenate(
        [part_re * cos_two + part_im * sin_two, part_im * cos_two - part_re * sin_two], axis=-1
    )
    quotients = jnp.arange(NK // RADIX, dtype=jnp.int32)
    angle_three = (
        2.0 * math.pi / RADIX * (digits[:, None] * quotients[None, :] % RADIX).astype(jnp.float32)
    )
    with_cos = jnp.einsum("rbc,bq->rqc", twisted, jnp.cos(angle_three), precision=highest)
    with_sin = jnp.einsum("rbc,bq->rqc", twisted, jnp.sin(angle_three), precision=highest)
    scale = 1.0 / math.sqrt(line_len)
    real_part = (with_cos[..., :RADIX] + with_sin[..., RADIX:]) * scale
    imag_part = (with_cos[..., RADIX:] - with_sin[..., :RADIX]) * scale
    return (real_part.reshape(n_items, n_lines, NK), imag_part.reshape(n_items, n_lines, NK))


def interp_kernel(local, lat_rows, *refs):
    if local:
        hi_ref, lo_ref, info_ref, out_ref = refs
    else:
        hi_ref, lo_ref, info_ref, base_ref, out_ref = refs
    block = pl.program_id(0)
    start = pl.multiple_of(block * LANES, LANES)
    c_index = lax.broadcasted_iota(jnp.int32, (WINDOW, LANES), 0).astype(jnp.float32)
    j_index = lax.broadcasted_iota(jnp.int32, (WINDOW, LANES), 1).astype(jnp.float32)
    for row in range(lat_rows):
        info = info_ref[row]
        offset_r = info[16:17, :]
        offset_d = info[17:18, :]
        tap = c_index - j_index - offset_d
        masks = [tap == float(b) for b in range(TAPS)]
        if local:
            acc = jnp.zeros(out_ref.shape[1:], jnp.float32)
        else:
            acc = base_ref[row]
        for p in range(2 * ROWS_OUT + 1):
            h = row + p
            inside = ROWS_OUT <= h < ROWS_OUT + lat_rows
            if inside != local:
                continue
            if local:
                index = h - ROWS_OUT
            else:
                index = h if h < ROWS_OUT else h - lat_rows
            picked = []
            for b in range(TAPS):
                value = jnp.zeros_like(offset_r)
                for a in range(TAPS):
                    if 0 <= p - a <= ROWS_OUT:
                        value = jnp.where(offset_r == float(p - a), info[4 * a + b : 4 * a + b + 1, :], value)
                picked.append(value)
            matrix = jnp.where(
                masks[0],
                picked[0],
                jnp.where(masks[1], picked[1], jnp.where(masks[2], picked[2], jnp.where(masks[3], picked[3], 0.0))),
            )
            m_hi = matrix.astype(jnp.bfloat16)
            m_lo = (matrix - m_hi.astype(jnp.float32)).astype(jnp.bfloat16)
            x_hi = hi_ref[index, :, pl.ds(start, WINDOW)]
            x_lo = lo_ref[index, :, pl.ds(start, WINDOW)]
            acc = acc + jnp.dot(x_hi, m_hi, preferred_element_type=jnp.float32)
            acc = acc + jnp.dot(x_hi, m_lo, preferred_element_type=jnp.float32)
            acc = acc + jnp.dot(x_lo, m_hi, preferred_element_type=jnp.float32)
        out_ref[row] = acc


def interpolate(x_hi, x_lo, info, lat_rows, lon_cols, base=None):
    n_rows, n_items, width = x_hi.shape
    blocks = lon_cols // LANES
    whole = pl.BlockSpec((n_rows, n_items, width), lambda jb: (0, 0, 0))
    tile = pl.BlockSpec((lat_rows, n_items, LANES), lambda jb: (0, 0, jb))
    specs = [whole, whole, pl.BlockSpec((lat_rows, info.shape[1], LANES), lambda jb: (0, 0, jb))]
    operands = [x_hi, x_lo, info]
    if base is not None:
        specs.append(tile)
        operands.append(base)
    return pl.pallas_call(
        functools.partial(interp_kernel, base is None, lat_rows),
        out_shape=jax.ShapeDtypeStruct((lat_rows, n_items, lon_cols), jnp.float32),
        grid=(blocks,),
        in_specs=specs,
        out_specs=tile,
        compiler_params=pltpu.CompilerParams(vmem_limit_bytes=48 * 1024 * 1024),
    )(*operands)


def vertical_mix(raw, bands):
    n_levels = raw.shape[-2]
    pad = [(0, 0)] * raw.ndim
    pad[-2] = (2, 2)
    stacked = jnp.pad(raw, pad)
    lead = (None,) * (raw.ndim - 3)
    mixed = bands[lead + (slice(None), 0, slice(None), None)] * stacked[..., 0:n_levels, :]
    for shift_k in range(1, 5):
        mixed = mixed + bands[lead + (slice(None), shift_k, slice(None), None)] * stacked[
            ..., shift_k : shift_k + n_levels, :
        ]
    return mixed


def widen(block):
    left, right = shifted(block, "lon", HALO, block.ndim - 1, True)
    return jnp.concatenate([left, block, right], axis=block.ndim - 1)


def split_rows(rows, width):
    pad = [(0, 0)] * (rows.ndim - 1) + [(0, width - rows.shape[-1])]
    padded = jnp.pad(rows, pad)
    rounded = lax.reduce_precision(padded, exponent_bits=8, mantissa_bits=7)
    return rounded.astype(jnp.bfloat16), (padded - rounded).astype(jnp.bfloat16)


def item_half(block, half, halves, parts):
    lead = block.shape[:-2]
    n_items, cols = block.shape[-2:]
    grouped = block.reshape(lead + (parts, halves, n_items // (parts * halves), cols))
    picked = lax.index_in_dim(grouped, half, axis=len(lead) + 1, keepdims=False)
    return picked.reshape(lead + (n_items // halves, cols))


def on_device(fields, weights, stencil, bands):
    n_fields, n_levels, lat_rows, lon_cols = fields.shape
    n_items = n_fields * n_levels
    parts = lax.axis_size("lon")
    halves = 2 if n_items % (parts * 16) == 0 else 1
    width = lon_cols + LANES

    mixed = vertical_mix(jnp.transpose(fields, (2, 0, 1, 3)), bands).reshape(lat_rows, n_items, lon_cols)

    lat_start = lax.axis_index("lat") * lat_rows
    lon_start = lax.axis_index("lon") * lon_cols
    line_len = lon_cols * parts
    row_g = lat_start + jnp.arange(lat_rows, dtype=jnp.int32)[:, None]
    col_g = lon_start + jnp.arange(lon_cols, dtype=jnp.int32)[None, :]
    offset_r = (stencil[0] - row_g + ROWS_OUT).astype(jnp.float32)
    offset_d = jnp.mod(stencil[1] - col_g + HALO, line_len).astype(jnp.float32)
    info = jnp.concatenate(
        [
            jnp.transpose(weights, (1, 0, 2)),
            offset_r[:, None, :],
            offset_d[:, None, :],
            jnp.zeros((lat_rows, 6, lon_cols), jnp.float32),
        ],
        axis=1,
    )

    tiles = [item_half(mixed, c, halves, parts) for c in range(halves)]
    received = []
    previous = None
    for c in range(halves):
        src_below = tiles[c][lat_rows - ROWS_OUT :]
        src_above = tiles[c][:ROWS_OUT]
        if previous is not None:
            src_below, src_above, _ = lax.optimization_barrier((src_below, src_above, previous))
        below, above = shifted_pair(src_below, src_above, "lat", False)
        received.append((below, above))
        previous = (below, above)
    partials = []
    for c in range(halves):
        local_hi, local_lo = split_rows(widen(tiles[c]), width)
        partials.append(interpolate(local_hi, local_lo, info, lat_rows, lon_cols))
    below0, above0, partials = lax.optimization_barrier((received[0][0], received[0][1], partials))
    received[0] = (below0, above0)

    real_parts = []
    imag_parts = []
    for c in range(halves):
        below, above = received[c]
        if real_parts:
            below, above, _ = lax.optimization_barrier((below, above, (real_parts[-1], imag_parts[-1])))
        halo_hi, halo_lo = split_rows(widen(jnp.concatenate([below, above], axis=0)), width)
        departed = interpolate(halo_hi, halo_lo, info, lat_rows, lon_cols, base=partials[c])
        gathered = lax.all_to_all(departed, "lon", split_axis=1, concat_axis=2, tiled=True)
        real_part, imag_part = spectrum(gathered)
        real_parts.append(real_part)
        imag_parts.append(imag_part)
    real_part = jnp.concatenate(real_parts, axis=1)
    imag_part = jnp.concatenate(imag_parts, axis=1)
    return (jnp.transpose(real_part, (1, 0, 2)), jnp.transpose(imag_part, (1, 0, 2)))


def solution(mesh):
    placed = (P(None, None, "lat", "lon"), P(None, "lat", "lon"), P(None, "lat", "lon"), P())
    return jax.shard_map(
        on_device,
        mesh=mesh,
        in_specs=placed,
        out_specs=(P("lon", "lat", None), P("lon", "lat", None)),
        check_vma=False,
    )
```

```python
import functools
import math

import jax
import jax.numpy as jnp
from jax import lax
from jax.experimental import pallas as pl
from jax.experimental.pallas import tpu as pltpu
from jax.sharding import PartitionSpec as P

RADIX = 64
NK = 1280
HALO = 16
ROWS_OUT = 3
TAPS = 4
LANES = 128
WINDOW = 256


def shifted(block, axis, width, dim, periodic):
    count = lax.axis_size(axis)
    forward = [(i, i + 1) for i in range(count - 1)]
    if periodic:
        forward.append((count - 1, 0))
    backward = [(target, source) for source, target in forward]
    low = lax.ppermute(
        lax.slice_in_dim(block, block.shape[dim] - width, None, axis=dim), axis, forward
    )
    high = lax.ppermute(lax.slice_in_dim(block, 0, width, axis=dim), axis, backward)
    return low, high


def spectrum(block):
    n_items, n_lines, line_len = block.shape
    highest = lax.Precision.HIGH
    folded = block.reshape(n_items * n_lines, RADIX, RADIX)
    digits = jnp.arange(RADIX, dtype=jnp.int32)
    angle_one = (
        2.0 * math.pi / RADIX * (digits[:, None] * digits[None, :] % RADIX).astype(jnp.float32)
    )
    first_table = jnp.concatenate([jnp.cos(angle_one), -jnp.sin(angle_one)], axis=1)
    partial_value = jnp.einsum("rab,ac->rbc", folded, first_table, precision=highest)
    angle_two = (
        2.0
        * math.pi
        / line_len
        * (digits[:, None] * digits[None, :] % line_len).astype(jnp.float32)
    )
    cos_two = jnp.cos(angle_two)
    sin_two = jnp.sin(angle_two)
    part_re = partial_value[..., :RADIX]
    part_im = partial_value[..., RADIX:]
    twisted = jnp.concatenate(
        [part_re * cos_two + part_im * sin_two, part_im * cos_two - part_re * sin_two], axis=-1
    )
    quotients = jnp.arange(NK // RADIX, dtype=jnp.int32)
    angle_three = (
        2.0 * math.pi / RADIX * (digits[:, None] * quotients[None, :] % RADIX).astype(jnp.float32)
    )
    with_cos = jnp.einsum("rbc,bq->rqc", twisted, jnp.cos(angle_three), precision=highest)
    with_sin = jnp.einsum("rbc,bq->rqc", twisted, jnp.sin(angle_three), precision=highest)
    scale = 1.0 / math.sqrt(line_len)
    real_part = (with_cos[..., :RADIX] + with_sin[..., RADIX:]) * scale
    imag_part = (with_cos[..., RADIX:] - with_sin[..., :RADIX]) * scale
    return (real_part.reshape(n_items, n_lines, NK), imag_part.reshape(n_items, n_lines, NK))


def interp_kernel(local, lat_rows, *refs):
    if local:
        hi_ref, lo_ref, info_ref, out_ref = refs
    else:
        hi_ref, lo_ref, info_ref, base_ref, out_ref = refs
    block = pl.program_id(0)
    start = pl.multiple_of(block * LANES, LANES)
    c_index = lax.broadcasted_iota(jnp.int32, (WINDOW, LANES), 0).astype(jnp.float32)
    j_index = lax.broadcasted_iota(jnp.int32, (WINDOW, LANES), 1).astype(jnp.float32)
    for row in range(lat_rows):
        info = info_ref[row]
        offset_r = info[16:17, :]
        offset_d = info[17:18, :]
        tap = c_index - j_index - offset_d
        masks = [tap == float(b) for b in range(TAPS)]
        if local:
            acc = jnp.zeros(out_ref.shape[1:], jnp.float32)
        else:
            acc = base_ref[row]
        for p in range(2 * ROWS_OUT + 1):
            h = row + p
            inside = ROWS_OUT <= h < ROWS_OUT + lat_rows
            if inside != local:
                continue
            if local:
                index = h - ROWS_OUT
            else:
                index = h if h < ROWS_OUT else h - lat_rows
            picked = []
            for b in range(TAPS):
                value = jnp.zeros_like(offset_r)
                for a in range(TAPS):
                    if 0 <= p - a <= ROWS_OUT:
                        value = jnp.where(offset_r == float(p - a), info[4 * a + b : 4 * a + b + 1, :], value)
                picked.append(value)
            matrix = jnp.where(
                masks[0],
                picked[0],
                jnp.where(masks[1], picked[1], jnp.where(masks[2], picked[2], jnp.where(masks[3], picked[3], 0.0))),
            )
            m_hi = matrix.astype(jnp.bfloat16)
            m_lo = (matrix - m_hi.astype(jnp.float32)).astype(jnp.bfloat16)
            x_hi = hi_ref[index, :, pl.ds(start, WINDOW)]
            x_lo = lo_ref[index, :, pl.ds(start, WINDOW)]
            acc = acc + jnp.dot(x_hi, m_hi, preferred_element_type=jnp.float32)
            acc = acc + jnp.dot(x_hi, m_lo, preferred_element_type=jnp.float32)
            acc = acc + jnp.dot(x_lo, m_hi, preferred_element_type=jnp.float32)
        out_ref[row] = acc


def interpolate(x_hi, x_lo, info, lat_rows, lon_cols, base=None):
    n_rows, n_items, width = x_hi.shape
    blocks = lon_cols // LANES
    whole = pl.BlockSpec((n_rows, n_items, width), lambda jb: (0, 0, 0))
    tile = pl.BlockSpec((lat_rows, n_items, LANES), lambda jb: (0, 0, jb))
    specs = [whole, whole, pl.BlockSpec((lat_rows, info.shape[1], LANES), lambda jb: (0, 0, jb))]
    operands = [x_hi, x_lo, info]
    if base is not None:
        specs.append(tile)
        operands.append(base)
    return pl.pallas_call(
        functools.partial(interp_kernel, base is None, lat_rows),
        out_shape=jax.ShapeDtypeStruct((lat_rows, n_items, lon_cols), jnp.float32),
        grid=(blocks,),
        in_specs=specs,
        out_specs=tile,
        compiler_params=pltpu.CompilerParams(vmem_limit_bytes=48 * 1024 * 1024),
    )(*operands)


def vertical_mix(raw, bands):
    n_levels = raw.shape[-2]
    pad = [(0, 0)] * raw.ndim
    pad[-2] = (2, 2)
    stacked = jnp.pad(raw, pad)
    lead = (None,) * (raw.ndim - 3)
    mixed = bands[lead + (slice(None), 0, slice(None), None)] * stacked[..., 0:n_levels, :]
    for shift_k in range(1, 5):
        mixed = mixed + bands[lead + (slice(None), shift_k, slice(None), None)] * stacked[
            ..., shift_k : shift_k + n_levels, :
        ]
    return mixed


def widen(block):
    left, right = shifted(block, "lon", HALO, block.ndim - 1, True)
    return jnp.concatenate([left, block, right], axis=block.ndim - 1)


def split_rows(rows, width):
    pad = [(0, 0)] * (rows.ndim - 1) + [(0, width - rows.shape[-1])]
    padded = jnp.pad(rows, pad)
    rounded = lax.reduce_precision(padded, exponent_bits=8, mantissa_bits=7)
    return rounded.astype(jnp.bfloat16), (padded - rounded).astype(jnp.bfloat16)


def on_device(fields, weights, stencil, bands):
    n_fields, n_levels, lat_rows, lon_cols = fields.shape
    n_items = n_fields * n_levels
    width = lon_cols + LANES
    local_rows = vertical_mix(jnp.transpose(fields, (2, 0, 1, 3)), bands)
    wide = widen(local_rows.reshape(lat_rows, n_items, lon_cols))
    below_wide, above_wide = shifted(wide, "lat", ROWS_OUT, 0, False)
    local_hi, local_lo = split_rows(wide, width)

    lat_start = lax.axis_index("lat") * lat_rows
    lon_start = lax.axis_index("lon") * lon_cols
    line_len = lon_cols * lax.axis_size("lon")
    row_g = lat_start + jnp.arange(lat_rows, dtype=jnp.int32)[:, None]
    col_g = lon_start + jnp.arange(lon_cols, dtype=jnp.int32)[None, :]
    offset_r = (stencil[0] - row_g + ROWS_OUT).astype(jnp.float32)
    offset_d = jnp.mod(stencil[1] - col_g + HALO, line_len).astype(jnp.float32)
    info = jnp.concatenate(
        [
            jnp.transpose(weights, (1, 0, 2)),
            offset_r[:, None, :],
            offset_d[:, None, :],
            jnp.zeros((lat_rows, 6, lon_cols), jnp.float32),
        ],
        axis=1,
    )
    partial = interpolate(local_hi, local_lo, info, lat_rows, lon_cols)

    below_wide, above_wide, partial = lax.optimization_barrier((below_wide, above_wide, partial))
    halo_hi, halo_lo = split_rows(jnp.concatenate([below_wide, above_wide], axis=0), width)
    departed = interpolate(halo_hi, halo_lo, info, lat_rows, lon_cols, base=partial)

    gathered = lax.all_to_all(departed, "lon", split_axis=1, concat_axis=2, tiled=True)
    real_part, imag_part = spectrum(gathered)
    return (jnp.transpose(real_part, (1, 0, 2)), jnp.transpose(imag_part, (1, 0, 2)))


def solution(mesh):
    placed = (P(None, None, "lat", "lon"), P(None, "lat", "lon"), P(None, "lat", "lon"), P())
    return jax.shard_map(
        on_device,
        mesh=mesh,
        in_specs=placed,
        out_specs=(P("lon", "lat", None), P("lon", "lat", None)),
        check_vma=False,
    )
```

```python
import functools
import math

import jax
import jax.numpy as jnp
from jax import lax
from jax.experimental import pallas as pl
from jax.experimental.pallas import tpu as pltpu
from jax.sharding import PartitionSpec as P

RADIX = 64
NK = 1280
HALO = 16
ROWS_OUT = 3
TAPS = 4
LANES = 128
WINDOW = 256


def shifted(block, axis, width, dim, periodic):
    count = lax.axis_size(axis)
    forward = [(i, i + 1) for i in range(count - 1)]
    if periodic:
        forward.append((count - 1, 0))
    backward = [(target, source) for source, target in forward]
    low = lax.ppermute(
        lax.slice_in_dim(block, block.shape[dim] - width, None, axis=dim), axis, forward
    )
    high = lax.ppermute(lax.slice_in_dim(block, 0, width, axis=dim), axis, backward)
    return low, high


def spectrum(pieces, owners):
    n_rows, n_items, piece_len = pieces[0].shape
    line_len = piece_len * len(pieces)
    highest = lax.Precision.HIGH
    digits = jnp.arange(RADIX, dtype=jnp.int32)
    angle_one = (
        2.0 * math.pi / RADIX * (digits[:, None] * digits[None, :] % RADIX).astype(jnp.float32)
    )
    first_table = jnp.concatenate([jnp.cos(angle_one), -jnp.sin(angle_one)], axis=1)
    per_piece = piece_len // RADIX
    partial_value = None
    for piece, owner in zip(pieces, owners):
        folded = piece.reshape(n_rows * n_items, per_piece, RADIX)
        table = lax.dynamic_slice_in_dim(first_table, owner * per_piece, per_piece, axis=0)
        term = jnp.einsum("rab,ac->rbc", folded, table, precision=highest)
        partial_value = term if partial_value is None else partial_value + term
    angle_two = (
        2.0
        * math.pi
        / line_len
        * (digits[:, None] * digits[None, :] % line_len).astype(jnp.float32)
    )
    cos_two = jnp.cos(angle_two)
    sin_two = jnp.sin(angle_two)
    part_re = partial_value[..., :RADIX]
    part_im = partial_value[..., RADIX:]
    twisted = jnp.concatenate(
        [part_re * cos_two + part_im * sin_two, part_im * cos_two - part_re * sin_two], axis=-1
    )
    quotients = jnp.arange(NK // RADIX, dtype=jnp.int32)
    angle_three = (
        2.0 * math.pi / RADIX * (digits[:, None] * quotients[None, :] % RADIX).astype(jnp.float32)
    )
    with_cos = jnp.einsum("rbc,bq->rqc", twisted, jnp.cos(angle_three), precision=highest)
    with_sin = jnp.einsum("rbc,bq->rqc", twisted, jnp.sin(angle_three), precision=highest)
    scale = 1.0 / math.sqrt(line_len)
    real_part = (with_cos[..., :RADIX] + with_sin[..., RADIX:]) * scale
    imag_part = (with_cos[..., RADIX:] - with_sin[..., :RADIX]) * scale
    return (real_part.reshape(n_rows, n_items, NK), imag_part.reshape(n_rows, n_items, NK))


def interp_kernel(local, lat_rows, *refs):
    if local:
        hi_ref, lo_ref, info_ref, out_ref = refs
    else:
        hi_ref, lo_ref, info_ref, base_ref, out_ref = refs
    block = pl.program_id(0)
    start = pl.multiple_of(block * LANES, LANES)
    c_index = lax.broadcasted_iota(jnp.int32, (WINDOW, LANES), 0).astype(jnp.float32)
    j_index = lax.broadcasted_iota(jnp.int32, (WINDOW, LANES), 1).astype(jnp.float32)
    for row in range(lat_rows):
        info = info_ref[row]
        offset_r = info[16:17, :]
        offset_d = info[17:18, :]
        tap = c_index - j_index - offset_d
        masks = [tap == float(b) for b in range(TAPS)]
        if local:
            acc = jnp.zeros(out_ref.shape[1:], jnp.float32)
        else:
            acc = base_ref[row]
        for p in range(2 * ROWS_OUT + 1):
            h = row + p
            inside = ROWS_OUT <= h < ROWS_OUT + lat_rows
            if inside != local:
                continue
            if local:
                index = h - ROWS_OUT
            else:
                index = h if h < ROWS_OUT else h - lat_rows
            picked = []
            for b in range(TAPS):
                value = jnp.zeros_like(offset_r)
                for a in range(TAPS):
                    if 0 <= p - a <= ROWS_OUT:
                        value = jnp.where(offset_r == float(p - a), info[4 * a + b : 4 * a + b + 1, :], value)
                picked.append(value)
            matrix = jnp.where(
                masks[0],
                picked[0],
                jnp.where(masks[1], picked[1], jnp.where(masks[2], picked[2], jnp.where(masks[3], picked[3], 0.0))),
            )
            m_hi = matrix.astype(jnp.bfloat16)
            m_lo = (matrix - m_hi.astype(jnp.float32)).astype(jnp.bfloat16)
            x_hi = hi_ref[index, :, pl.ds(start, WINDOW)]
            x_lo = lo_ref[index, :, pl.ds(start, WINDOW)]
            acc = acc + jnp.dot(x_hi, m_hi, preferred_element_type=jnp.float32)
            acc = acc + jnp.dot(x_hi, m_lo, preferred_element_type=jnp.float32)
            acc = acc + jnp.dot(x_lo, m_hi, preferred_element_type=jnp.float32)
        out_ref[row] = acc


def interpolate(x_hi, x_lo, info, lat_rows, lon_cols, base=None):
    n_rows, n_items, width = x_hi.shape
    blocks = lon_cols // LANES
    whole = pl.BlockSpec((n_rows, n_items, width), lambda jb: (0, 0, 0))
    tile = pl.BlockSpec((lat_rows, n_items, LANES), lambda jb: (0, 0, jb))
    specs = [whole, whole, pl.BlockSpec((lat_rows, info.shape[1], LANES), lambda jb: (0, 0, jb))]
    operands = [x_hi, x_lo, info]
    if base is not None:
        specs.append(tile)
        operands.append(base)
    return pl.pallas_call(
        functools.partial(interp_kernel, base is None, lat_rows),
        out_shape=jax.ShapeDtypeStruct((lat_rows, n_items, lon_cols), jnp.float32),
        grid=(blocks,),
        in_specs=specs,
        out_specs=tile,
        compiler_params=pltpu.CompilerParams(vmem_limit_bytes=48 * 1024 * 1024),
    )(*operands)


def vertical_mix(raw, bands):
    n_levels = raw.shape[-2]
    pad = [(0, 0)] * raw.ndim
    pad[-2] = (2, 2)
    stacked = jnp.pad(raw, pad)
    lead = (None,) * (raw.ndim - 3)
    mixed = bands[lead + (slice(None), 0, slice(None), None)] * stacked[..., 0:n_levels, :]
    for shift_k in range(1, 5):
        mixed = mixed + bands[lead + (slice(None), shift_k, slice(None), None)] * stacked[
            ..., shift_k : shift_k + n_levels, :
        ]
    return mixed


def widen(block):
    left, right = shifted(block, "lon", HALO, block.ndim - 1, True)
    return jnp.concatenate([left, block, right], axis=block.ndim - 1)


def split_rows(rows, width):
    pad = [(0, 0)] * (rows.ndim - 1) + [(0, width - rows.shape[-1])]
    padded = jnp.pad(rows, pad)
    rounded = lax.reduce_precision(padded, exponent_bits=8, mantissa_bits=7)
    return rounded.astype(jnp.bfloat16), (padded - rounded).astype(jnp.bfloat16)


def on_device(fields, weights, stencil, bands):
    n_fields, n_levels, lat_rows, lon_cols = fields.shape
    n_items = n_fields * n_levels
    below_raw, above_raw = shifted(fields, "lat", ROWS_OUT, 2, False)

    width = lon_cols + LANES
    local_rows = vertical_mix(jnp.transpose(fields, (2, 0, 1, 3)), bands)
    local_hi, local_lo = split_rows(widen(local_rows.reshape(lat_rows, n_items, lon_cols)), width)

    lat_start = lax.axis_index("lat") * lat_rows
    lon_start = lax.axis_index("lon") * lon_cols
    line_len = lon_cols * lax.axis_size("lon")
    row_g = lat_start + jnp.arange(lat_rows, dtype=jnp.int32)[:, None]
    col_g = lon_start + jnp.arange(lon_cols, dtype=jnp.int32)[None, :]
    offset_r = (stencil[0] - row_g + ROWS_OUT).astype(jnp.float32)
    offset_d = jnp.mod(stencil[1] - col_g + HALO, line_len).astype(jnp.float32)
    info = jnp.concatenate(
        [
            jnp.transpose(weights, (1, 0, 2)),
            offset_r[:, None, :],
            offset_d[:, None, :],
            jnp.zeros((lat_rows, 6, lon_cols), jnp.float32),
        ],
        axis=1,
    )
    partial = interpolate(local_hi, local_lo, info, lat_rows, lon_cols)

    below_raw, above_raw, partial = lax.optimization_barrier((below_raw, above_raw, partial))
    halo_raw = jnp.concatenate([below_raw, above_raw], axis=2)
    halo_rows = vertical_mix(jnp.transpose(halo_raw, (2, 0, 1, 3)), bands)
    halo_hi, halo_lo = split_rows(widen(halo_rows.reshape(2 * ROWS_OUT, n_items, lon_cols)), width)
    departed = interpolate(halo_hi, halo_lo, info, lat_rows, lon_cols, base=partial)

    parts = lax.axis_size("lon")
    me = lax.axis_index("lon")
    chunk = n_items // parts
    pieces = []
    owners = []
    for shift in range(parts):
        target = lax.rem(me + shift, parts)
        piece = lax.dynamic_slice_in_dim(departed, target * chunk, chunk, axis=1)
        if shift:
            piece = lax.ppermute(piece, "lon", [(i, (i + shift) % parts) for i in range(parts)])
        pieces.append(piece)
        owners.append(lax.rem(me - shift + parts, parts))
    real_part, imag_part = spectrum(pieces, owners)
    return (jnp.transpose(real_part, (1, 0, 2)), jnp.transpose(imag_part, (1, 0, 2)))


def solution(mesh):
    placed = (P(None, None, "lat", "lon"), P(None, "lat", "lon"), P(None, "lat", "lon"), P())
    return jax.shard_map(
        on_device,
        mesh=mesh,
        in_specs=placed,
        out_specs=(P("lon", "lat", None), P("lon", "lat", None)),
        check_vma=False,
    )
```

```python
import functools
import math

import jax
import jax.numpy as jnp
from jax import lax
from jax.experimental import pallas as pl
from jax.experimental.pallas import tpu as pltpu
from jax.sharding import PartitionSpec as P

RADIX = 64
NK = 1280
HALO = 16
ROWS_OUT = 3
TAPS = 4
LANES = 128
WINDOW = 256


def shifted(block, axis, width, dim, periodic):
    count = lax.axis_size(axis)
    forward = [(i, i + 1) for i in range(count - 1)]
    if periodic:
        forward.append((count - 1, 0))
    backward = [(target, source) for source, target in forward]
    low = lax.ppermute(
        lax.slice_in_dim(block, block.shape[dim] - width, None, axis=dim), axis, forward
    )
    high = lax.ppermute(lax.slice_in_dim(block, 0, width, axis=dim), axis, backward)
    return low, high


def spectrum(pieces, owners):
    n_rows, n_items, piece_len = pieces[0].shape
    line_len = piece_len * len(pieces)
    highest = lax.Precision.HIGH
    digits = jnp.arange(RADIX, dtype=jnp.int32)
    angle_one = (
        2.0 * math.pi / RADIX * (digits[:, None] * digits[None, :] % RADIX).astype(jnp.float32)
    )
    first_table = jnp.concatenate([jnp.cos(angle_one), -jnp.sin(angle_one)], axis=1)
    per_piece = piece_len // RADIX
    folded = jnp.concatenate(
        [piece.reshape(n_rows * n_items, per_piece, RADIX) for piece in pieces], axis=1
    )
    table = jnp.concatenate(
        [lax.dynamic_slice_in_dim(first_table, owner * per_piece, per_piece, axis=0) for owner in owners],
        axis=0,
    )
    partial_value = jnp.einsum("rab,ac->rbc", folded, table, precision=highest)
    angle_two = (
        2.0
        * math.pi
        / line_len
        * (digits[:, None] * digits[None, :] % line_len).astype(jnp.float32)
    )
    cos_two = jnp.cos(angle_two)
    sin_two = jnp.sin(angle_two)
    part_re = partial_value[..., :RADIX]
    part_im = partial_value[..., RADIX:]
    twisted = jnp.concatenate(
        [part_re * cos_two + part_im * sin_two, part_im * cos_two - part_re * sin_two], axis=-1
    )
    quotients = jnp.arange(NK // RADIX, dtype=jnp.int32)
    angle_three = (
        2.0 * math.pi / RADIX * (digits[:, None] * quotients[None, :] % RADIX).astype(jnp.float32)
    )
    with_cos = jnp.einsum("rbc,bq->rqc", twisted, jnp.cos(angle_three), precision=highest)
    with_sin = jnp.einsum("rbc,bq->rqc", twisted, jnp.sin(angle_three), precision=highest)
    scale = 1.0 / math.sqrt(line_len)
    real_part = (with_cos[..., :RADIX] + with_sin[..., RADIX:]) * scale
    imag_part = (with_cos[..., RADIX:] - with_sin[..., :RADIX]) * scale
    return (real_part.reshape(n_rows, n_items, NK), imag_part.reshape(n_rows, n_items, NK))


def interp_kernel(local, lat_rows, *refs):
    if local:
        hi_ref, lo_ref, info_ref, out_ref = refs
    else:
        hi_ref, lo_ref, info_ref, base_ref, out_ref = refs
    block = pl.program_id(0)
    start = pl.multiple_of(block * LANES, LANES)
    c_index = lax.broadcasted_iota(jnp.int32, (WINDOW, LANES), 0).astype(jnp.float32)
    j_index = lax.broadcasted_iota(jnp.int32, (WINDOW, LANES), 1).astype(jnp.float32)
    for row in range(lat_rows):
        info = info_ref[row]
        offset_r = info[16:17, :]
        offset_d = info[17:18, :]
        tap = c_index - j_index - offset_d
        masks = [tap == float(b) for b in range(TAPS)]
        if local:
            acc = jnp.zeros(out_ref.shape[1:], jnp.float32)
        else:
            acc = base_ref[row]
        for p in range(2 * ROWS_OUT + 1):
            h = row + p
            inside = ROWS_OUT <= h < ROWS_OUT + lat_rows
            if inside != local:
                continue
            if local:
                index = h - ROWS_OUT
            else:
                index = h if h < ROWS_OUT else h - lat_rows
            picked = []
            for b in range(TAPS):
                value = jnp.zeros_like(offset_r)
                for a in range(TAPS):
                    if 0 <= p - a <= ROWS_OUT:
                        value = jnp.where(offset_r == float(p - a), info[4 * a + b : 4 * a + b + 1, :], value)
                picked.append(value)
            matrix = jnp.where(
                masks[0],
                picked[0],
                jnp.where(masks[1], picked[1], jnp.where(masks[2], picked[2], jnp.where(masks[3], picked[3], 0.0))),
            )
            m_hi = matrix.astype(jnp.bfloat16)
            m_lo = (matrix - m_hi.astype(jnp.float32)).astype(jnp.bfloat16)
            x_hi = hi_ref[index, :, pl.ds(start, WINDOW)]
            x_lo = lo_ref[index, :, pl.ds(start, WINDOW)]
            acc = acc + jnp.dot(x_hi, m_hi, preferred_element_type=jnp.float32)
            acc = acc + jnp.dot(x_hi, m_lo, preferred_element_type=jnp.float32)
            acc = acc + jnp.dot(x_lo, m_hi, preferred_element_type=jnp.float32)
        out_ref[row] = acc


def interpolate(x_hi, x_lo, info, lat_rows, lon_cols, base=None):
    n_rows, n_items, width = x_hi.shape
    blocks = lon_cols // LANES
    whole = pl.BlockSpec((n_rows, n_items, width), lambda jb: (0, 0, 0))
    tile = pl.BlockSpec((lat_rows, n_items, LANES), lambda jb: (0, 0, jb))
    specs = [whole, whole, pl.BlockSpec((lat_rows, info.shape[1], LANES), lambda jb: (0, 0, jb))]
    operands = [x_hi, x_lo, info]
    if base is not None:
        specs.append(tile)
        operands.append(base)
    return pl.pallas_call(
        functools.partial(interp_kernel, base is None, lat_rows),
        out_shape=jax.ShapeDtypeStruct((lat_rows, n_items, lon_cols), jnp.float32),
        grid=(blocks,),
        in_specs=specs,
        out_specs=tile,
        compiler_params=pltpu.CompilerParams(vmem_limit_bytes=48 * 1024 * 1024),
    )(*operands)


def vertical_mix(raw, bands):
    n_levels = raw.shape[-2]
    pad = [(0, 0)] * raw.ndim
    pad[-2] = (2, 2)
    stacked = jnp.pad(raw, pad)
    lead = (None,) * (raw.ndim - 3)
    mixed = bands[lead + (slice(None), 0, slice(None), None)] * stacked[..., 0:n_levels, :]
    for shift_k in range(1, 5):
        mixed = mixed + bands[lead + (slice(None), shift_k, slice(None), None)] * stacked[
            ..., shift_k : shift_k + n_levels, :
        ]
    return mixed


def widen(block):
    left, right = shifted(block, "lon", HALO, block.ndim - 1, True)
    return jnp.concatenate([left, block, right], axis=block.ndim - 1)


def split_rows(rows, width):
    pad = [(0, 0)] * (rows.ndim - 1) + [(0, width - rows.shape[-1])]
    padded = jnp.pad(rows, pad)
    rounded = lax.reduce_precision(padded, exponent_bits=8, mantissa_bits=7)
    return rounded.astype(jnp.bfloat16), (padded - rounded).astype(jnp.bfloat16)


def on_device(fields, weights, stencil, bands):
    n_fields, n_levels, lat_rows, lon_cols = fields.shape
    n_items = n_fields * n_levels
    below_raw, above_raw = shifted(fields, "lat", ROWS_OUT, 2, False)

    width = lon_cols + LANES
    local_rows = vertical_mix(jnp.transpose(fields, (2, 0, 1, 3)), bands)
    local_hi, local_lo = split_rows(widen(local_rows.reshape(lat_rows, n_items, lon_cols)), width)

    lat_start = lax.axis_index("lat") * lat_rows
    lon_start = lax.axis_index("lon") * lon_cols
    line_len = lon_cols * lax.axis_size("lon")
    row_g = lat_start + jnp.arange(lat_rows, dtype=jnp.int32)[:, None]
    col_g = lon_start + jnp.arange(lon_cols, dtype=jnp.int32)[None, :]
    offset_r = (stencil[0] - row_g + ROWS_OUT).astype(jnp.float32)
    offset_d = jnp.mod(stencil[1] - col_g + HALO, line_len).astype(jnp.float32)
    info = jnp.concatenate(
        [
            jnp.transpose(weights, (1, 0, 2)),
            offset_r[:, None, :],
            offset_d[:, None, :],
            jnp.zeros((lat_rows, 6, lon_cols), jnp.float32),
        ],
        axis=1,
    )
    partial = interpolate(local_hi, local_lo, info, lat_rows, lon_cols)

    below_raw, above_raw, partial = lax.optimization_barrier((below_raw, above_raw, partial))
    halo_raw = jnp.concatenate([below_raw, above_raw], axis=2)
    halo_rows = vertical_mix(jnp.transpose(halo_raw, (2, 0, 1, 3)), bands)
    halo_hi, halo_lo = split_rows(widen(halo_rows.reshape(2 * ROWS_OUT, n_items, lon_cols)), width)
    departed = interpolate(halo_hi, halo_lo, info, lat_rows, lon_cols, base=partial)

    parts = lax.axis_size("lon")
    me = lax.axis_index("lon")
    chunk = n_items // parts
    pieces = []
    owners = []
    for shift in range(parts):
        target = lax.rem(me + shift, parts)
        piece = lax.dynamic_slice_in_dim(departed, target * chunk, chunk, axis=1)
        if shift:
            piece = lax.ppermute(piece, "lon", [(i, (i + shift) % parts) for i in range(parts)])
        pieces.append(piece)
        owners.append(lax.rem(me - shift + parts, parts))
    real_part, imag_part = spectrum(pieces, owners)
    return (jnp.transpose(real_part, (1, 0, 2)), jnp.transpose(imag_part, (1, 0, 2)))


def solution(mesh):
    placed = (P(None, None, "lat", "lon"), P(None, "lat", "lon"), P(None, "lat", "lon"), P())
    return jax.shard_map(
        on_device,
        mesh=mesh,
        in_specs=placed,
        out_specs=(P("lon", "lat", None), P("lon", "lat", None)),
        check_vma=False,
    )
```

```python
import functools
import math

import jax
import jax.numpy as jnp
from jax import lax
from jax.experimental import pallas as pl
from jax.experimental.pallas import tpu as pltpu
from jax.sharding import PartitionSpec as P

RADIX = 64
NK = 1280
HALO = 16
ROWS_OUT = 3
TAPS = 4
LANES = 128
WINDOW = 256


def shifted(block, axis, width, dim, periodic):
    count = lax.axis_size(axis)
    forward = [(i, i + 1) for i in range(count - 1)]
    if periodic:
        forward.append((count - 1, 0))
    backward = [(target, source) for source, target in forward]
    low = lax.ppermute(
        lax.slice_in_dim(block, block.shape[dim] - width, None, axis=dim), axis, forward
    )
    high = lax.ppermute(lax.slice_in_dim(block, 0, width, axis=dim), axis, backward)
    return low, high


def spectrum(pieces, owners):
    n_rows, n_items, piece_len = pieces[0].shape
    line_len = piece_len * len(pieces)
    highest = lax.Precision.HIGH
    digits = jnp.arange(RADIX, dtype=jnp.int32)
    angle_one = (
        2.0 * math.pi / RADIX * (digits[:, None] * digits[None, :] % RADIX).astype(jnp.float32)
    )
    first_table = jnp.concatenate([jnp.cos(angle_one), -jnp.sin(angle_one)], axis=1)
    per_piece = piece_len // RADIX
    folded = jnp.concatenate(
        [piece.reshape(n_rows * n_items, per_piece, RADIX) for piece in pieces], axis=1
    )
    table = jnp.concatenate(
        [lax.dynamic_slice_in_dim(first_table, owner * per_piece, per_piece, axis=0) for owner in owners],
        axis=0,
    )
    partial_value = jnp.einsum("rab,ac->rbc", folded, table, precision=highest)
    angle_two = (
        2.0
        * math.pi
        / line_len
        * (digits[:, None] * digits[None, :] % line_len).astype(jnp.float32)
    )
    cos_two = jnp.cos(angle_two)
    sin_two = jnp.sin(angle_two)
    part_re = partial_value[..., :RADIX]
    part_im = partial_value[..., RADIX:]
    twisted = jnp.concatenate(
        [part_re * cos_two + part_im * sin_two, part_im * cos_two - part_re * sin_two], axis=-1
    )
    quotients = jnp.arange(NK // RADIX, dtype=jnp.int32)
    angle_three = (
        2.0 * math.pi / RADIX * (digits[:, None] * quotients[None, :] % RADIX).astype(jnp.float32)
    )
    with_cos = jnp.einsum("rbc,bq->rqc", twisted, jnp.cos(angle_three), precision=highest)
    with_sin = jnp.einsum("rbc,bq->rqc", twisted, jnp.sin(angle_three), precision=highest)
    scale = 1.0 / math.sqrt(line_len)
    real_part = (with_cos[..., :RADIX] + with_sin[..., RADIX:]) * scale
    imag_part = (with_cos[..., RADIX:] - with_sin[..., :RADIX]) * scale
    return (real_part.reshape(n_rows, n_items, NK), imag_part.reshape(n_rows, n_items, NK))


def interp_kernel(local, lat_rows, *refs):
    if local:
        hi_ref, lo_ref, info_ref, out_ref = refs
    else:
        hi_ref, lo_ref, info_ref, base_ref, out_ref = refs
    block = pl.program_id(0)
    start = pl.multiple_of(block * LANES, LANES)
    c_index = lax.broadcasted_iota(jnp.int32, (WINDOW, LANES), 0).astype(jnp.float32)
    j_index = lax.broadcasted_iota(jnp.int32, (WINDOW, LANES), 1).astype(jnp.float32)
    for row in range(lat_rows):
        info = info_ref[row]
        offset_r = info[16:17, :]
        offset_d = info[17:18, :]
        tap = c_index - j_index - offset_d
        masks = [tap == float(b) for b in range(TAPS)]
        if local:
            acc = jnp.zeros(out_ref.shape[1:], jnp.float32)
        else:
            acc = base_ref[row]
        for p in range(2 * ROWS_OUT + 1):
            h = row + p
            inside = ROWS_OUT <= h < ROWS_OUT + lat_rows
            if inside != local:
                continue
            if local:
                index = h - ROWS_OUT
            else:
                index = h if h < ROWS_OUT else h - lat_rows
            picked = []
            for b in range(TAPS):
                value = jnp.zeros_like(offset_r)
                for a in range(TAPS):
                    if 0 <= p - a <= ROWS_OUT:
                        value = jnp.where(offset_r == float(p - a), info[4 * a + b : 4 * a + b + 1, :], value)
                picked.append(value)
            matrix = jnp.where(
                masks[0],
                picked[0],
                jnp.where(masks[1], picked[1], jnp.where(masks[2], picked[2], jnp.where(masks[3], picked[3], 0.0))),
            )
            m_hi = matrix.astype(jnp.bfloat16)
            m_lo = (matrix - m_hi.astype(jnp.float32)).astype(jnp.bfloat16)
            x_hi = hi_ref[index, :, pl.ds(start, WINDOW)]
            x_lo = lo_ref[index, :, pl.ds(start, WINDOW)]
            acc = acc + jnp.dot(x_hi, m_hi, preferred_element_type=jnp.float32)
            acc = acc + jnp.dot(x_hi, m_lo, preferred_element_type=jnp.float32)
            acc = acc + jnp.dot(x_lo, m_hi, preferred_element_type=jnp.float32)
        out_ref[row] = acc


def interpolate(x_hi, x_lo, info, lat_rows, lon_cols, base=None):
    n_rows, n_items, width = x_hi.shape
    blocks = lon_cols // LANES
    whole = pl.BlockSpec((n_rows, n_items, width), lambda jb: (0, 0, 0))
    tile = pl.BlockSpec((lat_rows, n_items, LANES), lambda jb: (0, 0, jb))
    specs = [whole, whole, pl.BlockSpec((lat_rows, info.shape[1], LANES), lambda jb: (0, 0, jb))]
    operands = [x_hi, x_lo, info]
    if base is not None:
        specs.append(tile)
        operands.append(base)
    return pl.pallas_call(
        functools.partial(interp_kernel, base is None, lat_rows),
        out_shape=jax.ShapeDtypeStruct((lat_rows, n_items, lon_cols), jnp.float32),
        grid=(blocks,),
        in_specs=specs,
        out_specs=tile,
        compiler_params=pltpu.CompilerParams(vmem_limit_bytes=48 * 1024 * 1024),
    )(*operands)


def vertical_mix(raw, bands):
    n_levels = raw.shape[-2]
    pad = [(0, 0)] * raw.ndim
    pad[-2] = (2, 2)
    stacked = jnp.pad(raw, pad)
    lead = (None,) * (raw.ndim - 3)
    mixed = bands[lead + (slice(None), 0, slice(None), None)] * stacked[..., 0:n_levels, :]
    for shift_k in range(1, 5):
        mixed = mixed + bands[lead + (slice(None), shift_k, slice(None), None)] * stacked[
            ..., shift_k : shift_k + n_levels, :
        ]
    return mixed


def widen(block):
    left, right = shifted(block, "lon", HALO, block.ndim - 1, True)
    return jnp.concatenate([left, block, right], axis=block.ndim - 1)


def split_rows(rows, width):
    pad = [(0, 0)] * (rows.ndim - 1) + [(0, width - rows.shape[-1])]
    padded = jnp.pad(rows, pad)
    rounded = lax.reduce_precision(padded, exponent_bits=8, mantissa_bits=7)
    return rounded.astype(jnp.bfloat16), (padded - rounded).astype(jnp.bfloat16)


def on_device(fields, weights, stencil, bands):
    n_fields, n_levels, lat_rows, lon_cols = fields.shape
    n_items = n_fields * n_levels
    below_raw, above_raw = shifted(fields, "lat", ROWS_OUT, 2, False)
    n_lat = lax.axis_size("lat")
    n_lon = lax.axis_size("lon")

    def diagonal(block, lat_step, lon_step):
        pairs = []
        for b in range(n_lat):
            if 0 <= b + lat_step < n_lat:
                for k in range(n_lon):
                    pairs.append((b * n_lon + k, (b + lat_step) * n_lon + (k + lon_step) % n_lon))
        return lax.ppermute(block, ("lat", "lon"), pairs)

    low_rows = fields[:, :, lat_rows - ROWS_OUT :, :]
    high_rows = fields[:, :, :ROWS_OUT, :]
    below_left = diagonal(low_rows[..., lon_cols - HALO :], 1, 1)
    below_right = diagonal(low_rows[..., :HALO], 1, -1)
    above_left = diagonal(high_rows[..., lon_cols - HALO :], -1, 1)
    above_right = diagonal(high_rows[..., :HALO], -1, -1)

    width = lon_cols + LANES
    local_rows = vertical_mix(jnp.transpose(fields, (2, 0, 1, 3)), bands)
    local_hi, local_lo = split_rows(widen(local_rows.reshape(lat_rows, n_items, lon_cols)), width)

    lat_start = lax.axis_index("lat") * lat_rows
    lon_start = lax.axis_index("lon") * lon_cols
    line_len = lon_cols * lax.axis_size("lon")
    row_g = lat_start + jnp.arange(lat_rows, dtype=jnp.int32)[:, None]
    col_g = lon_start + jnp.arange(lon_cols, dtype=jnp.int32)[None, :]
    offset_r = (stencil[0] - row_g + ROWS_OUT).astype(jnp.float32)
    offset_d = jnp.mod(stencil[1] - col_g + HALO, line_len).astype(jnp.float32)
    info = jnp.concatenate(
        [
            jnp.transpose(weights, (1, 0, 2)),
            offset_r[:, None, :],
            offset_d[:, None, :],
            jnp.zeros((lat_rows, 6, lon_cols), jnp.float32),
        ],
        axis=1,
    )
    partial = interpolate(local_hi, local_lo, info, lat_rows, lon_cols)

    below_raw, above_raw, partial = lax.optimization_barrier((below_raw, above_raw, partial))
    below_left, below_right, above_left, above_right = lax.optimization_barrier(
        (below_left, below_right, above_left, above_right)
    )
    halo_raw = jnp.concatenate(
        [
            jnp.concatenate([below_left, below_raw, below_right], axis=3),
            jnp.concatenate([above_left, above_raw, above_right], axis=3),
        ],
        axis=2,
    )
    halo_rows = vertical_mix(jnp.transpose(halo_raw, (2, 0, 1, 3)), bands)
    halo_hi, halo_lo = split_rows(halo_rows.reshape(2 * ROWS_OUT, n_items, lon_cols + 2 * HALO), width)
    departed = interpolate(halo_hi, halo_lo, info, lat_rows, lon_cols, base=partial)

    parts = lax.axis_size("lon")
    me = lax.axis_index("lon")
    chunk = n_items // parts
    pieces = []
    owners = []
    for shift in range(parts):
        target = lax.rem(me + shift, parts)
        piece = lax.dynamic_slice_in_dim(departed, target * chunk, chunk, axis=1)
        if shift:
            piece = lax.ppermute(piece, "lon", [(i, (i + shift) % parts) for i in range(parts)])
        pieces.append(piece)
        owners.append(lax.rem(me - shift + parts, parts))
    real_part, imag_part = spectrum(pieces, owners)
    return (jnp.transpose(real_part, (1, 0, 2)), jnp.transpose(imag_part, (1, 0, 2)))


def solution(mesh):
    placed = (P(None, None, "lat", "lon"), P(None, "lat", "lon"), P(None, "lat", "lon"), P())
    return jax.shard_map(
        on_device,
        mesh=mesh,
        in_specs=placed,
        out_specs=(P("lon", "lat", None), P("lon", "lat", None)),
        check_vma=False,
    )
```

```python
import functools
import math

import jax
import jax.numpy as jnp
from jax import lax
from jax.experimental import pallas as pl
from jax.experimental.pallas import tpu as pltpu
from jax.sharding import PartitionSpec as P

RADIX = 64
NK = 1280
HALO = 16
ROWS_OUT = 3
TAPS = 4
LANES = 128
WINDOW = 256


def shifted(block, axis, width, dim, periodic):
    count = lax.axis_size(axis)
    forward = [(i, i + 1) for i in range(count - 1)]
    if periodic:
        forward.append((count - 1, 0))
    backward = [(target, source) for source, target in forward]
    low = lax.ppermute(
        lax.slice_in_dim(block, block.shape[dim] - width, None, axis=dim), axis, forward
    )
    high = lax.ppermute(lax.slice_in_dim(block, 0, width, axis=dim), axis, backward)
    return low, high


def spectrum(pieces, owners):
    n_rows, n_items, piece_len = pieces[0].shape
    line_len = piece_len * len(pieces)
    highest = lax.Precision.HIGH
    digits = jnp.arange(RADIX, dtype=jnp.int32)
    angle_one = (
        2.0 * math.pi / RADIX * (digits[:, None] * digits[None, :] % RADIX).astype(jnp.float32)
    )
    first_table = jnp.concatenate([jnp.cos(angle_one), -jnp.sin(angle_one)], axis=1)
    per_piece = piece_len // RADIX
    folded = jnp.concatenate(
        [piece.reshape(n_rows * n_items, per_piece, RADIX) for piece in pieces], axis=1
    )
    table = jnp.concatenate(
        [lax.dynamic_slice_in_dim(first_table, owner * per_piece, per_piece, axis=0) for owner in owners],
        axis=0,
    )
    partial_value = jnp.einsum("rab,ac->rbc", folded, table, precision=highest)
    angle_two = (
        2.0
        * math.pi
        / line_len
        * (digits[:, None] * digits[None, :] % line_len).astype(jnp.float32)
    )
    cos_two = jnp.cos(angle_two)
    sin_two = jnp.sin(angle_two)
    part_re = partial_value[..., :RADIX]
    part_im = partial_value[..., RADIX:]
    twisted = jnp.concatenate(
        [part_re * cos_two + part_im * sin_two, part_im * cos_two - part_re * sin_two], axis=-1
    )
    quotients = jnp.arange(NK // RADIX, dtype=jnp.int32)
    angle_three = (
        2.0 * math.pi / RADIX * (digits[:, None] * quotients[None, :] % RADIX).astype(jnp.float32)
    )
    with_cos = jnp.einsum("rbc,bq->rqc", twisted, jnp.cos(angle_three), precision=highest)
    with_sin = jnp.einsum("rbc,bq->rqc", twisted, jnp.sin(angle_three), precision=highest)
    scale = 1.0 / math.sqrt(line_len)
    real_part = (with_cos[..., :RADIX] + with_sin[..., RADIX:]) * scale
    imag_part = (with_cos[..., RADIX:] - with_sin[..., :RADIX]) * scale
    return (real_part.reshape(n_rows, n_items, NK), imag_part.reshape(n_rows, n_items, NK))


def interp_kernel(local, lat_rows, *refs):
    if local:
        hi_ref, lo_ref, info_ref, out_ref = refs
    else:
        hi_ref, lo_ref, info_ref, base_ref, out_ref = refs
    block = pl.program_id(0)
    start = pl.multiple_of(block * LANES, LANES)
    c_index = lax.broadcasted_iota(jnp.int32, (WINDOW, LANES), 0).astype(jnp.float32)
    j_index = lax.broadcasted_iota(jnp.int32, (WINDOW, LANES), 1).astype(jnp.float32)
    for row in range(lat_rows):
        info = info_ref[row]
        offset_r = info[16:17, :]
        offset_d = info[17:18, :]
        tap = c_index - j_index - offset_d
        masks = [tap == float(b) for b in range(TAPS)]
        if local:
            acc = jnp.zeros(out_ref.shape[1:], jnp.float32)
        else:
            acc = base_ref[row]
        for p in range(2 * ROWS_OUT + 1):
            h = row + p
            inside = ROWS_OUT <= h < ROWS_OUT + lat_rows
            if inside != local:
                continue
            if local:
                index = h - ROWS_OUT
            else:
                index = h if h < ROWS_OUT else h - lat_rows
            picked = []
            for b in range(TAPS):
                value = jnp.zeros_like(offset_r)
                for a in range(TAPS):
                    if 0 <= p - a <= ROWS_OUT:
                        value = jnp.where(offset_r == float(p - a), info[4 * a + b : 4 * a + b + 1, :], value)
                picked.append(value)
            matrix = jnp.where(
                masks[0],
                picked[0],
                jnp.where(masks[1], picked[1], jnp.where(masks[2], picked[2], jnp.where(masks[3], picked[3], 0.0))),
            )
            m_hi = matrix.astype(jnp.bfloat16)
            m_lo = (matrix - m_hi.astype(jnp.float32)).astype(jnp.bfloat16)
            x_hi = hi_ref[index, :, pl.ds(start, WINDOW)]
            x_lo = lo_ref[index, :, pl.ds(start, WINDOW)]
            acc = acc + jnp.dot(x_hi, m_hi, preferred_element_type=jnp.float32)
            acc = acc + jnp.dot(x_hi, m_lo, preferred_element_type=jnp.float32)
            acc = acc + jnp.dot(x_lo, m_hi, preferred_element_type=jnp.float32)
        out_ref[row] = acc


def interpolate(x_hi, x_lo, info, lat_rows, lon_cols, base=None):
    n_rows, n_items, width = x_hi.shape
    blocks = lon_cols // LANES
    whole = pl.BlockSpec((n_rows, n_items, width), lambda jb: (0, 0, 0))
    tile = pl.BlockSpec((lat_rows, n_items, LANES), lambda jb: (0, 0, jb))
    specs = [whole, whole, pl.BlockSpec((lat_rows, info.shape[1], LANES), lambda jb: (0, 0, jb))]
    operands = [x_hi, x_lo, info]
    if base is not None:
        specs.append(tile)
        operands.append(base)
    return pl.pallas_call(
        functools.partial(interp_kernel, base is None, lat_rows),
        out_shape=jax.ShapeDtypeStruct((lat_rows, n_items, lon_cols), jnp.float32),
        grid=(blocks,),
        in_specs=specs,
        out_specs=tile,
        compiler_params=pltpu.CompilerParams(vmem_limit_bytes=48 * 1024 * 1024),
    )(*operands)


def vertical_mix(raw, bands):
    n_levels = raw.shape[-2]
    pad = [(0, 0)] * raw.ndim
    pad[-2] = (2, 2)
    stacked = jnp.pad(raw, pad)
    lead = (None,) * (raw.ndim - 3)
    mixed = bands[lead + (slice(None), 0, slice(None), None)] * stacked[..., 0:n_levels, :]
    for shift_k in range(1, 5):
        mixed = mixed + bands[lead + (slice(None), shift_k, slice(None), None)] * stacked[
            ..., shift_k : shift_k + n_levels, :
        ]
    return mixed


def widen(block):
    left, right = shifted(block, "lon", HALO, block.ndim - 1, True)
    return jnp.concatenate([left, block, right], axis=block.ndim - 1)


def split_rows(rows, width):
    pad = [(0, 0)] * (rows.ndim - 1) + [(0, width - rows.shape[-1])]
    padded = jnp.pad(rows, pad)
    rounded = lax.reduce_precision(padded, exponent_bits=8, mantissa_bits=7)
    return rounded.astype(jnp.bfloat16), (padded - rounded).astype(jnp.bfloat16)


def on_device(fields, weights, stencil, bands):
    n_fields, n_levels, lat_rows, lon_cols = fields.shape
    n_items = n_fields * n_levels
    below_raw, above_raw = shifted(fields, "lat", ROWS_OUT, 2, False)
    n_lat = lax.axis_size("lat")
    n_lon = lax.axis_size("lon")

    def diagonal(block, lat_step, lon_step):
        pairs = []
        for b in range(n_lat):
            if 0 <= b + lat_step < n_lat:
                for k in range(n_lon):
                    pairs.append((b * n_lon + k, (b + lat_step) * n_lon + (k + lon_step) % n_lon))
        return lax.ppermute(block, ("lat", "lon"), pairs)

    low_rows = fields[:, :, lat_rows - ROWS_OUT :, :]
    high_rows = fields[:, :, :ROWS_OUT, :]
    below_left = diagonal(low_rows[..., lon_cols - HALO :], 1, 1)
    below_right = diagonal(low_rows[..., :HALO], 1, -1)
    above_left = diagonal(high_rows[..., lon_cols - HALO :], -1, 1)
    above_right = diagonal(high_rows[..., :HALO], -1, -1)

    width = lon_cols + LANES
    local_rows = vertical_mix(jnp.transpose(fields, (2, 0, 1, 3)), bands)
    local_hi, local_lo = split_rows(widen(local_rows.reshape(lat_rows, n_items, lon_cols)), width)

    lat_start = lax.axis_index("lat") * lat_rows
    lon_start = lax.axis_index("lon") * lon_cols
    line_len = lon_cols * lax.axis_size("lon")
    row_g = lat_start + jnp.arange(lat_rows, dtype=jnp.int32)[:, None]
    col_g = lon_start + jnp.arange(lon_cols, dtype=jnp.int32)[None, :]
    offset_r = (stencil[0] - row_g + ROWS_OUT).astype(jnp.float32)
    offset_d = jnp.mod(stencil[1] - col_g + HALO, line_len).astype(jnp.float32)
    info = jnp.concatenate(
        [
            jnp.transpose(weights, (1, 0, 2)),
            offset_r[:, None, :],
            offset_d[:, None, :],
            jnp.zeros((lat_rows, 6, lon_cols), jnp.float32),
        ],
        axis=1,
    )
    partial = interpolate(local_hi, local_lo, info, lat_rows, lon_cols)

    below_raw, above_raw, corners, partial = lax.optimization_barrier(
        (below_raw, above_raw, (below_left, below_right, above_left, above_right), partial)
    )
    below_left, below_right, above_left, above_right = corners
    halo_raw = jnp.concatenate(
        [
            jnp.concatenate([below_left, below_raw, below_right], axis=3),
            jnp.concatenate([above_left, above_raw, above_right], axis=3),
        ],
        axis=2,
    )
    halo_rows = vertical_mix(jnp.transpose(halo_raw, (2, 0, 1, 3)), bands)
    halo_hi, halo_lo = split_rows(halo_rows.reshape(2 * ROWS_OUT, n_items, lon_cols + 2 * HALO), width)
    departed = interpolate(halo_hi, halo_lo, info, lat_rows, lon_cols, base=partial)

    parts = lax.axis_size("lon")
    me = lax.axis_index("lon")
    chunk = n_items // parts
    pieces = []
    owners = []
    for shift in range(parts):
        target = lax.rem(me + shift, parts)
        piece = lax.dynamic_slice_in_dim(departed, target * chunk, chunk, axis=1)
        if shift:
            piece = lax.ppermute(piece, "lon", [(i, (i + shift) % parts) for i in range(parts)])
        pieces.append(piece)
        owners.append(lax.rem(me - shift + parts, parts))
    real_part, imag_part = spectrum(pieces, owners)
    return (jnp.transpose(real_part, (1, 0, 2)), jnp.transpose(imag_part, (1, 0, 2)))


def solution(mesh):
    placed = (P(None, None, "lat", "lon"), P(None, "lat", "lon"), P(None, "lat", "lon"), P())
    return jax.shard_map(
        on_device,
        mesh=mesh,
        in_specs=placed,
        out_specs=(P("lon", "lat", None), P("lon", "lat", None)),
        check_vma=False,
    )
```

```python
import functools
import math

import jax
import jax.numpy as jnp
from jax import lax
from jax.experimental import pallas as pl
from jax.experimental.pallas import tpu as pltpu
from jax.sharding import PartitionSpec as P

RADIX = 64
NK = 1280
HALO = 16
ROWS_OUT = 3
TAPS = 4
LANES = 128
WINDOW = 256


def shifted(block, axis, width, dim, periodic):
    count = lax.axis_size(axis)
    forward = [(i, i + 1) for i in range(count - 1)]
    if periodic:
        forward.append((count - 1, 0))
    backward = [(target, source) for source, target in forward]
    low = lax.ppermute(
        lax.slice_in_dim(block, block.shape[dim] - width, None, axis=dim), axis, forward
    )
    high = lax.ppermute(lax.slice_in_dim(block, 0, width, axis=dim), axis, backward)
    return low, high


def spectrum(pieces, owners):
    n_rows, n_items, piece_len = pieces[0].shape
    line_len = piece_len * len(pieces)
    highest = lax.Precision.HIGH
    digits = jnp.arange(RADIX, dtype=jnp.int32)
    angle_one = (
        2.0 * math.pi / RADIX * (digits[:, None] * digits[None, :] % RADIX).astype(jnp.float32)
    )
    first_table = jnp.concatenate([jnp.cos(angle_one), -jnp.sin(angle_one)], axis=1)
    per_piece = piece_len // RADIX
    folded = jnp.stack([piece.reshape(n_rows * n_items, per_piece, RADIX) for piece in pieces])
    table = jnp.stack(
        [lax.dynamic_slice_in_dim(first_table, owner * per_piece, per_piece, axis=0) for owner in owners]
    )
    partial_value = jnp.einsum("prab,pac->rbc", folded, table, precision=highest)
    angle_two = (
        2.0
        * math.pi
        / line_len
        * (digits[:, None] * digits[None, :] % line_len).astype(jnp.float32)
    )
    cos_two = jnp.cos(angle_two)
    sin_two = jnp.sin(angle_two)
    part_re = partial_value[..., :RADIX]
    part_im = partial_value[..., RADIX:]
    twisted = jnp.concatenate(
        [part_re * cos_two + part_im * sin_two, part_im * cos_two - part_re * sin_two], axis=-1
    )
    quotients = jnp.arange(NK // RADIX, dtype=jnp.int32)
    angle_three = (
        2.0 * math.pi / RADIX * (digits[:, None] * quotients[None, :] % RADIX).astype(jnp.float32)
    )
    with_cos = jnp.einsum("rbc,bq->rqc", twisted, jnp.cos(angle_three), precision=highest)
    with_sin = jnp.einsum("rbc,bq->rqc", twisted, jnp.sin(angle_three), precision=highest)
    scale = 1.0 / math.sqrt(line_len)
    real_part = (with_cos[..., :RADIX] + with_sin[..., RADIX:]) * scale
    imag_part = (with_cos[..., RADIX:] - with_sin[..., :RADIX]) * scale
    return (real_part.reshape(n_rows, n_items, NK), imag_part.reshape(n_rows, n_items, NK))


def interp_kernel(local, lat_rows, *refs):
    if local:
        hi_ref, lo_ref, info_ref, out_ref = refs
    else:
        hi_ref, lo_ref, info_ref, base_ref, out_ref = refs
    block = pl.program_id(0)
    start = pl.multiple_of(block * LANES, LANES)
    c_index = lax.broadcasted_iota(jnp.int32, (WINDOW, LANES), 0).astype(jnp.float32)
    j_index = lax.broadcasted_iota(jnp.int32, (WINDOW, LANES), 1).astype(jnp.float32)
    for row in range(lat_rows):
        info = info_ref[row]
        offset_r = info[16:17, :]
        offset_d = info[17:18, :]
        tap = c_index - j_index - offset_d
        masks = [tap == float(b) for b in range(TAPS)]
        if local:
            acc = jnp.zeros(out_ref.shape[1:], jnp.float32)
        else:
            acc = base_ref[row]
        for p in range(2 * ROWS_OUT + 1):
            h = row + p
            inside = ROWS_OUT <= h < ROWS_OUT + lat_rows
            if inside != local:
                continue
            if local:
                index = h - ROWS_OUT
            else:
                index = h if h < ROWS_OUT else h - lat_rows
            picked = []
            for b in range(TAPS):
                value = jnp.zeros_like(offset_r)
                for a in range(TAPS):
                    if 0 <= p - a <= ROWS_OUT:
                        value = jnp.where(offset_r == float(p - a), info[4 * a + b : 4 * a + b + 1, :], value)
                picked.append(value)
            matrix = jnp.where(
                masks[0],
                picked[0],
                jnp.where(masks[1], picked[1], jnp.where(masks[2], picked[2], jnp.where(masks[3], picked[3], 0.0))),
            )
            m_hi = matrix.astype(jnp.bfloat16)
            m_lo = (matrix - m_hi.astype(jnp.float32)).astype(jnp.bfloat16)
            x_hi = hi_ref[index, :, pl.ds(start, WINDOW)]
            x_lo = lo_ref[index, :, pl.ds(start, WINDOW)]
            acc = acc + jnp.dot(x_hi, m_hi, preferred_element_type=jnp.float32)
            acc = acc + jnp.dot(x_hi, m_lo, preferred_element_type=jnp.float32)
            acc = acc + jnp.dot(x_lo, m_hi, preferred_element_type=jnp.float32)
        out_ref[row] = acc


def interpolate(x_hi, x_lo, info, lat_rows, lon_cols, base=None):
    n_rows, n_items, width = x_hi.shape
    blocks = lon_cols // LANES
    whole = pl.BlockSpec((n_rows, n_items, width), lambda jb: (0, 0, 0))
    tile = pl.BlockSpec((lat_rows, n_items, LANES), lambda jb: (0, 0, jb))
    specs = [whole, whole, pl.BlockSpec((lat_rows, info.shape[1], LANES), lambda jb: (0, 0, jb))]
    operands = [x_hi, x_lo, info]
    if base is not None:
        specs.append(tile)
        operands.append(base)
    return pl.pallas_call(
        functools.partial(interp_kernel, base is None, lat_rows),
        out_shape=jax.ShapeDtypeStruct((lat_rows, n_items, lon_cols), jnp.float32),
        grid=(blocks,),
        in_specs=specs,
        out_specs=tile,
        compiler_params=pltpu.CompilerParams(vmem_limit_bytes=48 * 1024 * 1024),
    )(*operands)


def vertical_mix(raw, bands):
    n_levels = raw.shape[-2]
    pad = [(0, 0)] * raw.ndim
    pad[-2] = (2, 2)
    stacked = jnp.pad(raw, pad)
    lead = (None,) * (raw.ndim - 3)
    mixed = bands[lead + (slice(None), 0, slice(None), None)] * stacked[..., 0:n_levels, :]
    for shift_k in range(1, 5):
        mixed = mixed + bands[lead + (slice(None), shift_k, slice(None), None)] * stacked[
            ..., shift_k : shift_k + n_levels, :
        ]
    return mixed


def widen(block):
    left, right = shifted(block, "lon", HALO, block.ndim - 1, True)
    return jnp.concatenate([left, block, right], axis=block.ndim - 1)


def split_rows(rows, width):
    pad = [(0, 0)] * (rows.ndim - 1) + [(0, width - rows.shape[-1])]
    padded = jnp.pad(rows, pad)
    rounded = lax.reduce_precision(padded, exponent_bits=8, mantissa_bits=7)
    return rounded.astype(jnp.bfloat16), (padded - rounded).astype(jnp.bfloat16)


def on_device(fields, weights, stencil, bands):
    n_fields, n_levels, lat_rows, lon_cols = fields.shape
    n_items = n_fields * n_levels
    below_raw, above_raw = shifted(fields, "lat", ROWS_OUT, 2, False)

    width = lon_cols + LANES
    local_rows = vertical_mix(jnp.transpose(fields, (2, 0, 1, 3)), bands)
    local_hi, local_lo = split_rows(widen(local_rows.reshape(lat_rows, n_items, lon_cols)), width)

    lat_start = lax.axis_index("lat") * lat_rows
    lon_start = lax.axis_index("lon") * lon_cols
    line_len = lon_cols * lax.axis_size("lon")
    row_g = lat_start + jnp.arange(lat_rows, dtype=jnp.int32)[:, None]
    col_g = lon_start + jnp.arange(lon_cols, dtype=jnp.int32)[None, :]
    offset_r = (stencil[0] - row_g + ROWS_OUT).astype(jnp.float32)
    offset_d = jnp.mod(stencil[1] - col_g + HALO, line_len).astype(jnp.float32)
    info = jnp.concatenate(
        [
            jnp.transpose(weights, (1, 0, 2)),
            offset_r[:, None, :],
            offset_d[:, None, :],
            jnp.zeros((lat_rows, 6, lon_cols), jnp.float32),
        ],
        axis=1,
    )
    partial = interpolate(local_hi, local_lo, info, lat_rows, lon_cols)

    below_raw, above_raw, partial = lax.optimization_barrier((below_raw, above_raw, partial))
    halo_raw = jnp.concatenate([below_raw, above_raw], axis=2)
    halo_rows = vertical_mix(jnp.transpose(halo_raw, (2, 0, 1, 3)), bands)
    halo_hi, halo_lo = split_rows(widen(halo_rows.reshape(2 * ROWS_OUT, n_items, lon_cols)), width)
    departed = interpolate(halo_hi, halo_lo, info, lat_rows, lon_cols, base=partial)

    parts = lax.axis_size("lon")
    me = lax.axis_index("lon")
    chunk = n_items // parts
    pieces = []
    owners = []
    for shift in range(parts):
        target = lax.rem(me + shift, parts)
        piece = lax.dynamic_slice_in_dim(departed, target * chunk, chunk, axis=1)
        if shift:
            piece = lax.ppermute(piece, "lon", [(i, (i + shift) % parts) for i in range(parts)])
        pieces.append(piece)
        owners.append(lax.rem(me - shift + parts, parts))
    real_part, imag_part = spectrum(pieces, owners)
    return (jnp.transpose(real_part, (1, 0, 2)), jnp.transpose(imag_part, (1, 0, 2)))


def solution(mesh):
    placed = (P(None, None, "lat", "lon"), P(None, "lat", "lon"), P(None, "lat", "lon"), P())
    return jax.shard_map(
        on_device,
        mesh=mesh,
        in_specs=placed,
        out_specs=(P("lon", "lat", None), P("lon", "lat", None)),
        check_vma=False,
    )
```

```python
import functools
import math

import jax
import jax.numpy as jnp
from jax import lax
from jax.experimental import pallas as pl
from jax.experimental.pallas import tpu as pltpu
from jax.sharding import PartitionSpec as P

RADIX = 64
NK = 1280
HALO = 16
ROWS_OUT = 3
TAPS = 4
LANES = 128
WINDOW = 256


def shifted(block, axis, width, dim, periodic):
    count = lax.axis_size(axis)
    forward = [(i, i + 1) for i in range(count - 1)]
    if periodic:
        forward.append((count - 1, 0))
    backward = [(target, source) for source, target in forward]
    low = lax.ppermute(
        lax.slice_in_dim(block, block.shape[dim] - width, None, axis=dim), axis, forward
    )
    high = lax.ppermute(lax.slice_in_dim(block, 0, width, axis=dim), axis, backward)
    return low, high


def spectrum(pieces, owners):
    n_rows, n_items, piece_len = pieces[0].shape
    line_len = piece_len * len(pieces)
    highest = lax.Precision.HIGH
    digits = jnp.arange(RADIX, dtype=jnp.int32)
    angle_one = (
        2.0 * math.pi / RADIX * (digits[:, None] * digits[None, :] % RADIX).astype(jnp.float32)
    )
    first_table = jnp.concatenate([jnp.cos(angle_one), -jnp.sin(angle_one)], axis=1)
    per_piece = piece_len // RADIX
    folded = jnp.stack([piece.reshape(n_rows * n_items, per_piece, RADIX) for piece in pieces])
    table = jnp.stack(
        [lax.dynamic_slice_in_dim(first_table, owner * per_piece, per_piece, axis=0) for owner in owners]
    )
    partial_value = jnp.einsum("prab,pac->rbc", folded, table, precision=highest)
    angle_two = (
        2.0
        * math.pi
        / line_len
        * (digits[:, None] * digits[None, :] % line_len).astype(jnp.float32)
    )
    cos_two = jnp.cos(angle_two)
    sin_two = jnp.sin(angle_two)
    part_re = partial_value[..., :RADIX]
    part_im = partial_value[..., RADIX:]
    twisted = jnp.concatenate(
        [part_re * cos_two + part_im * sin_two, part_im * cos_two - part_re * sin_two], axis=-1
    )
    quotients = jnp.arange(NK // RADIX, dtype=jnp.int32)
    angle_three = (
        2.0 * math.pi / RADIX * (digits[:, None] * quotients[None, :] % RADIX).astype(jnp.float32)
    )
    with_cos = jnp.einsum("rbc,bq->rqc", twisted, jnp.cos(angle_three), precision=highest)
    with_sin = jnp.einsum("rbc,bq->rqc", twisted, jnp.sin(angle_three), precision=highest)
    scale = 1.0 / math.sqrt(line_len)
    real_part = (with_cos[..., :RADIX] + with_sin[..., RADIX:]) * scale
    imag_part = (with_cos[..., RADIX:] - with_sin[..., :RADIX]) * scale
    return (real_part.reshape(n_rows, n_items, NK), imag_part.reshape(n_rows, n_items, NK))


def interp_kernel(local, lat_rows, *refs):
    if local:
        hi_ref, lo_ref, info_ref, out_ref = refs
    else:
        hi_ref, lo_ref, info_ref, base_ref, out_ref = refs
    block = pl.program_id(0)
    start = pl.multiple_of(block * LANES, LANES)
    c_index = lax.broadcasted_iota(jnp.int32, (WINDOW, LANES), 0).astype(jnp.float32)
    j_index = lax.broadcasted_iota(jnp.int32, (WINDOW, LANES), 1).astype(jnp.float32)
    for row in range(lat_rows):
        info = info_ref[row]
        offset_r = info[16:17, :]
        offset_d = info[17:18, :]
        tap = c_index - j_index - offset_d
        masks = [tap == float(b) for b in range(TAPS)]
        if local:
            acc = jnp.zeros(out_ref.shape[1:], jnp.float32)
        else:
            acc = base_ref[row]
        for p in range(2 * ROWS_OUT + 1):
            h = row + p
            inside = ROWS_OUT <= h < ROWS_OUT + lat_rows
            if inside != local:
                continue
            if local:
                index = h - ROWS_OUT
            else:
                index = h if h < ROWS_OUT else h - lat_rows
            picked = []
            for b in range(TAPS):
                value = jnp.zeros_like(offset_r)
                for a in range(TAPS):
                    if 0 <= p - a <= ROWS_OUT:
                        value = jnp.where(offset_r == float(p - a), info[4 * a + b : 4 * a + b + 1, :], value)
                picked.append(value)
            matrix = jnp.where(
                masks[0],
                picked[0],
                jnp.where(masks[1], picked[1], jnp.where(masks[2], picked[2], jnp.where(masks[3], picked[3], 0.0))),
            )
            m_hi = matrix.astype(jnp.bfloat16)
            m_lo = (matrix - m_hi.astype(jnp.float32)).astype(jnp.bfloat16)
            x_hi = hi_ref[index, :, pl.ds(start, WINDOW)]
            x_lo = lo_ref[index, :, pl.ds(start, WINDOW)]
            both = jnp.dot(x_hi, jnp.concatenate([m_hi, m_lo], axis=1), preferred_element_type=jnp.float32)
            acc = acc + both[:, :LANES] + both[:, LANES:]
            acc = acc + jnp.dot(x_lo, m_hi, preferred_element_type=jnp.float32)
        out_ref[row] = acc


def interpolate(x_hi, x_lo, info, lat_rows, lon_cols, base=None):
    n_rows, n_items, width = x_hi.shape
    blocks = lon_cols // LANES
    whole = pl.BlockSpec((n_rows, n_items, width), lambda jb: (0, 0, 0))
    tile = pl.BlockSpec((lat_rows, n_items, LANES), lambda jb: (0, 0, jb))
    specs = [whole, whole, pl.BlockSpec((lat_rows, info.shape[1], LANES), lambda jb: (0, 0, jb))]
    operands = [x_hi, x_lo, info]
    if base is not None:
        specs.append(tile)
        operands.append(base)
    return pl.pallas_call(
        functools.partial(interp_kernel, base is None, lat_rows),
        out_shape=jax.ShapeDtypeStruct((lat_rows, n_items, lon_cols), jnp.float32),
        grid=(blocks,),
        in_specs=specs,
        out_specs=tile,
        compiler_params=pltpu.CompilerParams(vmem_limit_bytes=48 * 1024 * 1024),
    )(*operands)


def vertical_mix(raw, bands):
    n_levels = raw.shape[-2]
    pad = [(0, 0)] * raw.ndim
    pad[-2] = (2, 2)
    stacked = jnp.pad(raw, pad)
    lead = (None,) * (raw.ndim - 3)
    mixed = bands[lead + (slice(None), 0, slice(None), None)] * stacked[..., 0:n_levels, :]
    for shift_k in range(1, 5):
        mixed = mixed + bands[lead + (slice(None), shift_k, slice(None), None)] * stacked[
            ..., shift_k : shift_k + n_levels, :
        ]
    return mixed


def widen(block):
    left, right = shifted(block, "lon", HALO, block.ndim - 1, True)
    return jnp.concatenate([left, block, right], axis=block.ndim - 1)


def split_rows(rows, width):
    pad = [(0, 0)] * (rows.ndim - 1) + [(0, width - rows.shape[-1])]
    padded = jnp.pad(rows, pad)
    rounded = lax.reduce_precision(padded, exponent_bits=8, mantissa_bits=7)
    return rounded.astype(jnp.bfloat16), (padded - rounded).astype(jnp.bfloat16)


def on_device(fields, weights, stencil, bands):
    n_fields, n_levels, lat_rows, lon_cols = fields.shape
    n_items = n_fields * n_levels
    below_raw, above_raw = shifted(fields, "lat", ROWS_OUT, 2, False)

    width = lon_cols + LANES
    local_rows = vertical_mix(jnp.transpose(fields, (2, 0, 1, 3)), bands)
    local_hi, local_lo = split_rows(widen(local_rows.reshape(lat_rows, n_items, lon_cols)), width)

    lat_start = lax.axis_index("lat") * lat_rows
    lon_start = lax.axis_index("lon") * lon_cols
    line_len = lon_cols * lax.axis_size("lon")
    row_g = lat_start + jnp.arange(lat_rows, dtype=jnp.int32)[:, None]
    col_g = lon_start + jnp.arange(lon_cols, dtype=jnp.int32)[None, :]
    offset_r = (stencil[0] - row_g + ROWS_OUT).astype(jnp.float32)
    offset_d = jnp.mod(stencil[1] - col_g + HALO, line_len).astype(jnp.float32)
    info = jnp.concatenate(
        [
            jnp.transpose(weights, (1, 0, 2)),
            offset_r[:, None, :],
            offset_d[:, None, :],
            jnp.zeros((lat_rows, 6, lon_cols), jnp.float32),
        ],
        axis=1,
    )
    partial = interpolate(local_hi, local_lo, info, lat_rows, lon_cols)

    below_raw, above_raw, partial = lax.optimization_barrier((below_raw, above_raw, partial))
    halo_raw = jnp.concatenate([below_raw, above_raw], axis=2)
    halo_rows = vertical_mix(jnp.transpose(halo_raw, (2, 0, 1, 3)), bands)
    halo_hi, halo_lo = split_rows(widen(halo_rows.reshape(2 * ROWS_OUT, n_items, lon_cols)), width)
    departed = interpolate(halo_hi, halo_lo, info, lat_rows, lon_cols, base=partial)

    parts = lax.axis_size("lon")
    me = lax.axis_index("lon")
    chunk = n_items // parts
    pieces = []
    owners = []
    for shift in range(parts):
        target = lax.rem(me + shift, parts)
        piece = lax.dynamic_slice_in_dim(departed, target * chunk, chunk, axis=1)
        if shift:
            piece = lax.ppermute(piece, "lon", [(i, (i + shift) % parts) for i in range(parts)])
        pieces.append(piece)
        owners.append(lax.rem(me - shift + parts, parts))
    real_part, imag_part = spectrum(pieces, owners)
    return (jnp.transpose(real_part, (1, 0, 2)), jnp.transpose(imag_part, (1, 0, 2)))


def solution(mesh):
    placed = (P(None, None, "lat", "lon"), P(None, "lat", "lon"), P(None, "lat", "lon"), P())
    return jax.shard_map(
        on_device,
        mesh=mesh,
        in_specs=placed,
        out_specs=(P("lon", "lat", None), P("lon", "lat", None)),
        check_vma=False,
    )
```

```python
import functools
import math

import jax
import jax.numpy as jnp
from jax import lax
from jax.experimental import pallas as pl
from jax.experimental.pallas import tpu as pltpu
from jax.sharding import PartitionSpec as P

RADIX = 64
NK = 1280
HALO = 16
ROWS_OUT = 3
TAPS = 4
LANES = 128
WINDOW = 256


def shifted(block, axis, width, dim, periodic):
    count = lax.axis_size(axis)
    forward = [(i, i + 1) for i in range(count - 1)]
    if periodic:
        forward.append((count - 1, 0))
    backward = [(target, source) for source, target in forward]
    low = lax.ppermute(
        lax.slice_in_dim(block, block.shape[dim] - width, None, axis=dim), axis, forward
    )
    high = lax.ppermute(lax.slice_in_dim(block, 0, width, axis=dim), axis, backward)
    return low, high


def spectrum(pieces, owners):
    n_rows, n_items, piece_len = pieces[0].shape
    line_len = piece_len * len(pieces)
    highest = lax.Precision.HIGH
    digits = jnp.arange(RADIX, dtype=jnp.int32)
    angle_one = (
        2.0 * math.pi / RADIX * (digits[:, None] * digits[None, :] % RADIX).astype(jnp.float32)
    )
    first_table = jnp.concatenate([jnp.cos(angle_one), -jnp.sin(angle_one)], axis=1)
    per_piece = piece_len // RADIX
    folded = jnp.stack([piece.reshape(n_rows * n_items, per_piece, RADIX) for piece in pieces])
    table = jnp.stack(
        [lax.dynamic_slice_in_dim(first_table, owner * per_piece, per_piece, axis=0) for owner in owners]
    )
    partial_value = jnp.einsum("prab,pac->rbc", folded, table, precision=highest)
    angle_two = (
        2.0
        * math.pi
        / line_len
        * (digits[:, None] * digits[None, :] % line_len).astype(jnp.float32)
    )
    cos_two = jnp.cos(angle_two)
    sin_two = jnp.sin(angle_two)
    part_re = partial_value[..., :RADIX]
    part_im = partial_value[..., RADIX:]
    twisted = jnp.concatenate(
        [part_re * cos_two + part_im * sin_two, part_im * cos_two - part_re * sin_two], axis=-1
    )
    quotients = jnp.arange(NK // RADIX, dtype=jnp.int32)
    angle_three = (
        2.0 * math.pi / RADIX * (digits[:, None] * quotients[None, :] % RADIX).astype(jnp.float32)
    )
    with_cos = jnp.einsum("rbc,bq->rqc", twisted, jnp.cos(angle_three), precision=highest)
    with_sin = jnp.einsum("rbc,bq->rqc", twisted, jnp.sin(angle_three), precision=highest)
    scale = 1.0 / math.sqrt(line_len)
    real_part = (with_cos[..., :RADIX] + with_sin[..., RADIX:]) * scale
    imag_part = (with_cos[..., RADIX:] - with_sin[..., :RADIX]) * scale
    return (real_part.reshape(n_rows, n_items, NK), imag_part.reshape(n_rows, n_items, NK))


def interp_kernel(local, lat_rows, *refs):
    if local:
        hi_ref, lo_ref, info_ref, out_ref = refs
    else:
        hi_ref, lo_ref, info_ref, base_ref, out_ref = refs
    block = pl.program_id(0)
    start = pl.multiple_of(block * LANES, LANES)
    c_index = lax.broadcasted_iota(jnp.int32, (WINDOW, LANES), 0).astype(jnp.float32)
    j_index = lax.broadcasted_iota(jnp.int32, (WINDOW, LANES), 1).astype(jnp.float32)
    for row in range(lat_rows):
        info = info_ref[row]
        offset_r = info[16:17, :]
        offset_d = info[17:18, :]
        tap = c_index - j_index - offset_d
        masks = [tap == float(b) for b in range(TAPS)]
        if local:
            acc = jnp.zeros(out_ref.shape[1:], jnp.float32)
        else:
            acc = base_ref[row]
        for p in range(2 * ROWS_OUT + 1):
            h = row + p
            inside = ROWS_OUT <= h < ROWS_OUT + lat_rows
            if inside != local:
                continue
            if local:
                index = h - ROWS_OUT
            else:
                index = h if h < ROWS_OUT else h - lat_rows
            picked = []
            for b in range(TAPS):
                value = jnp.zeros_like(offset_r)
                for a in range(TAPS):
                    if 0 <= p - a <= ROWS_OUT:
                        value = jnp.where(offset_r == float(p - a), info[4 * a + b : 4 * a + b + 1, :], value)
                picked.append(value)
            matrix = jnp.where(
                masks[0],
                picked[0],
                jnp.where(masks[1], picked[1], jnp.where(masks[2], picked[2], jnp.where(masks[3], picked[3], 0.0))),
            )
            m_hi = matrix.astype(jnp.bfloat16)
            m_lo = (matrix - m_hi.astype(jnp.float32)).astype(jnp.bfloat16)
            x_hi = hi_ref[index, :, pl.ds(start, WINDOW)]
            x_lo = lo_ref[index, :, pl.ds(start, WINDOW)]
            both = jnp.dot(x_hi, jnp.concatenate([m_hi, m_lo], axis=1), preferred_element_type=jnp.float32)
            acc = acc + both[:, :LANES] + both[:, LANES:]
            acc = acc + jnp.dot(x_lo, m_hi, preferred_element_type=jnp.float32)
        out_ref[row] = acc


def interpolate(x_hi, x_lo, info, lat_rows, lon_cols, base=None):
    n_rows, n_items, width = x_hi.shape
    blocks = lon_cols // LANES
    whole = pl.BlockSpec((n_rows, n_items, width), lambda jb: (0, 0, 0))
    tile = pl.BlockSpec((lat_rows, n_items, LANES), lambda jb: (0, 0, jb))
    specs = [whole, whole, pl.BlockSpec((lat_rows, info.shape[1], LANES), lambda jb: (0, 0, jb))]
    operands = [x_hi, x_lo, info]
    if base is not None:
        specs.append(tile)
        operands.append(base)
    return pl.pallas_call(
        functools.partial(interp_kernel, base is None, lat_rows),
        out_shape=jax.ShapeDtypeStruct((lat_rows, n_items, lon_cols), jnp.float32),
        grid=(blocks,),
        in_specs=specs,
        out_specs=tile,
        compiler_params=pltpu.CompilerParams(vmem_limit_bytes=48 * 1024 * 1024),
    )(*operands)


def vertical_mix(raw, bands):
    n_levels = raw.shape[-2]
    pad = [(0, 0)] * raw.ndim
    pad[-2] = (2, 2)
    stacked = jnp.pad(raw, pad)
    lead = (None,) * (raw.ndim - 3)
    mixed = bands[lead + (slice(None), 0, slice(None), None)] * stacked[..., 0:n_levels, :]
    for shift_k in range(1, 5):
        mixed = mixed + bands[lead + (slice(None), shift_k, slice(None), None)] * stacked[
            ..., shift_k : shift_k + n_levels, :
        ]
    return mixed


def widen(block):
    left, right = shifted(block, "lon", HALO, block.ndim - 1, True)
    return jnp.concatenate([left, block, right], axis=block.ndim - 1)


def split_rows(rows, width):
    pad = [(0, 0)] * (rows.ndim - 1) + [(0, width - rows.shape[-1])]
    padded = jnp.pad(rows, pad)
    rounded = lax.reduce_precision(padded, exponent_bits=8, mantissa_bits=7)
    return rounded.astype(jnp.bfloat16), (padded - rounded).astype(jnp.bfloat16)


def on_device(fields, weights, stencil, bands):
    n_fields, n_levels, lat_rows, lon_cols = fields.shape
    n_items = n_fields * n_levels
    count = lax.axis_size("lat")
    forward = [(i, i + 1) for i in range(count - 1)]
    backward = [(target, source) for source, target in forward]
    edge_low = vertical_mix(jnp.transpose(fields[:, :, lat_rows - ROWS_OUT :, :], (2, 0, 1, 3)), bands)
    edge_high = vertical_mix(jnp.transpose(fields[:, :, :ROWS_OUT, :], (2, 0, 1, 3)), bands)
    below_raw = lax.ppermute(jnp.transpose(edge_low, (1, 2, 0, 3)), "lat", forward)
    above_raw = lax.ppermute(jnp.transpose(edge_high, (1, 2, 0, 3)), "lat", backward)

    width = lon_cols + LANES
    local_rows = vertical_mix(jnp.transpose(fields, (2, 0, 1, 3)), bands)
    local_hi, local_lo = split_rows(widen(local_rows.reshape(lat_rows, n_items, lon_cols)), width)

    lat_start = lax.axis_index("lat") * lat_rows
    lon_start = lax.axis_index("lon") * lon_cols
    line_len = lon_cols * lax.axis_size("lon")
    row_g = lat_start + jnp.arange(lat_rows, dtype=jnp.int32)[:, None]
    col_g = lon_start + jnp.arange(lon_cols, dtype=jnp.int32)[None, :]
    offset_r = (stencil[0] - row_g + ROWS_OUT).astype(jnp.float32)
    offset_d = jnp.mod(stencil[1] - col_g + HALO, line_len).astype(jnp.float32)
    info = jnp.concatenate(
        [
            jnp.transpose(weights, (1, 0, 2)),
            offset_r[:, None, :],
            offset_d[:, None, :],
            jnp.zeros((lat_rows, 6, lon_cols), jnp.float32),
        ],
        axis=1,
    )
    partial = interpolate(local_hi, local_lo, info, lat_rows, lon_cols)

    below_raw, above_raw, partial = lax.optimization_barrier((below_raw, above_raw, partial))
    halo_raw = jnp.concatenate([below_raw, above_raw], axis=2)
    halo_rows = jnp.transpose(halo_raw, (2, 0, 1, 3))
    halo_hi, halo_lo = split_rows(widen(halo_rows.reshape(2 * ROWS_OUT, n_items, lon_cols)), width)
    departed = interpolate(halo_hi, halo_lo, info, lat_rows, lon_cols, base=partial)

    parts = lax.axis_size("lon")
    me = lax.axis_index("lon")
    chunk = n_items // parts
    pieces = []
    owners = []
    for shift in range(parts):
        target = lax.rem(me + shift, parts)
        piece = lax.dynamic_slice_in_dim(departed, target * chunk, chunk, axis=1)
        if shift:
            piece = lax.ppermute(piece, "lon", [(i, (i + shift) % parts) for i in range(parts)])
        pieces.append(piece)
        owners.append(lax.rem(me - shift + parts, parts))
    real_part, imag_part = spectrum(pieces, owners)
    return (jnp.transpose(real_part, (1, 0, 2)), jnp.transpose(imag_part, (1, 0, 2)))


def solution(mesh):
    placed = (P(None, None, "lat", "lon"), P(None, "lat", "lon"), P(None, "lat", "lon"), P())
    return jax.shard_map(
        on_device,
        mesh=mesh,
        in_specs=placed,
        out_specs=(P("lon", "lat", None), P("lon", "lat", None)),
        check_vma=False,
    )
```

```python
import functools
import math

import jax
import jax.numpy as jnp
from jax import lax
from jax.experimental import pallas as pl
from jax.experimental.pallas import tpu as pltpu
from jax.sharding import PartitionSpec as P

RADIX = 64
NK = 1280
HALO = 16
ROWS_OUT = 3
TAPS = 4
LANES = 128
WINDOW = 256


def shifted(block, axis, width, dim, periodic):
    count = lax.axis_size(axis)
    forward = [(i, i + 1) for i in range(count - 1)]
    if periodic:
        forward.append((count - 1, 0))
    backward = [(target, source) for source, target in forward]
    low = lax.ppermute(
        lax.slice_in_dim(block, block.shape[dim] - width, None, axis=dim), axis, forward
    )
    high = lax.ppermute(lax.slice_in_dim(block, 0, width, axis=dim), axis, backward)
    return low, high


def spectrum(pieces, owners):
    n_rows, n_items, piece_len = pieces[0].shape
    line_len = piece_len * len(pieces)
    highest = lax.Precision.HIGH
    digits = jnp.arange(RADIX, dtype=jnp.int32)
    angle_one = (
        2.0 * math.pi / RADIX * (digits[:, None] * digits[None, :] % RADIX).astype(jnp.float32)
    )
    first_table = jnp.concatenate([jnp.cos(angle_one), -jnp.sin(angle_one)], axis=1)
    per_piece = piece_len // RADIX
    folded = jnp.stack([piece.reshape(n_rows * n_items, per_piece, RADIX) for piece in pieces])
    table = jnp.stack(
        [lax.dynamic_slice_in_dim(first_table, owner * per_piece, per_piece, axis=0) for owner in owners]
    )
    partial_value = jnp.einsum("prab,pac->rbc", folded, table, precision=highest)
    angle_two = (
        2.0
        * math.pi
        / line_len
        * (digits[:, None] * digits[None, :] % line_len).astype(jnp.float32)
    )
    cos_two = jnp.cos(angle_two)
    sin_two = jnp.sin(angle_two)
    part_re = partial_value[..., :RADIX]
    part_im = partial_value[..., RADIX:]
    twisted = jnp.concatenate(
        [part_re * cos_two + part_im * sin_two, part_im * cos_two - part_re * sin_two], axis=-1
    )
    quotients = jnp.arange(NK // RADIX, dtype=jnp.int32)
    angle_three = (
        2.0 * math.pi / RADIX * (digits[:, None] * quotients[None, :] % RADIX).astype(jnp.float32)
    )
    with_cos = jnp.einsum("rbc,bq->rqc", twisted, jnp.cos(angle_three), precision=highest)
    with_sin = jnp.einsum("rbc,bq->rqc", twisted, jnp.sin(angle_three), precision=highest)
    scale = 1.0 / math.sqrt(line_len)
    real_part = (with_cos[..., :RADIX] + with_sin[..., RADIX:]) * scale
    imag_part = (with_cos[..., RADIX:] - with_sin[..., :RADIX]) * scale
    return (real_part.reshape(n_rows, n_items, NK), imag_part.reshape(n_rows, n_items, NK))


def interp_kernel(local, lat_rows, *refs):
    if local:
        hi_ref, lo_ref, info_ref, out_ref = refs
    else:
        hi_ref, lo_ref, info_ref, base_ref, out_ref = refs
    block = pl.program_id(0)
    start = pl.multiple_of(block * LANES, LANES)
    c_index = lax.broadcasted_iota(jnp.int32, (WINDOW, LANES), 0).astype(jnp.float32)
    j_index = lax.broadcasted_iota(jnp.int32, (WINDOW, LANES), 1).astype(jnp.float32)
    for row in range(lat_rows):
        info = info_ref[row]
        offset_r = info[16:17, :]
        offset_d = info[17:18, :]
        tap = c_index - j_index - offset_d
        masks = [tap == float(b) for b in range(TAPS)]
        if local:
            acc = jnp.zeros(out_ref.shape[1:], jnp.float32)
        else:
            acc = base_ref[row]
        for p in range(2 * ROWS_OUT + 1):
            h = row + p
            inside = ROWS_OUT <= h < ROWS_OUT + lat_rows
            if inside != local:
                continue
            if local:
                index = h - ROWS_OUT
            else:
                index = h if h < ROWS_OUT else h - lat_rows
            picked = []
            for b in range(TAPS):
                value = jnp.zeros_like(offset_r)
                for a in range(TAPS):
                    if 0 <= p - a <= ROWS_OUT:
                        value = jnp.where(offset_r == float(p - a), info[4 * a + b : 4 * a + b + 1, :], value)
                picked.append(value)
            matrix = jnp.where(
                masks[0],
                picked[0],
                jnp.where(masks[1], picked[1], jnp.where(masks[2], picked[2], jnp.where(masks[3], picked[3], 0.0))),
            )
            m_hi = matrix.astype(jnp.bfloat16)
            m_lo = (matrix - m_hi.astype(jnp.float32)).astype(jnp.bfloat16)
            x_hi = hi_ref[index, :, pl.ds(start, WINDOW)]
            x_lo = lo_ref[index, :, pl.ds(start, WINDOW)]
            both = jnp.dot(x_hi, jnp.concatenate([m_hi, m_lo], axis=1), preferred_element_type=jnp.float32)
            acc = acc + both[:, :LANES] + both[:, LANES:]
            acc = acc + jnp.dot(x_lo, m_hi, preferred_element_type=jnp.float32)
        out_ref[row] = acc


def interpolate(x_hi, x_lo, info, lat_rows, lon_cols, base=None):
    n_rows, n_items, width = x_hi.shape
    blocks = lon_cols // LANES
    whole = pl.BlockSpec((n_rows, n_items, width), lambda jb: (0, 0, 0))
    tile = pl.BlockSpec((lat_rows, n_items, LANES), lambda jb: (0, 0, jb))
    specs = [whole, whole, pl.BlockSpec((lat_rows, info.shape[1], LANES), lambda jb: (0, 0, jb))]
    operands = [x_hi, x_lo, info]
    if base is not None:
        specs.append(tile)
        operands.append(base)
    return pl.pallas_call(
        functools.partial(interp_kernel, base is None, lat_rows),
        out_shape=jax.ShapeDtypeStruct((lat_rows, n_items, lon_cols), jnp.float32),
        grid=(blocks,),
        in_specs=specs,
        out_specs=tile,
        compiler_params=pltpu.CompilerParams(vmem_limit_bytes=48 * 1024 * 1024),
    )(*operands)


def vertical_mix(raw, bands):
    n_levels = raw.shape[-2]
    pad = [(0, 0)] * raw.ndim
    pad[-2] = (2, 2)
    stacked = jnp.pad(raw, pad)
    lead = (None,) * (raw.ndim - 3)
    mixed = bands[lead + (slice(None), 0, slice(None), None)] * stacked[..., 0:n_levels, :]
    for shift_k in range(1, 5):
        mixed = mixed + bands[lead + (slice(None), shift_k, slice(None), None)] * stacked[
            ..., shift_k : shift_k + n_levels, :
        ]
    return mixed


def widen(block):
    left, right = shifted(block, "lon", HALO, block.ndim - 1, True)
    return jnp.concatenate([left, block, right], axis=block.ndim - 1)


def split_rows(rows, width):
    pad = [(0, 0)] * (rows.ndim - 1) + [(0, width - rows.shape[-1])]
    padded = jnp.pad(rows, pad)
    rounded = lax.reduce_precision(padded, exponent_bits=8, mantissa_bits=7)
    return rounded.astype(jnp.bfloat16), (padded - rounded).astype(jnp.bfloat16)


def on_device(fields, weights, stencil, bands):
    n_fields, n_levels, lat_rows, lon_cols = fields.shape
    n_items = n_fields * n_levels
    below_raw, above_raw = shifted(fields, "lat", ROWS_OUT, 2, False)

    width = lon_cols + LANES
    local_rows = vertical_mix(jnp.transpose(fields, (2, 0, 1, 3)), bands)
    local_hi, local_lo = split_rows(widen(local_rows.reshape(lat_rows, n_items, lon_cols)), width)

    lat_start = lax.axis_index("lat") * lat_rows
    lon_start = lax.axis_index("lon") * lon_cols
    line_len = lon_cols * lax.axis_size("lon")
    row_g = lat_start + jnp.arange(lat_rows, dtype=jnp.int32)[:, None]
    col_g = lon_start + jnp.arange(lon_cols, dtype=jnp.int32)[None, :]
    offset_r = (stencil[0] - row_g + ROWS_OUT).astype(jnp.float32)
    offset_d = jnp.mod(stencil[1] - col_g + HALO, line_len).astype(jnp.float32)
    info = jnp.concatenate(
        [
            jnp.transpose(weights, (1, 0, 2)),
            offset_r[:, None, :],
            offset_d[:, None, :],
            jnp.zeros((lat_rows, 6, lon_cols), jnp.float32),
        ],
        axis=1,
    )
    partial = interpolate(local_hi, local_lo, info, lat_rows, lon_cols)

    below_raw, above_raw, partial = lax.optimization_barrier((below_raw, above_raw, partial))
    halo_raw = jnp.concatenate([below_raw, above_raw], axis=2)
    halo_rows = vertical_mix(jnp.transpose(halo_raw, (2, 0, 1, 3)), bands)
    halo_main = halo_rows.reshape(2 * ROWS_OUT, n_items, lon_cols)
    left, right = shifted(halo_main, "lon", HALO, 2, True)
    parts_hi = []
    parts_lo = []
    for piece in (left, halo_main, right):
        piece_hi, piece_lo = split_rows(piece, piece.shape[-1])
        parts_hi.append(piece_hi)
        parts_lo.append(piece_lo)
    filler = jnp.zeros((2 * ROWS_OUT, n_items, width - lon_cols - 2 * HALO), jnp.bfloat16)
    halo_hi = jnp.concatenate(parts_hi + [filler], axis=2)
    halo_lo = jnp.concatenate(parts_lo + [filler], axis=2)
    departed = interpolate(halo_hi, halo_lo, info, lat_rows, lon_cols, base=partial)

    parts = lax.axis_size("lon")
    me = lax.axis_index("lon")
    chunk = n_items // parts
    pieces = []
    owners = []
    for shift in range(parts):
        target = lax.rem(me + shift, parts)
        piece = lax.dynamic_slice_in_dim(departed, target * chunk, chunk, axis=1)
        if shift:
            piece = lax.ppermute(piece, "lon", [(i, (i + shift) % parts) for i in range(parts)])
        pieces.append(piece)
        owners.append(lax.rem(me - shift + parts, parts))
    real_part, imag_part = spectrum(pieces, owners)
    return (jnp.transpose(real_part, (1, 0, 2)), jnp.transpose(imag_part, (1, 0, 2)))


def solution(mesh):
    placed = (P(None, None, "lat", "lon"), P(None, "lat", "lon"), P(None, "lat", "lon"), P())
    return jax.shard_map(
        on_device,
        mesh=mesh,
        in_specs=placed,
        out_specs=(P("lon", "lat", None), P("lon", "lat", None)),
        check_vma=False,
    )
```

```python
import functools
import math

import jax
import jax.numpy as jnp
from jax import lax
from jax.experimental import pallas as pl
from jax.experimental.pallas import tpu as pltpu
from jax.sharding import PartitionSpec as P

RADIX = 64
NK = 1280
HALO = 16
ROWS_OUT = 3
TAPS = 4
LANES = 128
WINDOW = 256


def shifted(block, axis, width, dim, periodic):
    count = lax.axis_size(axis)
    forward = [(i, i + 1) for i in range(count - 1)]
    if periodic:
        forward.append((count - 1, 0))
    backward = [(target, source) for source, target in forward]
    low = lax.ppermute(
        lax.slice_in_dim(block, block.shape[dim] - width, None, axis=dim), axis, forward
    )
    high = lax.ppermute(lax.slice_in_dim(block, 0, width, axis=dim), axis, backward)
    return low, high


def spectrum(pieces, owners):
    n_rows, n_items, piece_len = pieces[0].shape
    line_len = piece_len * len(pieces)
    highest = lax.Precision.HIGH
    digits = jnp.arange(RADIX, dtype=jnp.int32)
    angle_one = (
        2.0 * math.pi / RADIX * (digits[:, None] * digits[None, :] % RADIX).astype(jnp.float32)
    )
    first_table = jnp.concatenate([jnp.cos(angle_one), -jnp.sin(angle_one)], axis=1)
    per_piece = piece_len // RADIX
    folded = jnp.stack([piece.reshape(n_rows * n_items, per_piece, RADIX) for piece in pieces])
    table = jnp.stack(
        [lax.dynamic_slice_in_dim(first_table, owner * per_piece, per_piece, axis=0) for owner in owners]
    )
    partial_value = jnp.einsum("prab,pac->rbc", folded, table, precision=highest)
    angle_two = (
        2.0
        * math.pi
        / line_len
        * (digits[:, None] * digits[None, :] % line_len).astype(jnp.float32)
    )
    cos_two = jnp.cos(angle_two)
    sin_two = jnp.sin(angle_two)
    part_re = partial_value[..., :RADIX]
    part_im = partial_value[..., RADIX:]
    twisted = jnp.concatenate(
        [part_re * cos_two + part_im * sin_two, part_im * cos_two - part_re * sin_two], axis=-1
    )
    quotients = jnp.arange(NK // RADIX, dtype=jnp.int32)
    angle_three = (
        2.0 * math.pi / RADIX * (digits[:, None] * quotients[None, :] % RADIX).astype(jnp.float32)
    )
    with_cos = jnp.einsum("rbc,bq->rqc", twisted, jnp.cos(angle_three), precision=highest)
    with_sin = jnp.einsum("rbc,bq->rqc", twisted, jnp.sin(angle_three), precision=highest)
    scale = 1.0 / math.sqrt(line_len)
    real_part = (with_cos[..., :RADIX] + with_sin[..., RADIX:]) * scale
    imag_part = (with_cos[..., RADIX:] - with_sin[..., :RADIX]) * scale
    return (real_part.reshape(n_rows, n_items, NK), imag_part.reshape(n_rows, n_items, NK))


def interp_kernel(local, lat_rows, *refs):
    if local:
        hi_ref, lo_ref, info_ref, out_ref = refs
    else:
        hi_ref, lo_ref, info_ref, base_ref, out_ref = refs
    block = pl.program_id(0)
    start = pl.multiple_of(block * LANES, LANES)
    c_index = lax.broadcasted_iota(jnp.int32, (WINDOW, LANES), 0).astype(jnp.float32)
    j_index = lax.broadcasted_iota(jnp.int32, (WINDOW, LANES), 1).astype(jnp.float32)
    for row in range(lat_rows):
        info = info_ref[row]
        offset_r = info[16:17, :]
        offset_d = info[17:18, :]
        tap = c_index - j_index - offset_d
        masks = [tap == float(b) for b in range(TAPS)]
        if local:
            acc = jnp.zeros(out_ref.shape[1:], jnp.float32)
        else:
            acc = base_ref[row]
        for p in range(2 * ROWS_OUT + 1):
            h = row + p
            inside = ROWS_OUT <= h < ROWS_OUT + lat_rows
            if inside != local:
                continue
            if local:
                index = h - ROWS_OUT
            else:
                index = h if h < ROWS_OUT else h - lat_rows
            picked = []
            for b in range(TAPS):
                value = jnp.zeros_like(offset_r)
                for a in range(TAPS):
                    if 0 <= p - a <= ROWS_OUT:
                        value = jnp.where(offset_r == float(p - a), info[4 * a + b : 4 * a + b + 1, :], value)
                picked.append(value)
            matrix = jnp.where(
                masks[0],
                picked[0],
                jnp.where(masks[1], picked[1], jnp.where(masks[2], picked[2], jnp.where(masks[3], picked[3], 0.0))),
            )
            m_hi = matrix.astype(jnp.bfloat16)
            m_lo = (matrix - m_hi.astype(jnp.float32)).astype(jnp.bfloat16)
            x_hi = hi_ref[index, :, pl.ds(start, WINDOW)]
            x_lo = lo_ref[index, :, pl.ds(start, WINDOW)]
            both = jnp.dot(x_hi, jnp.concatenate([m_hi, m_lo], axis=1), preferred_element_type=jnp.float32)
            acc = acc + both[:, :LANES] + both[:, LANES:]
            acc = acc + jnp.dot(x_lo, m_hi, preferred_element_type=jnp.float32)
        out_ref[row] = acc


def interpolate(x_hi, x_lo, info, lat_rows, lon_cols, base=None):
    n_rows, n_items, width = x_hi.shape
    blocks = lon_cols // LANES
    whole = pl.BlockSpec((n_rows, n_items, width), lambda jb: (0, 0, 0))
    tile = pl.BlockSpec((lat_rows, n_items, LANES), lambda jb: (0, 0, jb))
    specs = [whole, whole, pl.BlockSpec((lat_rows, info.shape[1], LANES), lambda jb: (0, 0, jb))]
    operands = [x_hi, x_lo, info]
    if base is not None:
        specs.append(tile)
        operands.append(base)
    return pl.pallas_call(
        functools.partial(interp_kernel, base is None, lat_rows),
        out_shape=jax.ShapeDtypeStruct((lat_rows, n_items, lon_cols), jnp.float32),
        grid=(blocks,),
        in_specs=specs,
        out_specs=tile,
        compiler_params=pltpu.CompilerParams(vmem_limit_bytes=48 * 1024 * 1024),
    )(*operands)


def vertical_mix(raw, bands):
    n_levels = raw.shape[-2]
    pad = [(0, 0)] * raw.ndim
    pad[-2] = (2, 2)
    stacked = jnp.pad(raw, pad)
    lead = (None,) * (raw.ndim - 3)
    mixed = bands[lead + (slice(None), 0, slice(None), None)] * stacked[..., 0:n_levels, :]
    for shift_k in range(1, 5):
        mixed = mixed + bands[lead + (slice(None), shift_k, slice(None), None)] * stacked[
            ..., shift_k : shift_k + n_levels, :
        ]
    return mixed


def widen(block):
    left, right = shifted(block, "lon", HALO, block.ndim - 1, True)
    return jnp.concatenate([left, block, right], axis=block.ndim - 1)


def split_rows(rows, width):
    pad = [(0, 0)] * (rows.ndim - 1) + [(0, width - rows.shape[-1])]
    padded = jnp.pad(rows, pad)
    rounded = lax.reduce_precision(padded, exponent_bits=8, mantissa_bits=7)
    return rounded.astype(jnp.bfloat16), (padded - rounded).astype(jnp.bfloat16)


def on_device(fields, weights, stencil, bands):
    n_fields, n_levels, lat_rows, lon_cols = fields.shape
    n_items = n_fields * n_levels
    split_at = n_fields // 2
    lows = []
    highs = []
    for group in (fields[:split_at], fields[split_at:]):
        low, high = shifted(group, "lat", ROWS_OUT, 2, False)
        lows.append(low)
        highs.append(high)
    below_raw = jnp.concatenate(lows, axis=0)
    above_raw = jnp.concatenate(highs, axis=0)

    width = lon_cols + LANES
    local_rows = vertical_mix(jnp.transpose(fields, (2, 0, 1, 3)), bands)
    local_hi, local_lo = split_rows(widen(local_rows.reshape(lat_rows, n_items, lon_cols)), width)

    lat_start = lax.axis_index("lat") * lat_rows
    lon_start = lax.axis_index("lon") * lon_cols
    line_len = lon_cols * lax.axis_size("lon")
    row_g = lat_start + jnp.arange(lat_rows, dtype=jnp.int32)[:, None]
    col_g = lon_start + jnp.arange(lon_cols, dtype=jnp.int32)[None, :]
    offset_r = (stencil[0] - row_g + ROWS_OUT).astype(jnp.float32)
    offset_d = jnp.mod(stencil[1] - col_g + HALO, line_len).astype(jnp.float32)
    info = jnp.concatenate(
        [
            jnp.transpose(weights, (1, 0, 2)),
            offset_r[:, None, :],
            offset_d[:, None, :],
            jnp.zeros((lat_rows, 6, lon_cols), jnp.float32),
        ],
        axis=1,
    )
    partial = interpolate(local_hi, local_lo, info, lat_rows, lon_cols)

    below_raw, above_raw, partial = lax.optimization_barrier((below_raw, above_raw, partial))
    halo_raw = jnp.concatenate([below_raw, above_raw], axis=2)
    halo_rows = vertical_mix(jnp.transpose(halo_raw, (2, 0, 1, 3)), bands)
    halo_hi, halo_lo = split_rows(widen(halo_rows.reshape(2 * ROWS_OUT, n_items, lon_cols)), width)
    departed = interpolate(halo_hi, halo_lo, info, lat_rows, lon_cols, base=partial)

    parts = lax.axis_size("lon")
    me = lax.axis_index("lon")
    chunk = n_items // parts
    pieces = []
    owners = []
    for shift in range(parts):
        target = lax.rem(me + shift, parts)
        piece = lax.dynamic_slice_in_dim(departed, target * chunk, chunk, axis=1)
        if shift:
            piece = lax.ppermute(piece, "lon", [(i, (i + shift) % parts) for i in range(parts)])
        pieces.append(piece)
        owners.append(lax.rem(me - shift + parts, parts))
    real_part, imag_part = spectrum(pieces, owners)
    return (jnp.transpose(real_part, (1, 0, 2)), jnp.transpose(imag_part, (1, 0, 2)))


def solution(mesh):
    placed = (P(None, None, "lat", "lon"), P(None, "lat", "lon"), P(None, "lat", "lon"), P())
    return jax.shard_map(
        on_device,
        mesh=mesh,
        in_specs=placed,
        out_specs=(P("lon", "lat", None), P("lon", "lat", None)),
        check_vma=False,
    )
```

```python
import functools
import math

import jax
import jax.numpy as jnp
from jax import lax
from jax.experimental import pallas as pl
from jax.experimental.pallas import tpu as pltpu
from jax.sharding import PartitionSpec as P

RADIX = 64
NK = 1280
HALO = 16
ROWS_OUT = 3
TAPS = 4
LANES = 128
WINDOW = 256


def shifted(block, axis, width, dim, periodic):
    count = lax.axis_size(axis)
    forward = [(i, i + 1) for i in range(count - 1)]
    if periodic:
        forward.append((count - 1, 0))
    backward = [(target, source) for source, target in forward]
    low = lax.ppermute(
        lax.slice_in_dim(block, block.shape[dim] - width, None, axis=dim), axis, forward
    )
    high = lax.ppermute(lax.slice_in_dim(block, 0, width, axis=dim), axis, backward)
    return low, high


def spectrum(pieces, owners):
    n_rows, n_items, piece_len = pieces[0].shape
    line_len = piece_len * len(pieces)
    highest = lax.Precision.HIGH
    digits = jnp.arange(RADIX, dtype=jnp.int32)
    angle_one = (
        2.0 * math.pi / RADIX * (digits[:, None] * digits[None, :] % RADIX).astype(jnp.float32)
    )
    first_table = jnp.concatenate([jnp.cos(angle_one), -jnp.sin(angle_one)], axis=1)
    per_piece = piece_len // RADIX
    folded = jnp.stack([piece.reshape(n_rows * n_items, per_piece, RADIX) for piece in pieces])
    table = jnp.stack(
        [lax.dynamic_slice_in_dim(first_table, owner * per_piece, per_piece, axis=0) for owner in owners]
    )
    partial_value = jnp.einsum("prab,pac->rbc", folded, table, precision=highest)
    angle_two = (
        2.0
        * math.pi
        / line_len
        * (digits[:, None] * digits[None, :] % line_len).astype(jnp.float32)
    )
    cos_two = jnp.cos(angle_two)
    sin_two = jnp.sin(angle_two)
    part_re = partial_value[..., :RADIX]
    part_im = partial_value[..., RADIX:]
    twisted = jnp.concatenate(
        [part_re * cos_two + part_im * sin_two, part_im * cos_two - part_re * sin_two], axis=-1
    )
    quotients = jnp.arange(NK // RADIX, dtype=jnp.int32)
    angle_three = (
        2.0 * math.pi / RADIX * (digits[:, None] * quotients[None, :] % RADIX).astype(jnp.float32)
    )
    with_cos = jnp.einsum("rbc,bq->rqc", twisted, jnp.cos(angle_three), precision=highest)
    with_sin = jnp.einsum("rbc,bq->rqc", twisted, jnp.sin(angle_three), precision=highest)
    scale = 1.0 / math.sqrt(line_len)
    real_part = (with_cos[..., :RADIX] + with_sin[..., RADIX:]) * scale
    imag_part = (with_cos[..., RADIX:] - with_sin[..., :RADIX]) * scale
    return (real_part.reshape(n_rows, n_items, NK), imag_part.reshape(n_rows, n_items, NK))


def interp_kernel(local, lat_rows, *refs):
    if local:
        hi_ref, lo_ref, info_ref, out_ref = refs
    else:
        hi_ref, lo_ref, info_ref, base_ref, out_ref = refs
    block = pl.program_id(0)
    start = pl.multiple_of(block * LANES, LANES)
    c_index = lax.broadcasted_iota(jnp.int32, (WINDOW, LANES), 0).astype(jnp.float32)
    j_index = lax.broadcasted_iota(jnp.int32, (WINDOW, LANES), 1).astype(jnp.float32)
    for row in range(lat_rows):
        info = info_ref[row]
        offset_r = info[16:17, :]
        offset_d = info[17:18, :]
        tap = c_index - j_index - offset_d
        masks = [tap == float(b) for b in range(TAPS)]
        if local:
            acc = jnp.zeros(out_ref.shape[1:], jnp.float32)
        else:
            acc = base_ref[row]
        for p in range(2 * ROWS_OUT + 1):
            h = row + p
            inside = ROWS_OUT <= h < ROWS_OUT + lat_rows
            if inside != local:
                continue
            if local:
                index = h - ROWS_OUT
            else:
                index = h if h < ROWS_OUT else h - lat_rows
            picked = []
            for b in range(TAPS):
                value = jnp.zeros_like(offset_r)
                for a in range(TAPS):
                    if 0 <= p - a <= ROWS_OUT:
                        value = jnp.where(offset_r == float(p - a), info[4 * a + b : 4 * a + b + 1, :], value)
                picked.append(value)
            matrix = jnp.where(
                masks[0],
                picked[0],
                jnp.where(masks[1], picked[1], jnp.where(masks[2], picked[2], jnp.where(masks[3], picked[3], 0.0))),
            )
            m_hi = matrix.astype(jnp.bfloat16)
            m_lo = (matrix - m_hi.astype(jnp.float32)).astype(jnp.bfloat16)
            x_hi = hi_ref[index, :, pl.ds(start, WINDOW)]
            x_lo = lo_ref[index, :, pl.ds(start, WINDOW)]
            rows_hi = x_hi.shape[0]
            both = jnp.dot(
                jnp.concatenate([x_hi, x_lo], axis=0),
                jnp.concatenate([m_hi, m_lo], axis=1),
                preferred_element_type=jnp.float32,
            )
            acc = acc + both[:rows_hi, :LANES] + both[:rows_hi, LANES:] + both[rows_hi:, :LANES]
        out_ref[row] = acc


def interpolate(x_hi, x_lo, info, lat_rows, lon_cols, base=None):
    n_rows, n_items, width = x_hi.shape
    blocks = lon_cols // LANES
    whole = pl.BlockSpec((n_rows, n_items, width), lambda jb: (0, 0, 0))
    tile = pl.BlockSpec((lat_rows, n_items, LANES), lambda jb: (0, 0, jb))
    specs = [whole, whole, pl.BlockSpec((lat_rows, info.shape[1], LANES), lambda jb: (0, 0, jb))]
    operands = [x_hi, x_lo, info]
    if base is not None:
        specs.append(tile)
        operands.append(base)
    return pl.pallas_call(
        functools.partial(interp_kernel, base is None, lat_rows),
        out_shape=jax.ShapeDtypeStruct((lat_rows, n_items, lon_cols), jnp.float32),
        grid=(blocks,),
        in_specs=specs,
        out_specs=tile,
        compiler_params=pltpu.CompilerParams(vmem_limit_bytes=48 * 1024 * 1024),
    )(*operands)


def vertical_mix(raw, bands):
    n_levels = raw.shape[-2]
    pad = [(0, 0)] * raw.ndim
    pad[-2] = (2, 2)
    stacked = jnp.pad(raw, pad)
    lead = (None,) * (raw.ndim - 3)
    mixed = bands[lead + (slice(None), 0, slice(None), None)] * stacked[..., 0:n_levels, :]
    for shift_k in range(1, 5):
        mixed = mixed + bands[lead + (slice(None), shift_k, slice(None), None)] * stacked[
            ..., shift_k : shift_k + n_levels, :
        ]
    return mixed


def widen(block):
    left, right = shifted(block, "lon", HALO, block.ndim - 1, True)
    return jnp.concatenate([left, block, right], axis=block.ndim - 1)


def split_rows(rows, width):
    pad = [(0, 0)] * (rows.ndim - 1) + [(0, width - rows.shape[-1])]
    padded = jnp.pad(rows, pad)
    rounded = lax.reduce_precision(padded, exponent_bits=8, mantissa_bits=7)
    return rounded.astype(jnp.bfloat16), (padded - rounded).astype(jnp.bfloat16)


def on_device(fields, weights, stencil, bands):
    n_fields, n_levels, lat_rows, lon_cols = fields.shape
    n_items = n_fields * n_levels
    below_raw, above_raw = shifted(fields, "lat", ROWS_OUT, 2, False)

    width = lon_cols + LANES
    local_rows = vertical_mix(jnp.transpose(fields, (2, 0, 1, 3)), bands)
    local_hi, local_lo = split_rows(widen(local_rows.reshape(lat_rows, n_items, lon_cols)), width)

    lat_start = lax.axis_index("lat") * lat_rows
    lon_start = lax.axis_index("lon") * lon_cols
    line_len = lon_cols * lax.axis_size("lon")
    row_g = lat_start + jnp.arange(lat_rows, dtype=jnp.int32)[:, None]
    col_g = lon_start + jnp.arange(lon_cols, dtype=jnp.int32)[None, :]
    offset_r = (stencil[0] - row_g + ROWS_OUT).astype(jnp.float32)
    offset_d = jnp.mod(stencil[1] - col_g + HALO, line_len).astype(jnp.float32)
    info = jnp.concatenate(
        [
            jnp.transpose(weights, (1, 0, 2)),
            offset_r[:, None, :],
            offset_d[:, None, :],
            jnp.zeros((lat_rows, 6, lon_cols), jnp.float32),
        ],
        axis=1,
    )
    partial = interpolate(local_hi, local_lo, info, lat_rows, lon_cols)

    below_raw, above_raw, partial = lax.optimization_barrier((below_raw, above_raw, partial))
    halo_raw = jnp.concatenate([below_raw, above_raw], axis=2)
    halo_rows = vertical_mix(jnp.transpose(halo_raw, (2, 0, 1, 3)), bands)
    halo_hi, halo_lo = split_rows(widen(halo_rows.reshape(2 * ROWS_OUT, n_items, lon_cols)), width)
    departed = interpolate(halo_hi, halo_lo, info, lat_rows, lon_cols, base=partial)

    parts = lax.axis_size("lon")
    me = lax.axis_index("lon")
    chunk = n_items // parts
    pieces = []
    owners = []
    for shift in range(parts):
        target = lax.rem(me + shift, parts)
        piece = lax.dynamic_slice_in_dim(departed, target * chunk, chunk, axis=1)
        if shift:
            piece = lax.ppermute(piece, "lon", [(i, (i + shift) % parts) for i in range(parts)])
        pieces.append(piece)
        owners.append(lax.rem(me - shift + parts, parts))
    real_part, imag_part = spectrum(pieces, owners)
    return (jnp.transpose(real_part, (1, 0, 2)), jnp.transpose(imag_part, (1, 0, 2)))


def solution(mesh):
    placed = (P(None, None, "lat", "lon"), P(None, "lat", "lon"), P(None, "lat", "lon"), P())
    return jax.shard_map(
        on_device,
        mesh=mesh,
        in_specs=placed,
        out_specs=(P("lon", "lat", None), P("lon", "lat", None)),
        check_vma=False,
    )
```

```python
import functools
import math

import jax
import jax.numpy as jnp
from jax import lax
from jax.experimental import pallas as pl
from jax.experimental.pallas import tpu as pltpu
from jax.sharding import PartitionSpec as P

RADIX = 64
NK = 1280
HALO = 16
ROWS_OUT = 3
TAPS = 4
LANES = 128
WINDOW = 256


def shifted(block, axis, width, dim, periodic):
    count = lax.axis_size(axis)
    forward = [(i, i + 1) for i in range(count - 1)]
    if periodic:
        forward.append((count - 1, 0))
    backward = [(target, source) for source, target in forward]
    low = lax.ppermute(
        lax.slice_in_dim(block, block.shape[dim] - width, None, axis=dim), axis, forward
    )
    high = lax.ppermute(lax.slice_in_dim(block, 0, width, axis=dim), axis, backward)
    return low, high


def spectrum(pieces, owners):
    n_rows, n_items, piece_len = pieces[0].shape
    line_len = piece_len * len(pieces)
    highest = lax.Precision.HIGH
    digits = jnp.arange(RADIX, dtype=jnp.int32)
    angle_one = (
        2.0 * math.pi / RADIX * (digits[:, None] * digits[None, :] % RADIX).astype(jnp.float32)
    )
    first_table = jnp.concatenate([jnp.cos(angle_one), -jnp.sin(angle_one)], axis=1)
    per_piece = piece_len // RADIX
    folded = jnp.stack([piece.reshape(n_rows * n_items, per_piece, RADIX) for piece in pieces])
    table = jnp.stack(
        [lax.dynamic_slice_in_dim(first_table, owner * per_piece, per_piece, axis=0) for owner in owners]
    )
    partial_value = jnp.einsum("prab,pac->rbc", folded, table, precision=highest)
    angle_two = (
        2.0
        * math.pi
        / line_len
        * (digits[:, None] * digits[None, :] % line_len).astype(jnp.float32)
    )
    cos_two = jnp.cos(angle_two)
    sin_two = jnp.sin(angle_two)
    part_re = partial_value[..., :RADIX]
    part_im = partial_value[..., RADIX:]
    twisted = jnp.concatenate(
        [part_re * cos_two + part_im * sin_two, part_im * cos_two - part_re * sin_two], axis=-1
    )
    quotients = jnp.arange(NK // RADIX, dtype=jnp.int32)
    angle_three = (
        2.0 * math.pi / RADIX * (digits[:, None] * quotients[None, :] % RADIX).astype(jnp.float32)
    )
    with_cos = jnp.einsum("rbc,bq->rqc", twisted, jnp.cos(angle_three), precision=highest)
    with_sin = jnp.einsum("rbc,bq->rqc", twisted, jnp.sin(angle_three), precision=highest)
    scale = 1.0 / math.sqrt(line_len)
    real_part = (with_cos[..., :RADIX] + with_sin[..., RADIX:]) * scale
    imag_part = (with_cos[..., RADIX:] - with_sin[..., :RADIX]) * scale
    return (real_part.reshape(n_rows, n_items, NK), imag_part.reshape(n_rows, n_items, NK))


def interp_kernel(local, lat_rows, parts, *refs):
    if local:
        hi_ref, lo_ref, info_ref, out_ref = refs
    else:
        me_ref, hi_ref, lo_ref, info_ref, base_ref, out_ref = refs
    block = pl.program_id(0)
    start = pl.multiple_of(block * LANES, LANES)
    c_index = lax.broadcasted_iota(jnp.int32, (WINDOW, LANES), 0).astype(jnp.float32)
    j_index = lax.broadcasted_iota(jnp.int32, (WINDOW, LANES), 1).astype(jnp.float32)
    for row in range(lat_rows):
        info = info_ref[row]
        offset_r = info[16:17, :]
        offset_d = info[17:18, :]
        tap = c_index - j_index - offset_d
        masks = [tap == float(b) for b in range(TAPS)]
        if local:
            acc = jnp.zeros(out_ref.shape[1:], jnp.float32)
        else:
            acc = base_ref[row]
        for p in range(2 * ROWS_OUT + 1):
            h = row + p
            inside = ROWS_OUT <= h < ROWS_OUT + lat_rows
            if inside != local:
                continue
            if local:
                index = h - ROWS_OUT
            else:
                index = h if h < ROWS_OUT else h - lat_rows
            picked = []
            for b in range(TAPS):
                value = jnp.zeros_like(offset_r)
                for a in range(TAPS):
                    if 0 <= p - a <= ROWS_OUT:
                        value = jnp.where(offset_r == float(p - a), info[4 * a + b : 4 * a + b + 1, :], value)
                picked.append(value)
            matrix = jnp.where(
                masks[0],
                picked[0],
                jnp.where(masks[1], picked[1], jnp.where(masks[2], picked[2], jnp.where(masks[3], picked[3], 0.0))),
            )
            m_hi = matrix.astype(jnp.bfloat16)
            m_lo = (matrix - m_hi.astype(jnp.float32)).astype(jnp.bfloat16)
            x_hi = hi_ref[index, :, pl.ds(start, WINDOW)]
            x_lo = lo_ref[index, :, pl.ds(start, WINDOW)]
            rows_hi = x_hi.shape[0]
            both = jnp.dot(
                jnp.concatenate([x_hi, x_lo], axis=0),
                jnp.concatenate([m_hi, m_lo], axis=1),
                preferred_element_type=jnp.float32,
            )
            acc = acc + both[:rows_hi, :LANES] + both[:rows_hi, LANES:] + both[rows_hi:, :LANES]
        if local:
            out_ref[row] = acc
        else:
            chunk = acc.shape[0] // parts
            for c in range(parts):
                slot = lax.rem(c - me_ref[0] + parts, parts)
                out_ref[slot, row] = acc[c * chunk : (c + 1) * chunk]


def interpolate(x_hi, x_lo, info, lat_rows, lon_cols, base=None):
    n_rows, n_items, width = x_hi.shape
    blocks = lon_cols // LANES
    whole = pl.BlockSpec((n_rows, n_items, width), lambda jb: (0, 0, 0))
    tile = pl.BlockSpec((lat_rows, n_items, LANES), lambda jb: (0, 0, jb))
    specs = [whole, whole, pl.BlockSpec((lat_rows, info.shape[1], LANES), lambda jb: (0, 0, jb))]
    operands = [x_hi, x_lo, info]
    parts = 1
    out_shape = jax.ShapeDtypeStruct((lat_rows, n_items, lon_cols), jnp.float32)
    out_spec = tile
    if base is not None:
        parts = lax.axis_size("lon")
        me = jnp.reshape(lax.axis_index("lon"), (1,)).astype(jnp.int32)
        specs = [pl.BlockSpec(memory_space=pltpu.SMEM)] + specs + [tile]
        operands = [me] + operands + [base]
        chunk = n_items // parts
        out_shape = jax.ShapeDtypeStruct((parts, lat_rows, chunk, lon_cols), jnp.float32)
        out_spec = pl.BlockSpec((parts, lat_rows, chunk, LANES), lambda jb: (0, 0, 0, jb))
    return pl.pallas_call(
        functools.partial(interp_kernel, base is None, lat_rows, parts),
        out_shape=out_shape,
        grid=(blocks,),
        in_specs=specs,
        out_specs=out_spec,
        compiler_params=pltpu.CompilerParams(vmem_limit_bytes=48 * 1024 * 1024),
    )(*operands)


def vertical_mix(raw, bands):
    n_levels = raw.shape[-2]
    pad = [(0, 0)] * raw.ndim
    pad[-2] = (2, 2)
    stacked = jnp.pad(raw, pad)
    lead = (None,) * (raw.ndim - 3)
    mixed = bands[lead + (slice(None), 0, slice(None), None)] * stacked[..., 0:n_levels, :]
    for shift_k in range(1, 5):
        mixed = mixed + bands[lead + (slice(None), shift_k, slice(None), None)] * stacked[
            ..., shift_k : shift_k + n_levels, :
        ]
    return mixed


def widen(block):
    left, right = shifted(block, "lon", HALO, block.ndim - 1, True)
    return jnp.concatenate([left, block, right], axis=block.ndim - 1)


def split_rows(rows, width):
    pad = [(0, 0)] * (rows.ndim - 1) + [(0, width - rows.shape[-1])]
    padded = jnp.pad(rows, pad)
    rounded = lax.reduce_precision(padded, exponent_bits=8, mantissa_bits=7)
    return rounded.astype(jnp.bfloat16), (padded - rounded).astype(jnp.bfloat16)


def on_device(fields, weights, stencil, bands):
    n_fields, n_levels, lat_rows, lon_cols = fields.shape
    n_items = n_fields * n_levels
    below_raw, above_raw = shifted(fields, "lat", ROWS_OUT, 2, False)

    width = lon_cols + LANES
    local_rows = vertical_mix(jnp.transpose(fields, (2, 0, 1, 3)), bands)
    local_hi, local_lo = split_rows(widen(local_rows.reshape(lat_rows, n_items, lon_cols)), width)

    lat_start = lax.axis_index("lat") * lat_rows
    lon_start = lax.axis_index("lon") * lon_cols
    line_len = lon_cols * lax.axis_size("lon")
    row_g = lat_start + jnp.arange(lat_rows, dtype=jnp.int32)[:, None]
    col_g = lon_start + jnp.arange(lon_cols, dtype=jnp.int32)[None, :]
    offset_r = (stencil[0] - row_g + ROWS_OUT).astype(jnp.float32)
    offset_d = jnp.mod(stencil[1] - col_g + HALO, line_len).astype(jnp.float32)
    info = jnp.concatenate(
        [
            jnp.transpose(weights, (1, 0, 2)),
            offset_r[:, None, :],
            offset_d[:, None, :],
            jnp.zeros((lat_rows, 6, lon_cols), jnp.float32),
        ],
        axis=1,
    )
    partial = interpolate(local_hi, local_lo, info, lat_rows, lon_cols)

    below_raw, above_raw, partial = lax.optimization_barrier((below_raw, above_raw, partial))
    halo_raw = jnp.concatenate([below_raw, above_raw], axis=2)
    halo_rows = vertical_mix(jnp.transpose(halo_raw, (2, 0, 1, 3)), bands)
    halo_hi, halo_lo = split_rows(widen(halo_rows.reshape(2 * ROWS_OUT, n_items, lon_cols)), width)
    departed = interpolate(halo_hi, halo_lo, info, lat_rows, lon_cols, base=partial)

    parts = lax.axis_size("lon")
    me = lax.axis_index("lon")
    chunk = n_items // parts
    pieces = []
    owners = []
    for shift in range(parts):
        piece = departed[shift]
        if shift:
            piece = lax.ppermute(piece, "lon", [(i, (i + shift) % parts) for i in range(parts)])
        pieces.append(piece)
        owners.append(lax.rem(me - shift + parts, parts))
    real_part, imag_part = spectrum(pieces, owners)
    return (jnp.transpose(real_part, (1, 0, 2)), jnp.transpose(imag_part, (1, 0, 2)))


def solution(mesh):
    placed = (P(None, None, "lat", "lon"), P(None, "lat", "lon"), P(None, "lat", "lon"), P())
    return jax.shard_map(
        on_device,
        mesh=mesh,
        in_specs=placed,
        out_specs=(P("lon", "lat", None), P("lon", "lat", None)),
        check_vma=False,
    )
```

```python
import functools
import math

import jax
import jax.numpy as jnp
from jax import lax
from jax.experimental import pallas as pl
from jax.experimental.pallas import tpu as pltpu
from jax.sharding import PartitionSpec as P

RADIX = 64
NK = 1280
HALO = 16
ROWS_OUT = 3
TAPS = 4
LANES = 128
WINDOW = 256


def shifted(block, axis, width, dim, periodic):
    count = lax.axis_size(axis)
    forward = [(i, i + 1) for i in range(count - 1)]
    if periodic:
        forward.append((count - 1, 0))
    backward = [(target, source) for source, target in forward]
    low = lax.ppermute(
        lax.slice_in_dim(block, block.shape[dim] - width, None, axis=dim), axis, forward
    )
    high = lax.ppermute(lax.slice_in_dim(block, 0, width, axis=dim), axis, backward)
    return low, high


def spectrum(pieces, owners):
    n_rows, n_items, piece_len = pieces[0].shape
    line_len = piece_len * len(pieces)
    highest = lax.Precision.HIGH
    digits = jnp.arange(RADIX, dtype=jnp.int32)
    angle_one = (
        2.0 * math.pi / RADIX * (digits[:, None] * digits[None, :] % RADIX).astype(jnp.float32)
    )
    first_table = jnp.concatenate([jnp.cos(angle_one), -jnp.sin(angle_one)], axis=1)
    per_piece = piece_len // RADIX
    folded = jnp.stack([piece.reshape(n_rows * n_items, per_piece, RADIX) for piece in pieces])
    table = jnp.stack(
        [lax.dynamic_slice_in_dim(first_table, owner * per_piece, per_piece, axis=0) for owner in owners]
    )
    partial_value = jnp.einsum("prab,pac->rbc", folded, table, precision=highest)
    angle_two = (
        2.0
        * math.pi
        / line_len
        * (digits[:, None] * digits[None, :] % line_len).astype(jnp.float32)
    )
    cos_two = jnp.cos(angle_two)
    sin_two = jnp.sin(angle_two)
    part_re = partial_value[..., :RADIX]
    part_im = partial_value[..., RADIX:]
    twisted = jnp.concatenate(
        [part_re * cos_two + part_im * sin_two, part_im * cos_two - part_re * sin_two], axis=-1
    )
    quotients = jnp.arange(NK // RADIX, dtype=jnp.int32)
    angle_three = (
        2.0 * math.pi / RADIX * (digits[:, None] * quotients[None, :] % RADIX).astype(jnp.float32)
    )
    modes = NK // RADIX
    both = jnp.einsum(
        "rbc,bq->rqc",
        twisted,
        jnp.concatenate([jnp.cos(angle_three), jnp.sin(angle_three)], axis=1),
        precision=highest,
    )
    with_cos = both[:, :modes]
    with_sin = both[:, modes:]
    scale = 1.0 / math.sqrt(line_len)
    real_part = (with_cos[..., :RADIX] + with_sin[..., RADIX:]) * scale
    imag_part = (with_cos[..., RADIX:] - with_sin[..., :RADIX]) * scale
    return (real_part.reshape(n_rows, n_items, NK), imag_part.reshape(n_rows, n_items, NK))


def interp_kernel(local, lat_rows, *refs):
    if local:
        hi_ref, lo_ref, info_ref, out_ref = refs
    else:
        hi_ref, lo_ref, info_ref, base_ref, out_ref = refs
    block = pl.program_id(0)
    start = pl.multiple_of(block * LANES, LANES)
    c_index = lax.broadcasted_iota(jnp.int32, (WINDOW, LANES), 0).astype(jnp.float32)
    j_index = lax.broadcasted_iota(jnp.int32, (WINDOW, LANES), 1).astype(jnp.float32)
    for row in range(lat_rows):
        info = info_ref[row]
        offset_r = info[16:17, :]
        offset_d = info[17:18, :]
        tap = c_index - j_index - offset_d
        masks = [tap == float(b) for b in range(TAPS)]
        if local:
            acc = jnp.zeros(out_ref.shape[1:], jnp.float32)
        else:
            acc = base_ref[row]
        for p in range(2 * ROWS_OUT + 1):
            h = row + p
            inside = ROWS_OUT <= h < ROWS_OUT + lat_rows
            if inside != local:
                continue
            if local:
                index = h - ROWS_OUT
            else:
                index = h if h < ROWS_OUT else h - lat_rows
            picked = []
            for b in range(TAPS):
                value = jnp.zeros_like(offset_r)
                for a in range(TAPS):
                    if 0 <= p - a <= ROWS_OUT:
                        value = jnp.where(offset_r == float(p - a), info[4 * a + b : 4 * a + b + 1, :], value)
                picked.append(value)
            matrix = jnp.where(
                masks[0],
                picked[0],
                jnp.where(masks[1], picked[1], jnp.where(masks[2], picked[2], jnp.where(masks[3], picked[3], 0.0))),
            )
            m_hi = matrix.astype(jnp.bfloat16)
            m_lo = (matrix - m_hi.astype(jnp.float32)).astype(jnp.bfloat16)
            x_hi = hi_ref[index, :, pl.ds(start, WINDOW)]
            x_lo = lo_ref[index, :, pl.ds(start, WINDOW)]
            rows_hi = x_hi.shape[0]
            both = jnp.dot(
                jnp.concatenate([x_hi, x_lo], axis=0),
                jnp.concatenate([m_hi, m_lo], axis=1),
                preferred_element_type=jnp.float32,
            )
            acc = acc + both[:rows_hi, :LANES] + both[:rows_hi, LANES:] + both[rows_hi:, :LANES]
        out_ref[row] = acc


def interpolate(x_hi, x_lo, info, lat_rows, lon_cols, base=None):
    n_rows, n_items, width = x_hi.shape
    blocks = lon_cols // LANES
    whole = pl.BlockSpec((n_rows, n_items, width), lambda jb: (0, 0, 0))
    tile = pl.BlockSpec((lat_rows, n_items, LANES), lambda jb: (0, 0, jb))
    specs = [whole, whole, pl.BlockSpec((lat_rows, info.shape[1], LANES), lambda jb: (0, 0, jb))]
    operands = [x_hi, x_lo, info]
    if base is not None:
        specs.append(tile)
        operands.append(base)
    return pl.pallas_call(
        functools.partial(interp_kernel, base is None, lat_rows),
        out_shape=jax.ShapeDtypeStruct((lat_rows, n_items, lon_cols), jnp.float32),
        grid=(blocks,),
        in_specs=specs,
        out_specs=tile,
        compiler_params=pltpu.CompilerParams(vmem_limit_bytes=48 * 1024 * 1024),
    )(*operands)


def vertical_mix(raw, bands):
    n_levels = raw.shape[-2]
    pad = [(0, 0)] * raw.ndim
    pad[-2] = (2, 2)
    stacked = jnp.pad(raw, pad)
    lead = (None,) * (raw.ndim - 3)
    mixed = bands[lead + (slice(None), 0, slice(None), None)] * stacked[..., 0:n_levels, :]
    for shift_k in range(1, 5):
        mixed = mixed + bands[lead + (slice(None), shift_k, slice(None), None)] * stacked[
            ..., shift_k : shift_k + n_levels, :
        ]
    return mixed


def widen(block):
    left, right = shifted(block, "lon", HALO, block.ndim - 1, True)
    return jnp.concatenate([left, block, right], axis=block.ndim - 1)


def split_rows(rows, width):
    pad = [(0, 0)] * (rows.ndim - 1) + [(0, width - rows.shape[-1])]
    padded = jnp.pad(rows, pad)
    rounded = lax.reduce_precision(padded, exponent_bits=8, mantissa_bits=7)
    return rounded.astype(jnp.bfloat16), (padded - rounded).astype(jnp.bfloat16)


def on_device(fields, weights, stencil, bands):
    n_fields, n_levels, lat_rows, lon_cols = fields.shape
    n_items = n_fields * n_levels
    below_raw, above_raw = shifted(fields, "lat", ROWS_OUT, 2, False)

    width = lon_cols + LANES
    local_rows = vertical_mix(jnp.transpose(fields, (2, 0, 1, 3)), bands)
    local_hi, local_lo = split_rows(widen(local_rows.reshape(lat_rows, n_items, lon_cols)), width)

    lat_start = lax.axis_index("lat") * lat_rows
    lon_start = lax.axis_index("lon") * lon_cols
    line_len = lon_cols * lax.axis_size("lon")
    row_g = lat_start + jnp.arange(lat_rows, dtype=jnp.int32)[:, None]
    col_g = lon_start + jnp.arange(lon_cols, dtype=jnp.int32)[None, :]
    offset_r = (stencil[0] - row_g + ROWS_OUT).astype(jnp.float32)
    offset_d = jnp.mod(stencil[1] - col_g + HALO, line_len).astype(jnp.float32)
    info = jnp.concatenate(
        [
            jnp.transpose(weights, (1, 0, 2)),
            offset_r[:, None, :],
            offset_d[:, None, :],
            jnp.zeros((lat_rows, 6, lon_cols), jnp.float32),
        ],
        axis=1,
    )
    partial = interpolate(local_hi, local_lo, info, lat_rows, lon_cols)

    below_raw, above_raw, partial = lax.optimization_barrier((below_raw, above_raw, partial))
    halo_raw = jnp.concatenate([below_raw, above_raw], axis=2)
    halo_rows = vertical_mix(jnp.transpose(halo_raw, (2, 0, 1, 3)), bands)
    halo_hi, halo_lo = split_rows(widen(halo_rows.reshape(2 * ROWS_OUT, n_items, lon_cols)), width)
    departed = interpolate(halo_hi, halo_lo, info, lat_rows, lon_cols, base=partial)

    parts = lax.axis_size("lon")
    me = lax.axis_index("lon")
    chunk = n_items // parts
    pieces = []
    owners = []
    for shift in range(parts):
        target = lax.rem(me + shift, parts)
        piece = lax.dynamic_slice_in_dim(departed, target * chunk, chunk, axis=1)
        if shift:
            piece = lax.ppermute(piece, "lon", [(i, (i + shift) % parts) for i in range(parts)])
        pieces.append(piece)
        owners.append(lax.rem(me - shift + parts, parts))
    real_part, imag_part = spectrum(pieces, owners)
    return (jnp.transpose(real_part, (1, 0, 2)), jnp.transpose(imag_part, (1, 0, 2)))


def solution(mesh):
    placed = (P(None, None, "lat", "lon"), P(None, "lat", "lon"), P(None, "lat", "lon"), P())
    return jax.shard_map(
        on_device,
        mesh=mesh,
        in_specs=placed,
        out_specs=(P("lon", "lat", None), P("lon", "lat", None)),
        check_vma=False,
    )
```
